32 devices in a mesh: space: 8 (over z, y), match: 4 (over x, core).
Axes of the slice: x: 2, y: 2, z: 4, core: 2. Of those that a mesh axis runs over, the one named last changes fastest.
Arguments:
- source: bfloat16 [32, 256, 128], P('space', 'match'), may hold values from -200 to 200
- targets: bfloat16 [8192, 128], P('match'), may hold values from -200 to 200
- conv_in: bfloat16 [3, 3, 128, 128], replicated, may hold values from -0.1875 to 0.1875
- flow_proj: float32 [2, 128], replicated, may hold values from -4 to 4
- in_bias: float32 [128], replicated, may hold values from -3 to 3
- conv_out: bfloat16 [2, 3, 3, 128], replicated, may hold values from -0.1875 to 0.1875
Outputs:
- refined: float32 [2, 32, 256], P(None, 'space', 'match')
The draws below stay inside these ranges and needn't reach their ends.
All inputs are finite; a program needn't handle non-finite values.
Results may differ from the reference program's by a relative error of at most 0.0066.
Values may be sent and summed in bfloat16 or wider, within the bound.
No kernel may reach another device: no remote copies, remote signals or barrier semaphores. Data moves between devices by JAX's collectives and lax.ppermute only.
A program may use at most 64 MiB of HBM per device.

```python
import math
import jax
import jax.numpy as jnp
from jax import lax

C = 128
NROWS = 32
WIDTH = 256
NT = 8192


def base_field(key, shape):
    return jax.random.normal(key, shape, jnp.float32)


def feature_pair(key):
    target_base = base_field(jax.random.fold_in(key, 11), (NT, C))
    source_base = base_field(jax.random.fold_in(key, 12), (NROWS * WIDTH, C))
    return (target_base, source_base, jax.random.fold_in(key, 13))


def draw_targets(key, part):
    target_base, source_base, noise_key = feature_pair(key)
    noise = jax.random.normal(noise_key, (NT, C), jnp.float32)
    before = jnp.roll(target_base, 1, axis=0)
    places = jnp.arange(NT, dtype=jnp.int32)
    near = places % 64 == 6
    result = jnp.where(near[:, None], before + 0.1 * noise, target_base)
    return result.astype(jnp.bfloat16)


def draw_source(key, part):
    target_base, source_base, noise_key = feature_pair(key)
    places = jnp.arange(NROWS * WIDTH, dtype=jnp.int32)
    picked = places % 97 == 3
    partner = 64 * (places * 13 % (NT // 64)) + 5
    strength = 20.0 + 10.0 * (places // 97 % 3).astype(jnp.float32)
    aligned = jnp.clip(strength[:, None] * target_base[partner], -200.0, 200.0)
    result = jnp.where(picked[:, None], aligned, source_base)
    return result.reshape(NROWS, WIDTH, C).astype(jnp.bfloat16)


def scatter_about(rng, shape, scale, bound, held_as=jnp.bfloat16):
    entries = jax.random.normal(rng, shape, jnp.float32) * scale
    return jnp.minimum(jnp.maximum(entries, -bound), bound).astype(held_as)


def setup_inputs(seed: int = 0) -> dict:
    seeds = jax.random.split(jax.random.key(seed), 7)
    return {
        "source": draw_source(jax.random.fold_in(seeds[6], 71), 0),
        "targets": draw_targets(jax.random.fold_in(seeds[6], 71), 0),
        "conv_in": scatter_about(seeds[2], (3, 3, C, C), (9 * C) ** -0.5, 0.1875),
        "flow_proj": scatter_about(seeds[3], (2, C), 2 ** -0.5, 4.0, jnp.float32),
        "in_bias": scatter_about(seeds[4], (C,), 0.5, 3.0, jnp.float32),
        "conv_out": scatter_about(seeds[5], (2, 3, 3, C), (9 * C) ** -0.5, 0.1875),
    }


def block_terms(query, keys, start, width):
    scale = 1.0 / math.sqrt(query.shape[1])
    scores = jnp.dot(query, keys.T, preferred_element_type=jnp.float32) * scale
    peak = lax.optimization_barrier(jnp.max(scores, axis=1))
    weight = jnp.exp(scores - peak[:, None])
    probs = weight.astype(jnp.bfloat16)
    total = lax.optimization_barrier(jnp.sum(weight, axis=1))
    accum = jnp.dot(probs, keys, preferred_element_type=jnp.float32)
    index = start + jnp.arange(keys.shape[0], dtype=jnp.int32)
    col_pos = (index % width).astype(jnp.float32) / width
    row_pos = (index // width).astype(jnp.float32) / width
    sum_x = lax.optimization_barrier(jnp.sum(weight * col_pos[None, :], axis=1))
    sum_y = lax.optimization_barrier(jnp.sum(weight * row_pos[None, :], axis=1))
    return (peak, total, accum, sum_x, sum_y)

def band_terms(queries, keys, start, width):
    count = queries.shape[0]
    step_rows = math.gcd(count, 512)
    blocks = queries.reshape(count // step_rows, step_rows, queries.shape[1])
    peak, total, accum, sum_x, sum_y = lax.map(lambda blk: block_terms(blk, keys, start, width), blocks)
    return (peak.reshape(count), total.reshape(count), accum.reshape(count, -1), sum_x.reshape(count), sum_y.reshape(count))

def reference(source, targets, conv_in, flow_proj, in_bias, conv_out):
    queries = source.reshape(NROWS * WIDTH, C)
    peak, total, accum, sum_x, sum_y = band_terms(queries, targets, 0, WIDTH)
    warped = (accum / total[:, None]).reshape(NROWS, WIDTH, C)
    col_pos = jnp.arange(WIDTH, dtype=jnp.float32) / WIDTH
    row_pos = jnp.arange(NROWS, dtype=jnp.float32) / WIDTH
    flow_x = (sum_x / total).reshape(NROWS, WIDTH) - col_pos[None, :]
    flow_y = (sum_y / total).reshape(NROWS, WIDTH) - row_pos[:, None]
    padded = jnp.pad(warped, ((1, 1), (1, 1), (0, 0)))
    pre = jnp.zeros((NROWS, WIDTH, C), jnp.float32)
    for tap_a in range(3):
        for tap_b in range(3):
            pre = pre + jnp.einsum('hwc,cd->hwd', padded[tap_a:tap_a + NROWS, tap_b:tap_b + WIDTH], conv_in[tap_a, tap_b].astype(jnp.float32), precision=lax.Precision.HIGHEST)
    pre = pre + flow_x[:, :, None] * flow_proj[0] + flow_y[:, :, None] * flow_proj[1] + in_bias
    hidden = jax.nn.silu(pre).astype(jnp.bfloat16)
    hpad = jnp.pad(hidden, ((1, 1), (1, 1), (0, 0)))
    delta = jnp.zeros((2, NROWS, WIDTH), jnp.float32)
    for tap_a in range(3):
        for tap_b in range(3):
            delta = delta + jnp.einsum('hwc,oc->ohw', hpad[tap_a:tap_a + NROWS, tap_b:tap_b + WIDTH].astype(jnp.float32), conv_out[:, tap_a, tap_b, :].astype(jnp.float32))
    return jnp.stack([flow_x, flow_y]) + delta
```

```python
import functools
import math

import jax
import jax.numpy as jnp
from jax import lax
from jax.experimental import pallas as pl
from jax.experimental.pallas import tpu as pltpu
from jax.sharding import PartitionSpec as P

HALO = 2


def extended(block, sides, width):
    for axis, dim in sides:
        count = lax.axis_size(axis)
        forward = [(i, i + 1) for i in range(count - 1)]
        backward = [(target, source) for source, target in forward]
        low = lax.ppermute(
            lax.slice_in_dim(block, block.shape[dim] - width, None, axis=dim), axis, forward
        )
        high = lax.ppermute(lax.slice_in_dim(block, 0, width, axis=dim), axis, backward)
        block = jnp.concatenate([low, block, high], axis=dim)
    return block


def match_kernel(q_ref, k_ref, pos_ref, warped_ref, flow_ref,
                 m_ref, acc_ref, tot_ref, sx_ref, sy_ref, *, scale, tk, nk):
    phase = pl.program_id(1)
    kb = pl.program_id(2)
    s = lax.dot_general(
        q_ref[...], k_ref[...], (((1,), (1,)), ((), ())),
        preferred_element_type=jnp.float32,
    ) * scale

    @pl.when((phase == 0) & (kb == 0))
    def _():
        m_ref[...] = jnp.full(m_ref.shape, -jnp.inf, jnp.float32)

    @pl.when(phase == 0)
    def _():
        m_ref[...] = jnp.maximum(m_ref[...], jnp.max(s, axis=1, keepdims=True))

    @pl.when((phase == 1) & (kb == 0))
    def _():
        acc_ref[...] = jnp.zeros(acc_ref.shape, jnp.float32)
        tot_ref[...] = jnp.zeros(tot_ref.shape, jnp.float32)
        sx_ref[...] = jnp.zeros(sx_ref.shape, jnp.float32)
        sy_ref[...] = jnp.zeros(sy_ref.shape, jnp.float32)

    @pl.when(phase == 1)
    def _():
        w = jnp.exp(s - m_ref[...])
        acc_ref[...] += jnp.dot(
            w.astype(jnp.bfloat16), k_ref[...], preferred_element_type=jnp.float32
        )
        tot = tot_ref[...]
        sx = sx_ref[...]
        sy = sy_ref[...]
        for c in range(tk // 128):
            part = w[:, c * 128:(c + 1) * 128]
            tot = tot + part
            sx = sx + part * pos_ref[0:1, c * 128:(c + 1) * 128]
            sy = sy + part * pos_ref[1:2, c * 128:(c + 1) * 128]
        tot_ref[...] = tot
        sx_ref[...] = sx
        sy_ref[...] = sy

    @pl.when((phase == 1) & (kb == nk - 1))
    def _():
        total = jnp.sum(tot_ref[...], axis=1, keepdims=True)
        warped_ref[...] = acc_ref[...] / total
        fx = jnp.sum(sx_ref[...], axis=1, keepdims=True) / total
        fy = jnp.sum(sy_ref[...], axis=1, keepdims=True) / total
        lane = lax.broadcasted_iota(jnp.int32, flow_ref.shape, 1)
        flow_ref[...] = jnp.where(lane == 0, fx, jnp.where(lane == 1, fy, 0.0))


def match(queries, keys, pos):
    count, chans = queries.shape
    total_keys = keys.shape[0]
    nq = -(-count // 1024)
    tq = -(-count // nq)
    tq = -(-tq // 8) * 8
    padded = tq * nq
    if padded != count:
        queries = jnp.pad(queries, ((0, padded - count), (0, 0)))
    tk = math.gcd(total_keys, 2048)
    nk = total_keys // tk
    kernel = functools.partial(
        match_kernel, scale=1.0 / math.sqrt(chans), tk=tk, nk=nk
    )
    warped, flow = pl.pallas_call(
        kernel,
        grid=(nq, 2, nk),
        in_specs=[
            pl.BlockSpec((tq, chans), lambda i, p, k: (i, 0)),
            pl.BlockSpec((tk, chans), lambda i, p, k: (k, 0)),
            pl.BlockSpec((8, tk), lambda i, p, k: (0, k)),
        ],
        out_specs=[
            pl.BlockSpec((tq, chans), lambda i, p, k: (i, 0)),
            pl.BlockSpec((tq, 128), lambda i, p, k: (i, 0)),
        ],
        out_shape=[
            jax.ShapeDtypeStruct((padded, chans), jnp.float32),
            jax.ShapeDtypeStruct((padded, 128), jnp.float32),
        ],
        scratch_shapes=[
            pltpu.VMEM((tq, 1), jnp.float32),
            pltpu.VMEM((tq, chans), jnp.float32),
            pltpu.VMEM((tq, 128), jnp.float32),
            pltpu.VMEM((tq, 128), jnp.float32),
            pltpu.VMEM((tq, 128), jnp.float32),
        ],
        compiler_params=pltpu.CompilerParams(
            dimension_semantics=("arbitrary", "arbitrary", "arbitrary"),
        ),
    )(queries, keys, pos)
    return warped[:count], flow[:count, 0], flow[:count, 1]


def local(source, targets, conv_in, flow_proj, in_bias, conv_out):
    rows, cols, chans = source.shape
    all_rows = rows * lax.axis_size("space")
    width = cols * lax.axis_size("match")
    row_first = lax.axis_index("space") * rows
    col_first = lax.axis_index("match") * cols
    keys = lax.all_gather(targets, "match", axis=0, tiled=True)
    index = jnp.arange(keys.shape[0], dtype=jnp.int32)
    pos = jnp.zeros((8, keys.shape[0]), jnp.float32)
    pos = pos.at[0].set((index % width).astype(jnp.float32) / width)
    pos = pos.at[1].set((index // width).astype(jnp.float32) / width)

    ext = extended(source, (("match", 1), ("space", 0)), HALO)
    erows, ecols = rows + 2 * HALO, cols + 2 * HALO
    warped, sum_x, sum_y = match(ext.reshape(erows * ecols, chans), keys, pos)
    warped = warped.reshape(erows, ecols, chans)
    grow = row_first - HALO + jnp.arange(erows, dtype=jnp.int32)
    gcol = col_first - HALO + jnp.arange(ecols, dtype=jnp.int32)
    inside = ((grow >= 0) & (grow < all_rows))[:, None] & ((gcol >= 0) & (gcol < width))[None, :]
    warped = jnp.where(inside[:, :, None], warped, 0.0)
    col_pos = gcol.astype(jnp.float32) / width
    row_pos = grow.astype(jnp.float32) / width
    flow_x = sum_x.reshape(erows, ecols) - col_pos[None, :]
    flow_y = sum_y.reshape(erows, ecols) - row_pos[:, None]

    pre = lax.conv_general_dilated(
        warped[None], conv_in.astype(jnp.float32), (1, 1), "VALID",
        dimension_numbers=("NHWC", "HWIO", "NHWC"),
        precision=lax.Precision.HIGHEST,
        preferred_element_type=jnp.float32,
    )[0]
    fx1 = flow_x[1:-1, 1:-1]
    fy1 = flow_y[1:-1, 1:-1]
    pre = pre + fx1[:, :, None] * flow_proj[0] + fy1[:, :, None] * flow_proj[1] + in_bias
    hidden = jax.nn.silu(pre).astype(jnp.bfloat16)
    hidden = jnp.where(inside[1:-1, 1:-1, None], hidden, jnp.zeros((), jnp.bfloat16))
    delta = lax.conv_general_dilated(
        hidden[None], jnp.transpose(conv_out, (1, 2, 3, 0)), (1, 1), "VALID",
        dimension_numbers=("NHWC", "HWIO", "NHWC"),
        preferred_element_type=jnp.float32,
    )[0]
    flows = jnp.stack([flow_x[HALO:-HALO, HALO:-HALO], flow_y[HALO:-HALO, HALO:-HALO]])
    return flows + jnp.transpose(delta, (2, 0, 1))


def solution(mesh):
    in_specs = (P("space", "match", None), P("match", None), P(), P(), P(), P())
    out_specs = P(None, "space", "match")
    return jax.shard_map(local, mesh=mesh, in_specs=in_specs, out_specs=out_specs, check_vma=False)
```

```python
import functools
import math

import jax
import jax.numpy as jnp
from jax import lax
from jax.experimental import pallas as pl
from jax.experimental.pallas import tpu as pltpu
from jax.sharding import PartitionSpec as P

HALO = 2


def extended(block, sides, width):
    for axis, dim in sides:
        count = lax.axis_size(axis)
        forward = [(i, i + 1) for i in range(count - 1)]
        backward = [(target, source) for source, target in forward]
        low = lax.ppermute(
            lax.slice_in_dim(block, block.shape[dim] - width, None, axis=dim), axis, forward
        )
        high = lax.ppermute(lax.slice_in_dim(block, 0, width, axis=dim), axis, backward)
        block = jnp.concatenate([low, block, high], axis=dim)
    return block


def shard_kernel(*refs, scale, chans, first, last):
    if first:
        q_ref, km_ref = refs[:2]
        outs = refs[2:]
    else:
        q_ref, km_ref, m_ref, acc_ref, st_ref = refs[:5]
        outs = refs[5:]
    s = lax.dot_general(
        q_ref[...], km_ref[:, 0:chans], (((1,), (1,)), ((), ())),
        preferred_element_type=jnp.float32,
    ) * scale
    peak = jnp.max(s, axis=1, keepdims=True)
    if not first:
        old = m_ref[:, 0:1]
        peak = jnp.maximum(old, peak)
    w = jnp.exp(s - peak)
    hi = w.astype(jnp.bfloat16)
    lo = (w - hi.astype(jnp.float32)).astype(jnp.bfloat16)
    both = jnp.dot(hi, km_ref[...], preferred_element_type=jnp.float32)
    acc = both[:, 0:chans]
    st = both[:, chans:] + jnp.dot(
        lo, km_ref[:, chans:], preferred_element_type=jnp.float32
    )
    if not first:
        alpha = jnp.exp(old - peak)
        acc = acc_ref[...] * alpha + acc
        st = st_ref[...] * alpha + st
    if last:
        warped_ref, flow_ref = outs
        total = st[:, 0:1]
        warped_ref[...] = acc / total
        fx = (st[:, 1:2] + st[:, 2:3]) / total
        fy = (st[:, 3:4] + st[:, 4:5]) / total
        lane = lax.broadcasted_iota(jnp.int32, flow_ref.shape, 1)
        flow_ref[...] = jnp.where(lane == 0, fx, jnp.where(lane == 1, fy, 0.0))
    else:
        m_out, acc_out, st_out = outs
        m_out[...] = jnp.broadcast_to(peak, m_out.shape)
        acc_out[...] = acc
        st_out[...] = st


def split_bf16(x):
    hi = x.astype(jnp.bfloat16)
    return hi, (x - hi.astype(jnp.float32)).astype(jnp.bfloat16)


def with_positions(keys, offset, width):
    count = keys.shape[0]
    index = offset + jnp.arange(count, dtype=jnp.int32)
    col_hi, col_lo = split_bf16((index % width).astype(jnp.float32) / width)
    row_hi, row_lo = split_bf16((index // width).astype(jnp.float32) / width)
    cols = jnp.stack(
        [jnp.ones((count,), jnp.bfloat16), col_hi, col_lo, row_hi, row_lo], axis=1
    )
    cols = jnp.pad(cols, ((0, 0), (0, 128 - cols.shape[1])))
    return jnp.concatenate([keys, cols], axis=1)


def match_step(queries, km, state, tq, first, last):
    padded, chans = queries.shape
    nq = padded // tq
    tk = km.shape[0]
    kernel = functools.partial(
        shard_kernel, scale=1.0 / math.sqrt(chans), chans=chans, first=first, last=last
    )
    row_spec = lambda width: pl.BlockSpec((tq, width), lambda i: (i, 0))
    in_specs = [row_spec(chans), pl.BlockSpec((tk, km.shape[1]), lambda i: (0, 0))]
    args = [queries, km]
    if not first:
        in_specs += [row_spec(128), row_spec(chans), row_spec(128)]
        args += list(state)
    if last:
        out_specs = [row_spec(chans), row_spec(128)]
        out_shape = [
            jax.ShapeDtypeStruct((padded, chans), jnp.float32),
            jax.ShapeDtypeStruct((padded, 128), jnp.float32),
        ]
    else:
        out_specs = [row_spec(128), row_spec(chans), row_spec(128)]
        out_shape = [
            jax.ShapeDtypeStruct((padded, 128), jnp.float32),
            jax.ShapeDtypeStruct((padded, chans), jnp.float32),
            jax.ShapeDtypeStruct((padded, 128), jnp.float32),
        ]
    return pl.pallas_call(
        kernel,
        grid=(nq,),
        in_specs=in_specs,
        out_specs=out_specs,
        out_shape=out_shape,
        compiler_params=pltpu.CompilerParams(dimension_semantics=("arbitrary",)),
    )(*args)


def match(queries, targets, width):
    count, chans = queries.shape
    tk = targets.shape[0]
    cap = max(8, (1024 * 2048 // tk) // 8 * 8)
    nq = -(-count // cap)
    tq = -(-(-(-count // nq)) // 8) * 8
    padded = tq * nq
    if padded != count:
        queries = jnp.pad(queries, ((0, padded - count), (0, 0)))
    n = lax.axis_size("match")
    me = lax.axis_index("match")
    shards = [(targets, me)]
    for shift in range(1, n):
        moved = lax.ppermute(targets, "match", [(j, (j + shift) % n) for j in range(n)])
        shards.append((moved, (me - shift) % n))
    state = None
    for step, (keys, owner) in enumerate(shards):
        km = with_positions(keys, owner * tk, width)
        state = match_step(queries, km, state, tq, step == 0, step == n - 1)
    warped, flow = state
    return warped[:count], flow[:count, 0], flow[:count, 1]


def local(source, targets, conv_in, flow_proj, in_bias, conv_out):
    rows, cols, chans = source.shape
    all_rows = rows * lax.axis_size("space")
    width = cols * lax.axis_size("match")
    row_first = lax.axis_index("space") * rows
    col_first = lax.axis_index("match") * cols
    ext = extended(source, (("match", 1), ("space", 0)), HALO)
    erows, ecols = rows + 2 * HALO, cols + 2 * HALO
    warped, sum_x, sum_y = match(ext.reshape(erows * ecols, chans), targets, width)
    warped = warped.reshape(erows, ecols, chans)
    grow = row_first - HALO + jnp.arange(erows, dtype=jnp.int32)
    gcol = col_first - HALO + jnp.arange(ecols, dtype=jnp.int32)
    inside = ((grow >= 0) & (grow < all_rows))[:, None] & ((gcol >= 0) & (gcol < width))[None, :]
    warped = jnp.where(inside[:, :, None], warped, 0.0)
    col_pos = gcol.astype(jnp.float32) / width
    row_pos = grow.astype(jnp.float32) / width
    flow_x = sum_x.reshape(erows, ecols) - col_pos[None, :]
    flow_y = sum_y.reshape(erows, ecols) - row_pos[:, None]

    pre = lax.conv_general_dilated(
        warped[None], conv_in.astype(jnp.float32), (1, 1), "VALID",
        dimension_numbers=("NHWC", "HWIO", "NHWC"),
        precision=lax.Precision.HIGHEST,
        preferred_element_type=jnp.float32,
    )[0]
    fx1 = flow_x[1:-1, 1:-1]
    fy1 = flow_y[1:-1, 1:-1]
    pre = pre + fx1[:, :, None] * flow_proj[0] + fy1[:, :, None] * flow_proj[1] + in_bias
    hidden = jax.nn.silu(pre).astype(jnp.bfloat16)
    hidden = jnp.where(inside[1:-1, 1:-1, None], hidden, jnp.zeros((), jnp.bfloat16))
    delta = lax.conv_general_dilated(
        hidden[None], jnp.transpose(conv_out, (1, 2, 3, 0)), (1, 1), "VALID",
        dimension_numbers=("NHWC", "HWIO", "NHWC"),
        preferred_element_type=jnp.float32,
    )[0]
    flows = jnp.stack([flow_x[HALO:-HALO, HALO:-HALO], flow_y[HALO:-HALO, HALO:-HALO]])
    return flows + jnp.transpose(delta, (2, 0, 1))


def solution(mesh):
    in_specs = (P("space", "match", None), P("match", None), P(), P(), P(), P())
    out_specs = P(None, "space", "match")
    return jax.shard_map(local, mesh=mesh, in_specs=in_specs, out_specs=out_specs, check_vma=False)
```

```python
import functools
import math

import jax
import jax.numpy as jnp
from jax import lax
from jax.experimental import pallas as pl
from jax.experimental.pallas import tpu as pltpu
from jax.sharding import PartitionSpec as P

HALO = 2


def extended(block, sides, width):
    for axis, dim in sides:
        count = lax.axis_size(axis)
        forward = [(i, i + 1) for i in range(count - 1)]
        backward = [(target, source) for source, target in forward]
        low = lax.ppermute(
            lax.slice_in_dim(block, block.shape[dim] - width, None, axis=dim), axis, forward
        )
        high = lax.ppermute(lax.slice_in_dim(block, 0, width, axis=dim), axis, backward)
        block = jnp.concatenate([low, block, high], axis=dim)
    return block


def shard_kernel(*refs, scale, chans, first, last):
    if first:
        q_ref, k_ref, pos_ref = refs[:3]
        outs = refs[3:]
    else:
        q_ref, k_ref, pos_ref, m_ref, acc_ref, st_ref = refs[:6]
        outs = refs[6:]
    s = lax.dot_general(
        q_ref[...], k_ref[...], (((1,), (1,)), ((), ())),
        preferred_element_type=jnp.float32,
    ) * scale
    peak = jnp.max(s, axis=1, keepdims=True)
    if not first:
        old = m_ref[:, 0:1]
        peak = jnp.maximum(old, peak)
    w = jnp.exp(s - peak)
    hi = w.astype(jnp.bfloat16)
    lo = (w - hi.astype(jnp.float32)).astype(jnp.bfloat16)
    acc = jnp.dot(hi, k_ref[...], preferred_element_type=jnp.float32)
    st = jnp.dot(hi, pos_ref[...], preferred_element_type=jnp.float32) + jnp.dot(
        lo, pos_ref[...], preferred_element_type=jnp.float32
    )
    if not first:
        alpha = jnp.exp(old - peak)
        acc = acc_ref[...] * alpha + acc
        st = st_ref[...] * alpha + st
    if last:
        warped_ref, flow_ref = outs
        total = st[:, 0:1]
        warped_ref[...] = acc / total
        fx = (st[:, 1:2] + st[:, 2:3]) / total
        fy = (st[:, 3:4] + st[:, 4:5]) / total
        lane = lax.broadcasted_iota(jnp.int32, flow_ref.shape, 1)
        flow_ref[...] = jnp.where(lane == 0, fx, jnp.where(lane == 1, fy, 0.0))
    else:
        m_out, acc_out, st_out = outs
        m_out[...] = jnp.broadcast_to(peak, m_out.shape)
        acc_out[...] = acc
        st_out[...] = st


def split_bf16(x):
    hi = x.astype(jnp.bfloat16)
    return hi, (x - hi.astype(jnp.float32)).astype(jnp.bfloat16)


def positions(count, offset, width):
    index = offset + jnp.arange(count, dtype=jnp.int32)
    col_hi, col_lo = split_bf16((index % width).astype(jnp.float32) / width)
    row_hi, row_lo = split_bf16((index // width).astype(jnp.float32) / width)
    cols = jnp.stack(
        [jnp.ones((count,), jnp.bfloat16), col_hi, col_lo, row_hi, row_lo], axis=1
    )
    return jnp.pad(cols, ((0, 0), (0, 128 - cols.shape[1])))


def match_step(queries, keys, pos, state, tq, first, last):
    padded, chans = queries.shape
    nq = padded // tq
    tk = keys.shape[0]
    kernel = functools.partial(
        shard_kernel, scale=1.0 / math.sqrt(chans), chans=chans, first=first, last=last
    )
    row_spec = lambda width: pl.BlockSpec((tq, width), lambda i: (i, 0))
    in_specs = [
        row_spec(chans),
        pl.BlockSpec((tk, chans), lambda i: (0, 0)),
        pl.BlockSpec((tk, 128), lambda i: (0, 0)),
    ]
    args = [queries, keys, pos]
    if not first:
        in_specs += [row_spec(128), row_spec(chans), row_spec(128)]
        args += list(state)
    if last:
        out_specs = [row_spec(chans), row_spec(128)]
        out_shape = [
            jax.ShapeDtypeStruct((padded, chans), jnp.float32),
            jax.ShapeDtypeStruct((padded, 128), jnp.float32),
        ]
    else:
        out_specs = [row_spec(128), row_spec(chans), row_spec(128)]
        out_shape = [
            jax.ShapeDtypeStruct((padded, 128), jnp.float32),
            jax.ShapeDtypeStruct((padded, chans), jnp.float32),
            jax.ShapeDtypeStruct((padded, 128), jnp.float32),
        ]
    return pl.pallas_call(
        kernel,
        grid=(nq,),
        in_specs=in_specs,
        out_specs=out_specs,
        out_shape=out_shape,
        compiler_params=pltpu.CompilerParams(dimension_semantics=("arbitrary",)),
    )(*args)


def match(queries, targets, width):
    count, chans = queries.shape
    tk = targets.shape[0]
    cap = max(8, (1024 * 2048 // tk) // 8 * 8)
    nq = -(-count // cap)
    tq = -(-(-(-count // nq)) // 8) * 8
    padded = tq * nq
    if padded != count:
        queries = jnp.pad(queries, ((0, padded - count), (0, 0)))
    n = lax.axis_size("match")
    me = lax.axis_index("match")
    shards = [(targets, me)]
    for shift in range(1, n):
        moved = lax.ppermute(targets, "match", [(j, (j + shift) % n) for j in range(n)])
        shards.append((moved, (me - shift) % n))
    state = None
    for step, (keys, owner) in enumerate(shards):
        pos = positions(tk, owner * tk, width)
        state = match_step(queries, keys, pos, state, tq, step == 0, step == n - 1)
    warped, flow = state
    return warped[:count], flow[:count, 0], flow[:count, 1]


def local(source, targets, conv_in, flow_proj, in_bias, conv_out):
    rows, cols, chans = source.shape
    all_rows = rows * lax.axis_size("space")
    width = cols * lax.axis_size("match")
    row_first = lax.axis_index("space") * rows
    col_first = lax.axis_index("match") * cols
    ext = extended(source, (("match", 1),), HALO)
    targets, ext = lax.optimization_barrier((targets, ext))
    ext = extended(ext, (("space", 0),), HALO)
    erows, ecols = rows + 2 * HALO, cols + 2 * HALO
    warped, sum_x, sum_y = match(ext.reshape(erows * ecols, chans), targets, width)
    warped = warped.reshape(erows, ecols, chans)
    grow = row_first - HALO + jnp.arange(erows, dtype=jnp.int32)
    gcol = col_first - HALO + jnp.arange(ecols, dtype=jnp.int32)
    inside = ((grow >= 0) & (grow < all_rows))[:, None] & ((gcol >= 0) & (gcol < width))[None, :]
    warped = jnp.where(inside[:, :, None], warped, 0.0)
    col_pos = gcol.astype(jnp.float32) / width
    row_pos = grow.astype(jnp.float32) / width
    flow_x = sum_x.reshape(erows, ecols) - col_pos[None, :]
    flow_y = sum_y.reshape(erows, ecols) - row_pos[:, None]

    pre = lax.conv_general_dilated(
        warped[None], conv_in.astype(jnp.float32), (1, 1), "VALID",
        dimension_numbers=("NHWC", "HWIO", "NHWC"),
        precision=lax.Precision.HIGHEST,
        preferred_element_type=jnp.float32,
    )[0]
    fx1 = flow_x[1:-1, 1:-1]
    fy1 = flow_y[1:-1, 1:-1]
    pre = pre + fx1[:, :, None] * flow_proj[0] + fy1[:, :, None] * flow_proj[1] + in_bias
    hidden = jax.nn.silu(pre).astype(jnp.bfloat16)
    hidden = jnp.where(inside[1:-1, 1:-1, None], hidden, jnp.zeros((), jnp.bfloat16))
    delta = lax.conv_general_dilated(
        hidden[None], jnp.transpose(conv_out, (1, 2, 3, 0)), (1, 1), "VALID",
        dimension_numbers=("NHWC", "HWIO", "NHWC"),
        preferred_element_type=jnp.float32,
    )[0]
    flows = jnp.stack([flow_x[HALO:-HALO, HALO:-HALO], flow_y[HALO:-HALO, HALO:-HALO]])
    return flows + jnp.transpose(delta, (2, 0, 1))


def solution(mesh):
    in_specs = (P("space", "match", None), P("match", None), P(), P(), P(), P())
    out_specs = P(None, "space", "match")
    return jax.shard_map(local, mesh=mesh, in_specs=in_specs, out_specs=out_specs, check_vma=False)
```

```python
import functools
import math

import jax
import jax.numpy as jnp
from jax import lax
from jax.experimental import pallas as pl
from jax.experimental.pallas import tpu as pltpu
from jax.sharding import PartitionSpec as P

HALO = 2


def extended(block, sides, width):
    for axis, dim in sides:
        count = lax.axis_size(axis)
        forward = [(i, i + 1) for i in range(count - 1)]
        backward = [(target, source) for source, target in forward]
        low = lax.ppermute(
            lax.slice_in_dim(block, block.shape[dim] - width, None, axis=dim), axis, forward
        )
        high = lax.ppermute(lax.slice_in_dim(block, 0, width, axis=dim), axis, backward)
        block = jnp.concatenate([low, block, high], axis=dim)
    return block


def shard_kernel(*refs, scale, chans, first, last):
    if first:
        q_ref, k_ref, pos_ref = refs[:3]
        outs = refs[3:]
    else:
        q_ref, k_ref, pos_ref, m_ref, acc_ref, st_ref = refs[:6]
        outs = refs[6:]
    s = lax.dot_general(
        q_ref[...], k_ref[...], (((1,), (1,)), ((), ())),
        preferred_element_type=jnp.float32,
    ) * scale
    peak = jnp.max(s, axis=1, keepdims=True)
    if not first:
        old = m_ref[:, 0:1]
        peak = jnp.maximum(old, peak)
    w = jnp.exp(s - peak)
    hi = w.astype(jnp.bfloat16)
    lo = (w - hi.astype(jnp.float32)).astype(jnp.bfloat16)
    acc = jnp.dot(hi, k_ref[...], preferred_element_type=jnp.float32)
    st = jnp.dot(hi, pos_ref[...], preferred_element_type=jnp.float32) + jnp.dot(
        lo, pos_ref[...], preferred_element_type=jnp.float32
    )
    if not first:
        alpha = jnp.exp(old - peak)
        acc = acc_ref[...] * alpha + acc
        st = st_ref[...] * alpha + st
    if last:
        (out_ref,) = outs
        total = st[:, 0:1]
        out_ref[:, 0:chans] = acc / total
        fx = (st[:, 1:2] + st[:, 2:3]) / total
        fy = (st[:, 3:4] + st[:, 4:5]) / total
        lane = lax.broadcasted_iota(jnp.int32, (st.shape[0], 128), 1)
        out_ref[:, chans:] = jnp.where(lane == 0, fx, jnp.where(lane == 1, fy, 0.0))
    else:
        m_out, acc_out, st_out = outs
        m_out[...] = jnp.broadcast_to(peak, m_out.shape)
        acc_out[...] = acc
        st_out[...] = st


def split_bf16(x):
    hi = x.astype(jnp.bfloat16)
    return hi, (x - hi.astype(jnp.float32)).astype(jnp.bfloat16)


def positions(count, offset, width):
    index = offset + jnp.arange(count, dtype=jnp.int32)[:, None]
    col_hi, col_lo = split_bf16((index % width).astype(jnp.float32) / width)
    row_hi, row_lo = split_bf16((index // width).astype(jnp.float32) / width)
    lane = jnp.arange(128, dtype=jnp.int32)[None, :]
    zero = jnp.zeros((), jnp.bfloat16)
    pos = jnp.where(lane == 4, row_lo, zero)
    pos = jnp.where(lane == 3, row_hi, pos)
    pos = jnp.where(lane == 2, col_lo, pos)
    pos = jnp.where(lane == 1, col_hi, pos)
    return jnp.where(lane == 0, jnp.ones((), jnp.bfloat16), pos)


def match_step(queries, keys, pos, state, tq, first, last):
    padded, chans = queries.shape
    nq = padded // tq
    tk = keys.shape[0]
    kernel = functools.partial(
        shard_kernel, scale=1.0 / math.sqrt(chans), chans=chans, first=first, last=last
    )
    row_spec = lambda width: pl.BlockSpec((tq, width), lambda i: (i, 0))
    in_specs = [
        row_spec(chans),
        pl.BlockSpec((tk, chans), lambda i: (0, 0)),
        pl.BlockSpec((tk, 128), lambda i: (0, 0)),
    ]
    args = [queries, keys, pos]
    if not first:
        in_specs += [row_spec(128), row_spec(chans), row_spec(128)]
        args += list(state)
    if last:
        out_specs = [row_spec(chans + 128)]
        out_shape = [jax.ShapeDtypeStruct((padded, chans + 128), jnp.float32)]
    else:
        out_specs = [row_spec(128), row_spec(chans), row_spec(128)]
        out_shape = [
            jax.ShapeDtypeStruct((padded, 128), jnp.float32),
            jax.ShapeDtypeStruct((padded, chans), jnp.float32),
            jax.ShapeDtypeStruct((padded, 128), jnp.float32),
        ]
    return pl.pallas_call(
        kernel,
        grid=(nq,),
        in_specs=in_specs,
        out_specs=out_specs,
        out_shape=out_shape,
        compiler_params=pltpu.CompilerParams(dimension_semantics=("arbitrary",)),
    )(*args)


def match(queries, targets, width):
    count, chans = queries.shape
    tk = targets.shape[0]
    cap = max(8, (1024 * 2048 // tk) // 8 * 8)
    nq = -(-count // cap)
    tq = -(-(-(-count // nq)) // 8) * 8
    padded = tq * nq
    if padded != count:
        queries = jnp.pad(queries, ((0, padded - count), (0, 0)))
    n = lax.axis_size("match")
    me = lax.axis_index("match")
    shards = [(targets, me)]
    for shift in range(1, n):
        moved = lax.ppermute(targets, "match", [(j, (j + shift) % n) for j in range(n)])
        shards.append((moved, (me - shift) % n))
    state = None
    for step, (keys, owner) in enumerate(shards):
        pos = positions(tk, owner * tk, width)
        state = match_step(queries, keys, pos, state, tq, step == 0, step == n - 1)
    (out,) = state
    return out[:count]


def local(source, targets, conv_in, flow_proj, in_bias, conv_out):
    rows, cols, chans = source.shape
    all_rows = rows * lax.axis_size("space")
    width = cols * lax.axis_size("match")
    row_first = lax.axis_index("space") * rows
    col_first = lax.axis_index("match") * cols
    out = match(source.reshape(rows * cols, chans), targets, width)
    ext = extended(out.reshape(rows, cols, out.shape[1]), (("match", 1), ("space", 0)), HALO)
    erows, ecols = rows + 2 * HALO, cols + 2 * HALO
    grow = row_first - HALO + jnp.arange(erows, dtype=jnp.int32)
    gcol = col_first - HALO + jnp.arange(ecols, dtype=jnp.int32)
    inside = ((grow >= 0) & (grow < all_rows))[:, None] & ((gcol >= 0) & (gcol < width))[None, :]
    warped = jnp.where(inside[:, :, None], ext[:, :, 0:chans], 0.0)
    col_pos = gcol.astype(jnp.float32) / width
    row_pos = grow.astype(jnp.float32) / width
    flow_x = ext[:, :, chans] - col_pos[None, :]
    flow_y = ext[:, :, chans + 1] - row_pos[:, None]

    pre = lax.conv_general_dilated(
        warped[None], conv_in.astype(jnp.float32), (1, 1), "VALID",
        dimension_numbers=("NHWC", "HWIO", "NHWC"),
        precision=lax.Precision.HIGHEST,
        preferred_element_type=jnp.float32,
    )[0]
    fx1 = flow_x[1:-1, 1:-1]
    fy1 = flow_y[1:-1, 1:-1]
    pre = pre + fx1[:, :, None] * flow_proj[0] + fy1[:, :, None] * flow_proj[1] + in_bias
    hidden = jax.nn.silu(pre).astype(jnp.bfloat16)
    hidden = jnp.where(inside[1:-1, 1:-1, None], hidden, jnp.zeros((), jnp.bfloat16))
    delta = lax.conv_general_dilated(
        hidden[None], jnp.transpose(conv_out, (1, 2, 3, 0)), (1, 1), "VALID",
        dimension_numbers=("NHWC", "HWIO", "NHWC"),
        preferred_element_type=jnp.float32,
    )[0]
    flows = jnp.stack([flow_x[HALO:-HALO, HALO:-HALO], flow_y[HALO:-HALO, HALO:-HALO]])
    return flows + jnp.transpose(delta, (2, 0, 1))


def solution(mesh):
    in_specs = (P("space", "match", None), P("match", None), P(), P(), P(), P())
    out_specs = P(None, "space", "match")
    return jax.shard_map(local, mesh=mesh, in_specs=in_specs, out_specs=out_specs, check_vma=False)
```

```python
import functools
import math

import jax
import jax.numpy as jnp
from jax import lax
from jax.experimental import pallas as pl
from jax.experimental.pallas import tpu as pltpu
from jax.sharding import PartitionSpec as P

HALO = 2


def extended(block, sides, width):
    for axis, dim in sides:
        count = lax.axis_size(axis)
        forward = [(i, i + 1) for i in range(count - 1)]
        backward = [(target, source) for source, target in forward]
        low = lax.ppermute(
            lax.slice_in_dim(block, block.shape[dim] - width, None, axis=dim), axis, forward
        )
        high = lax.ppermute(lax.slice_in_dim(block, 0, width, axis=dim), axis, backward)
        block = jnp.concatenate([low, block, high], axis=dim)
    return block


def shard_kernel(*refs, scale, chans, first, last):
    if first:
        q_ref, k_ref, pos_ref = refs[:3]
        outs = refs[3:]
    else:
        q_ref, k_ref, pos_ref, m_ref, acc_ref, st_ref = refs[:6]
        outs = refs[6:]
    s = lax.dot_general(
        q_ref[...], k_ref[...], (((1,), (1,)), ((), ())),
        preferred_element_type=jnp.float32,
    ) * scale
    peak = jnp.max(s, axis=1, keepdims=True)
    if not first:
        old = m_ref[:, 0:1]
        peak = jnp.maximum(old, peak)
    w = jnp.exp(s - peak)
    hi = w.astype(jnp.bfloat16)
    lo = (w - hi.astype(jnp.float32)).astype(jnp.bfloat16)
    acc = jnp.dot(hi, k_ref[...], preferred_element_type=jnp.float32)
    lanes = (((1,), (1,)), ((), ()))
    st = lax.dot_general(
        hi, pos_ref[...], lanes, preferred_element_type=jnp.float32
    ) + lax.dot_general(lo, pos_ref[...], lanes, preferred_element_type=jnp.float32)
    if not first:
        alpha = jnp.exp(old - peak)
        acc = acc_ref[...] * alpha + acc
        st = st_ref[...] * alpha + st
    if last:
        warped_ref, flow_ref = outs
        total = st[:, 0:1]
        warped_ref[...] = acc / total
        fx = (st[:, 1:2] + st[:, 2:3]) / total
        fy = (st[:, 3:4] + st[:, 4:5]) / total
        lane = lax.broadcasted_iota(jnp.int32, flow_ref.shape, 1)
        flow_ref[...] = jnp.where(lane == 0, fx, jnp.where(lane == 1, fy, 0.0))
    else:
        m_out, acc_out, st_out = outs
        m_out[...] = jnp.broadcast_to(peak, m_out.shape)
        acc_out[...] = acc
        st_out[...] = st


def split_bf16(x):
    hi = x.astype(jnp.bfloat16)
    return hi, (x - hi.astype(jnp.float32)).astype(jnp.bfloat16)


def positions(count, offset, width):
    index = offset + jnp.arange(count, dtype=jnp.int32)
    col_hi, col_lo = split_bf16((index % width).astype(jnp.float32) / width)
    row_hi, row_lo = split_bf16((index // width).astype(jnp.float32) / width)
    zero = jnp.zeros((count,), jnp.bfloat16)
    one = jnp.ones((count,), jnp.bfloat16)
    return jnp.stack([one, col_hi, col_lo, row_hi, row_lo, zero, zero, zero])


def match_step(queries, keys, pos, state, tq, first, last):
    padded, chans = queries.shape
    nq = padded // tq
    tk = keys.shape[0]
    kernel = functools.partial(
        shard_kernel, scale=1.0 / math.sqrt(chans), chans=chans, first=first, last=last
    )
    row_spec = lambda width: pl.BlockSpec((tq, width), lambda i: (i, 0))
    in_specs = [
        row_spec(chans),
        pl.BlockSpec((tk, chans), lambda i: (0, 0)),
        pl.BlockSpec((8, tk), lambda i: (0, 0)),
    ]
    args = [queries, keys, pos]
    if not first:
        in_specs += [row_spec(128), row_spec(chans), row_spec(8)]
        args += list(state)
    if last:
        out_specs = [row_spec(chans), row_spec(128)]
        out_shape = [
            jax.ShapeDtypeStruct((padded, chans), jnp.float32),
            jax.ShapeDtypeStruct((padded, 128), jnp.float32),
        ]
    else:
        out_specs = [row_spec(128), row_spec(chans), row_spec(8)]
        out_shape = [
            jax.ShapeDtypeStruct((padded, 128), jnp.float32),
            jax.ShapeDtypeStruct((padded, chans), jnp.float32),
            jax.ShapeDtypeStruct((padded, 8), jnp.float32),
        ]
    return pl.pallas_call(
        kernel,
        grid=(nq,),
        in_specs=in_specs,
        out_specs=out_specs,
        out_shape=out_shape,
        compiler_params=pltpu.CompilerParams(dimension_semantics=("arbitrary",)),
    )(*args)


def match(queries, targets, width):
    count, chans = queries.shape
    tk = targets.shape[0]
    cap = max(8, (1024 * 2048 // tk) // 8 * 8)
    nq = -(-count // cap)
    tq = -(-(-(-count // nq)) // 8) * 8
    padded = tq * nq
    if padded != count:
        queries = jnp.pad(queries, ((0, padded - count), (0, 0)))
    n = lax.axis_size("match")
    me = lax.axis_index("match")
    shards = [(targets, me)]
    for shift in range(1, n):
        moved = lax.ppermute(targets, "match", [(j, (j + shift) % n) for j in range(n)])
        shards.append((moved, (me - shift) % n))
    state = None
    for step, (keys, owner) in enumerate(shards):
        pos = positions(tk, owner * tk, width)
        state = match_step(queries, keys, pos, state, tq, step == 0, step == n - 1)
    warped, flow = state
    return warped[:count], flow[:count, 0], flow[:count, 1]


def local(source, targets, conv_in, flow_proj, in_bias, conv_out):
    rows, cols, chans = source.shape
    all_rows = rows * lax.axis_size("space")
    width = cols * lax.axis_size("match")
    row_first = lax.axis_index("space") * rows
    col_first = lax.axis_index("match") * cols
    ext = extended(source, (("match", 1),), HALO)
    targets, ext = lax.optimization_barrier((targets, ext))
    ext = extended(ext, (("space", 0),), HALO)
    erows, ecols = rows + 2 * HALO, cols + 2 * HALO
    warped, sum_x, sum_y = match(ext.reshape(erows * ecols, chans), targets, width)
    warped = warped.reshape(erows, ecols, chans)
    grow = row_first - HALO + jnp.arange(erows, dtype=jnp.int32)
    gcol = col_first - HALO + jnp.arange(ecols, dtype=jnp.int32)
    inside = ((grow >= 0) & (grow < all_rows))[:, None] & ((gcol >= 0) & (gcol < width))[None, :]
    warped = jnp.where(inside[:, :, None], warped, 0.0)
    col_pos = gcol.astype(jnp.float32) / width
    row_pos = grow.astype(jnp.float32) / width
    flow_x = sum_x.reshape(erows, ecols) - col_pos[None, :]
    flow_y = sum_y.reshape(erows, ecols) - row_pos[:, None]

    pre = lax.conv_general_dilated(
        warped[None], conv_in.astype(jnp.float32), (1, 1), "VALID",
        dimension_numbers=("NHWC", "HWIO", "NHWC"),
        precision=lax.Precision.HIGHEST,
        preferred_element_type=jnp.float32,
    )[0]
    fx1 = flow_x[1:-1, 1:-1]
    fy1 = flow_y[1:-1, 1:-1]
    pre = pre + fx1[:, :, None] * flow_proj[0] + fy1[:, :, None] * flow_proj[1] + in_bias
    hidden = jax.nn.silu(pre).astype(jnp.bfloat16)
    hidden = jnp.where(inside[1:-1, 1:-1, None], hidden, jnp.zeros((), jnp.bfloat16))
    delta = lax.conv_general_dilated(
        hidden[None], jnp.transpose(conv_out, (1, 2, 3, 0)), (1, 1), "VALID",
        dimension_numbers=("NHWC", "HWIO", "NHWC"),
        preferred_element_type=jnp.float32,
    )[0]
    flows = jnp.stack([flow_x[HALO:-HALO, HALO:-HALO], flow_y[HALO:-HALO, HALO:-HALO]])
    return flows + jnp.transpose(delta, (2, 0, 1))


def solution(mesh):
    in_specs = (P("space", "match", None), P("match", None), P(), P(), P(), P())
    out_specs = P(None, "space", "match")
    return jax.shard_map(local, mesh=mesh, in_specs=in_specs, out_specs=out_specs, check_vma=False)
```

```python
import functools
import math

import jax
import jax.numpy as jnp
from jax import lax
from jax.experimental import pallas as pl
from jax.experimental.pallas import tpu as pltpu
from jax.sharding import PartitionSpec as P

HALO = 2


def extended(block, sides, width):
    for axis, dim in sides:
        count = lax.axis_size(axis)
        forward = [(i, i + 1) for i in range(count - 1)]
        backward = [(target, source) for source, target in forward]
        low = lax.ppermute(
            lax.slice_in_dim(block, block.shape[dim] - width, None, axis=dim), axis, forward
        )
        high = lax.ppermute(lax.slice_in_dim(block, 0, width, axis=dim), axis, backward)
        block = jnp.concatenate([low, block, high], axis=dim)
    return block


def row_sums(w, base_ref, width):
    area = w[:, 0:width]
    weighted = None
    for g in range(1, w.shape[1] // width):
        part = w[:, g * width:(g + 1) * width]
        area = area + part
        weighted = part * float(g) if weighted is None else weighted + part * float(g)
    lane = lax.broadcasted_iota(jnp.int32, (1, width), 1)
    col = lane.astype(jnp.float32) / width
    total = jnp.sum(area, axis=1, keepdims=True)
    sum_x = jnp.sum(area * col, axis=1, keepdims=True)
    local = jnp.zeros_like(total) if weighted is None else jnp.sum(weighted, axis=1, keepdims=True)
    sum_y = (base_ref[0:1, 0:1] * total + local) / width
    lane8 = lax.broadcasted_iota(jnp.int32, (w.shape[0], 8), 1)
    zero = jnp.zeros((), jnp.float32)
    return jnp.where(lane8 == 0, total, jnp.where(lane8 == 1, sum_x, jnp.where(lane8 == 3, sum_y, zero)))


def shard_kernel(*refs, scale, chans, first, last, width):
    if first:
        q_ref, k_ref, pos_ref = refs[:3]
        outs = refs[3:]
    else:
        q_ref, k_ref, pos_ref, m_ref, acc_ref, st_ref = refs[:6]
        outs = refs[6:]
    s = lax.dot_general(
        q_ref[...], k_ref[...], (((1,), (1,)), ((), ())),
        preferred_element_type=jnp.float32,
    ) * scale
    peak = jnp.max(s, axis=1, keepdims=True)
    if not first:
        old = m_ref[:, 0:1]
        peak = jnp.maximum(old, peak)
    w = jnp.exp(s - peak)
    hi = w.astype(jnp.bfloat16)
    if not width:
        lo = (w - hi.astype(jnp.float32)).astype(jnp.bfloat16)
    acc = jnp.dot(hi, k_ref[...], preferred_element_type=jnp.float32)
    if width:
        st = row_sums(w, pos_ref, width)
    else:
        lanes = (((1,), (1,)), ((), ()))
        st = lax.dot_general(
            hi, pos_ref[...], lanes, preferred_element_type=jnp.float32
        ) + lax.dot_general(lo, pos_ref[...], lanes, preferred_element_type=jnp.float32)
    if not first:
        alpha = jnp.exp(old - peak)
        acc = acc_ref[...] * alpha + acc
        st = st_ref[...] * alpha + st
    if last:
        warped_ref, flow_ref = outs
        total = st[:, 0:1]
        warped_ref[...] = acc / total
        fx = (st[:, 1:2] + st[:, 2:3]) / total
        fy = (st[:, 3:4] + st[:, 4:5]) / total
        lane = lax.broadcasted_iota(jnp.int32, flow_ref.shape, 1)
        flow_ref[...] = jnp.where(lane == 0, fx, jnp.where(lane == 1, fy, 0.0))
    else:
        m_out, acc_out, st_out = outs
        m_out[...] = jnp.broadcast_to(peak, m_out.shape)
        acc_out[...] = acc
        st_out[...] = st


def split_bf16(x):
    hi = x.astype(jnp.bfloat16)
    return hi, (x - hi.astype(jnp.float32)).astype(jnp.bfloat16)


def positions(count, offset, width):
    index = offset + jnp.arange(count, dtype=jnp.int32)
    col_hi, col_lo = split_bf16((index % width).astype(jnp.float32) / width)
    row_hi, row_lo = split_bf16((index // width).astype(jnp.float32) / width)
    zero = jnp.zeros((count,), jnp.bfloat16)
    one = jnp.ones((count,), jnp.bfloat16)
    return jnp.stack([one, col_hi, col_lo, row_hi, row_lo, zero, zero, zero])


def match_step(queries, keys, pos, state, tq, first, last, width):
    padded, chans = queries.shape
    nq = padded // tq
    tk = keys.shape[0]
    kernel = functools.partial(
        shard_kernel, scale=1.0 / math.sqrt(chans), chans=chans, first=first, last=last,
        width=width,
    )
    row_spec = lambda width: pl.BlockSpec((tq, width), lambda i: (i, 0))
    in_specs = [
        row_spec(chans),
        pl.BlockSpec((tk, chans), lambda i: (0, 0)),
        pl.BlockSpec(pos.shape, lambda i: (0, 0)),
    ]
    args = [queries, keys, pos]
    if not first:
        in_specs += [row_spec(128), row_spec(chans), row_spec(8)]
        args += list(state)
    if last:
        out_specs = [row_spec(chans), row_spec(128)]
        out_shape = [
            jax.ShapeDtypeStruct((padded, chans), jnp.float32),
            jax.ShapeDtypeStruct((padded, 128), jnp.float32),
        ]
    else:
        out_specs = [row_spec(128), row_spec(chans), row_spec(8)]
        out_shape = [
            jax.ShapeDtypeStruct((padded, 128), jnp.float32),
            jax.ShapeDtypeStruct((padded, chans), jnp.float32),
            jax.ShapeDtypeStruct((padded, 8), jnp.float32),
        ]
    return pl.pallas_call(
        kernel,
        grid=(nq,),
        in_specs=in_specs,
        out_specs=out_specs,
        out_shape=out_shape,
        compiler_params=pltpu.CompilerParams(dimension_semantics=("arbitrary",)),
    )(*args)


def match(queries, targets, width):
    count, chans = queries.shape
    tk = targets.shape[0]
    cap = max(8, (1024 * 2048 // tk) // 8 * 8)
    nq = -(-count // cap)
    tq = -(-(-(-count // nq)) // 8) * 8
    padded = tq * nq
    if padded != count:
        queries = jnp.pad(queries, ((0, padded - count), (0, 0)))
    n = lax.axis_size("match")
    me = lax.axis_index("match")
    shards = [(targets, me)]
    for shift in range(1, n):
        moved = lax.ppermute(targets, "match", [(j, (j + shift) % n) for j in range(n)])
        shards.append((moved, (me - shift) % n))
    state = None
    for step, (keys, owner) in enumerate(shards):
        if tk % width == 0:
            base = (owner * (tk // width)).astype(jnp.float32)
            pos = jnp.full((8, 128), base, jnp.float32)
            seg = width
        else:
            pos = positions(tk, owner * tk, width)
            seg = 0
        state = match_step(queries, keys, pos, state, tq, step == 0, step == n - 1, seg)
    warped, flow = state
    return warped[:count], flow[:count, 0], flow[:count, 1]


def local(source, targets, conv_in, flow_proj, in_bias, conv_out):
    rows, cols, chans = source.shape
    all_rows = rows * lax.axis_size("space")
    width = cols * lax.axis_size("match")
    row_first = lax.axis_index("space") * rows
    col_first = lax.axis_index("match") * cols
    ext = extended(source, (("match", 1),), HALO)
    targets, ext = lax.optimization_barrier((targets, ext))
    ext = extended(ext, (("space", 0),), HALO)
    erows, ecols = rows + 2 * HALO, cols + 2 * HALO
    warped, sum_x, sum_y = match(ext.reshape(erows * ecols, chans), targets, width)
    warped = warped.reshape(erows, ecols, chans)
    grow = row_first - HALO + jnp.arange(erows, dtype=jnp.int32)
    gcol = col_first - HALO + jnp.arange(ecols, dtype=jnp.int32)
    inside = ((grow >= 0) & (grow < all_rows))[:, None] & ((gcol >= 0) & (gcol < width))[None, :]
    warped = jnp.where(inside[:, :, None], warped, 0.0)
    col_pos = gcol.astype(jnp.float32) / width
    row_pos = grow.astype(jnp.float32) / width
    flow_x = sum_x.reshape(erows, ecols) - col_pos[None, :]
    flow_y = sum_y.reshape(erows, ecols) - row_pos[:, None]

    pre = lax.conv_general_dilated(
        warped[None], conv_in.astype(jnp.float32), (1, 1), "VALID",
        dimension_numbers=("NHWC", "HWIO", "NHWC"),
        precision=lax.Precision.HIGHEST,
        preferred_element_type=jnp.float32,
    )[0]
    fx1 = flow_x[1:-1, 1:-1]
    fy1 = flow_y[1:-1, 1:-1]
    pre = pre + fx1[:, :, None] * flow_proj[0] + fy1[:, :, None] * flow_proj[1] + in_bias
    hidden = jax.nn.silu(pre).astype(jnp.bfloat16)
    hidden = jnp.where(inside[1:-1, 1:-1, None], hidden, jnp.zeros((), jnp.bfloat16))
    delta = lax.conv_general_dilated(
        hidden[None], jnp.transpose(conv_out, (1, 2, 3, 0)), (1, 1), "VALID",
        dimension_numbers=("NHWC", "HWIO", "NHWC"),
        preferred_element_type=jnp.float32,
    )[0]
    flows = jnp.stack([flow_x[HALO:-HALO, HALO:-HALO], flow_y[HALO:-HALO, HALO:-HALO]])
    return flows + jnp.transpose(delta, (2, 0, 1))


def solution(mesh):
    in_specs = (P("space", "match", None), P("match", None), P(), P(), P(), P())
    out_specs = P(None, "space", "match")
    return jax.shard_map(local, mesh=mesh, in_specs=in_specs, out_specs=out_specs, check_vma=False)
```

```python
import functools
import math

import jax
import jax.numpy as jnp
from jax import lax
from jax.experimental import pallas as pl
from jax.experimental.pallas import tpu as pltpu
from jax.sharding import PartitionSpec as P

HALO = 2


def extended(block, sides, width):
    for axis, dim in sides:
        count = lax.axis_size(axis)
        forward = [(i, i + 1) for i in range(count - 1)]
        backward = [(target, source) for source, target in forward]
        low = lax.ppermute(
            lax.slice_in_dim(block, block.shape[dim] - width, None, axis=dim), axis, forward
        )
        high = lax.ppermute(lax.slice_in_dim(block, 0, width, axis=dim), axis, backward)
        block = jnp.concatenate([low, block, high], axis=dim)
    return block


def row_sums(w, base_ref, width, slot):
    area = w[:, 0:width]
    weighted = None
    for g in range(1, w.shape[1] // width):
        part = w[:, g * width:(g + 1) * width]
        area = area + part
        weighted = part * float(g) if weighted is None else weighted + part * float(g)
    lane = lax.broadcasted_iota(jnp.int32, (1, width), 1)
    col = lane.astype(jnp.float32) / width
    total = jnp.sum(area, axis=1, keepdims=True)
    sum_x = jnp.sum(area * col, axis=1, keepdims=True)
    local = jnp.zeros_like(total) if weighted is None else jnp.sum(weighted, axis=1, keepdims=True)
    sum_y = (base_ref[0:1, slot:slot + 1] * total + local) / width
    lane8 = lax.broadcasted_iota(jnp.int32, (w.shape[0], 8), 1)
    zero = jnp.zeros((), jnp.float32)
    return jnp.where(lane8 == 0, total, jnp.where(lane8 == 1, sum_x, jnp.where(lane8 == 3, sum_y, zero)))


def shard_kernel(*refs, scale, chans, first, last, width, slot):
    if first:
        q_ref, k_ref, pos_ref = refs[:3]
        outs = refs[3:]
    else:
        q_ref, k_ref, pos_ref, m_ref, acc_ref, st_ref = refs[:6]
        outs = refs[6:]
    s = lax.dot_general(
        q_ref[...], k_ref[...], (((1,), (1,)), ((), ())),
        preferred_element_type=jnp.float32,
    ) * scale
    peak = jnp.max(s, axis=1, keepdims=True)
    if not first:
        old = m_ref[:, 0:1]
        peak = jnp.maximum(old, peak)
    w = jnp.exp(s - peak)
    hi = w.astype(jnp.bfloat16)
    if not width:
        lo = (w - hi.astype(jnp.float32)).astype(jnp.bfloat16)
    acc = jnp.dot(hi, k_ref[...], preferred_element_type=jnp.float32)
    if width:
        st = row_sums(w, pos_ref, width, slot)
    else:
        lanes = (((1,), (1,)), ((), ()))
        st = lax.dot_general(
            hi, pos_ref[...], lanes, preferred_element_type=jnp.float32
        ) + lax.dot_general(lo, pos_ref[...], lanes, preferred_element_type=jnp.float32)
    if not first:
        alpha = jnp.exp(old - peak)
        acc = acc_ref[...] * alpha + acc
        st = st_ref[...] * alpha + st
    if last:
        warped_ref, flow_ref = outs
        total = st[:, 0:1]
        warped_ref[...] = acc / total
        fx = (st[:, 1:2] + st[:, 2:3]) / total
        fy = (st[:, 3:4] + st[:, 4:5]) / total
        lane = lax.broadcasted_iota(jnp.int32, flow_ref.shape, 1)
        flow_ref[...] = jnp.where(lane == 0, fx, jnp.where(lane == 1, fy, 0.0))
    else:
        m_out, acc_out, st_out = outs
        m_out[...] = jnp.broadcast_to(peak, m_out.shape)
        acc_out[...] = acc
        st_out[...] = st


def split_bf16(x):
    hi = x.astype(jnp.bfloat16)
    return hi, (x - hi.astype(jnp.float32)).astype(jnp.bfloat16)


def positions(count, offset, width):
    index = offset + jnp.arange(count, dtype=jnp.int32)
    col_hi, col_lo = split_bf16((index % width).astype(jnp.float32) / width)
    row_hi, row_lo = split_bf16((index // width).astype(jnp.float32) / width)
    zero = jnp.zeros((count,), jnp.bfloat16)
    one = jnp.ones((count,), jnp.bfloat16)
    return jnp.stack([one, col_hi, col_lo, row_hi, row_lo, zero, zero, zero])


def match_step(queries, keys, pos, state, tq, first, last, width, slot):
    padded, chans = queries.shape
    nq = padded // tq
    tk = keys.shape[0]
    kernel = functools.partial(
        shard_kernel, scale=1.0 / math.sqrt(chans), chans=chans, first=first, last=last,
        width=width, slot=slot,
    )
    row_spec = lambda width: pl.BlockSpec((tq, width), lambda i: (i, 0))
    in_specs = [
        row_spec(chans),
        pl.BlockSpec((tk, chans), lambda i: (0, 0)),
        pl.BlockSpec(pos.shape, lambda i: (0, 0)),
    ]
    args = [queries, keys, pos]
    if not first:
        in_specs += [row_spec(128), row_spec(chans), row_spec(8)]
        args += list(state)
    if last:
        out_specs = [row_spec(chans), row_spec(128)]
        out_shape = [
            jax.ShapeDtypeStruct((padded, chans), jnp.float32),
            jax.ShapeDtypeStruct((padded, 128), jnp.float32),
        ]
    else:
        out_specs = [row_spec(128), row_spec(chans), row_spec(8)]
        out_shape = [
            jax.ShapeDtypeStruct((padded, 128), jnp.float32),
            jax.ShapeDtypeStruct((padded, chans), jnp.float32),
            jax.ShapeDtypeStruct((padded, 8), jnp.float32),
        ]
    return pl.pallas_call(
        kernel,
        grid=(nq,),
        in_specs=in_specs,
        out_specs=out_specs,
        out_shape=out_shape,
        compiler_params=pltpu.CompilerParams(dimension_semantics=("arbitrary",)),
    )(*args)


def match(queries, targets, width):
    count, chans = queries.shape
    tk = targets.shape[0]
    cap = max(8, (1024 * 2048 // tk) // 8 * 8)
    nq = -(-count // cap)
    tq = -(-(-(-count // nq)) // 8) * 8
    padded = tq * nq
    if padded != count:
        queries = jnp.pad(queries, ((0, padded - count), (0, 0)))
    n = lax.axis_size("match")
    me = lax.axis_index("match")
    shards = [(targets, me)]
    for shift in range(1, n):
        moved = lax.ppermute(targets, "match", [(j, (j + shift) % n) for j in range(n)])
        shards.append((moved, (me - shift) % n))
    state = None
    if tk % width == 0:
        lane = jnp.arange(128, dtype=jnp.int32)
        bases = ((me - lane) % n) * (tk // width)
        table = jnp.broadcast_to(bases.astype(jnp.float32)[None, :], (8, 128))
    for step, (keys, owner) in enumerate(shards):
        if tk % width == 0:
            pos = table
            seg = width
        else:
            pos = positions(tk, owner * tk, width)
            seg = 0
        state = match_step(
            queries, keys, pos, state, tq, step == 0, step == n - 1, seg, step % 128
        )
    warped, flow = state
    return warped[:count], flow[:count, 0], flow[:count, 1]


def local(source, targets, conv_in, flow_proj, in_bias, conv_out):
    rows, cols, chans = source.shape
    all_rows = rows * lax.axis_size("space")
    width = cols * lax.axis_size("match")
    row_first = lax.axis_index("space") * rows
    col_first = lax.axis_index("match") * cols
    ext = extended(source, (("match", 1),), HALO)
    targets, ext = lax.optimization_barrier((targets, ext))
    ext = extended(ext, (("space", 0),), HALO)
    erows, ecols = rows + 2 * HALO, cols + 2 * HALO
    warped, sum_x, sum_y = match(ext.reshape(erows * ecols, chans), targets, width)
    warped = warped.reshape(erows, ecols, chans)
    grow = row_first - HALO + jnp.arange(erows, dtype=jnp.int32)
    gcol = col_first - HALO + jnp.arange(ecols, dtype=jnp.int32)
    inside = ((grow >= 0) & (grow < all_rows))[:, None] & ((gcol >= 0) & (gcol < width))[None, :]
    warped = jnp.where(inside[:, :, None], warped, 0.0)
    col_pos = gcol.astype(jnp.float32) / width
    row_pos = grow.astype(jnp.float32) / width
    flow_x = sum_x.reshape(erows, ecols) - col_pos[None, :]
    flow_y = sum_y.reshape(erows, ecols) - row_pos[:, None]

    pre = lax.conv_general_dilated(
        warped[None], conv_in.astype(jnp.float32), (1, 1), "VALID",
        dimension_numbers=("NHWC", "HWIO", "NHWC"),
        precision=lax.Precision.HIGHEST,
        preferred_element_type=jnp.float32,
    )[0]
    fx1 = flow_x[1:-1, 1:-1]
    fy1 = flow_y[1:-1, 1:-1]
    pre = pre + fx1[:, :, None] * flow_proj[0] + fy1[:, :, None] * flow_proj[1] + in_bias
    hidden = jax.nn.silu(pre).astype(jnp.bfloat16)
    hidden = jnp.where(inside[1:-1, 1:-1, None], hidden, jnp.zeros((), jnp.bfloat16))
    delta = lax.conv_general_dilated(
        hidden[None], jnp.transpose(conv_out, (1, 2, 3, 0)), (1, 1), "VALID",
        dimension_numbers=("NHWC", "HWIO", "NHWC"),
        preferred_element_type=jnp.float32,
    )[0]
    flows = jnp.stack([flow_x[HALO:-HALO, HALO:-HALO], flow_y[HALO:-HALO, HALO:-HALO]])
    return flows + jnp.transpose(delta, (2, 0, 1))


def solution(mesh):
    in_specs = (P("space", "match", None), P("match", None), P(), P(), P(), P())
    out_specs = P(None, "space", "match")
    return jax.shard_map(local, mesh=mesh, in_specs=in_specs, out_specs=out_specs, check_vma=False)
```

```python
import functools
import math

import jax
import jax.numpy as jnp
from jax import lax
from jax.experimental import pallas as pl
from jax.experimental.pallas import tpu as pltpu
from jax.sharding import PartitionSpec as P

HALO = 2


def extended(block, sides, width):
    for axis, dim in sides:
        count = lax.axis_size(axis)
        forward = [(i, i + 1) for i in range(count - 1)]
        backward = [(target, source) for source, target in forward]
        low = lax.ppermute(
            lax.slice_in_dim(block, block.shape[dim] - width, None, axis=dim), axis, forward
        )
        high = lax.ppermute(lax.slice_in_dim(block, 0, width, axis=dim), axis, backward)
        block = jnp.concatenate([low, block, high], axis=dim)
    return block


def row_sums(w, base_ref, width, slot):
    area = w[:, 0:width]
    weighted = None
    for g in range(1, w.shape[1] // width):
        part = w[:, g * width:(g + 1) * width]
        area = area + part
        weighted = part * float(g) if weighted is None else weighted + part * float(g)
    lane = lax.broadcasted_iota(jnp.int32, (1, width), 1)
    col = lane.astype(jnp.float32) / width
    total = jnp.sum(area, axis=1, keepdims=True)
    sum_x = jnp.sum(area * col, axis=1, keepdims=True)
    local = jnp.zeros_like(total) if weighted is None else jnp.sum(weighted, axis=1, keepdims=True)
    sum_y = (base_ref[0:1, slot:slot + 1] * total + local) / width
    lane8 = lax.broadcasted_iota(jnp.int32, (w.shape[0], 8), 1)
    zero = jnp.zeros((), jnp.float32)
    return jnp.where(lane8 == 0, total, jnp.where(lane8 == 1, sum_x, jnp.where(lane8 == 3, sum_y, zero)))


def shard_kernel(*refs, scale, chans, first, last, width, slot):
    if first:
        q_ref, k_ref, pos_ref = refs[:3]
        outs = refs[3:]
    else:
        q_ref, k_ref, pos_ref, m_ref, acc_ref, st_ref = refs[:6]
        outs = refs[6:]
    s = lax.dot_general(
        q_ref[...], k_ref[...], (((1,), (1,)), ((), ())),
        preferred_element_type=jnp.float32,
    ) * scale
    peak = jnp.max(s, axis=1, keepdims=True)
    if not first:
        old = m_ref[:, 0:1]
        peak = jnp.maximum(old, peak)
    w = jnp.exp(s - peak)
    hi = w.astype(jnp.bfloat16)
    if not width:
        lo = (w - hi.astype(jnp.float32)).astype(jnp.bfloat16)
    acc = jnp.dot(hi, k_ref[...], preferred_element_type=jnp.float32)
    if width:
        st = row_sums(w, pos_ref, width, slot)
    else:
        lanes = (((1,), (1,)), ((), ()))
        st = lax.dot_general(
            hi, pos_ref[...], lanes, preferred_element_type=jnp.float32
        ) + lax.dot_general(lo, pos_ref[...], lanes, preferred_element_type=jnp.float32)
    if not first:
        alpha = jnp.exp(old - peak)
        acc = acc_ref[...] * alpha + acc
        st = st_ref[...] * alpha + st
    if last:
        warped_ref, flow_ref = outs
        total = st[:, 0:1]
        warped_ref[...] = acc / total
        fx = (st[:, 1:2] + st[:, 2:3]) / total
        fy = (st[:, 3:4] + st[:, 4:5]) / total
        lane = lax.broadcasted_iota(jnp.int32, flow_ref.shape, 1)
        flow_ref[...] = jnp.where(lane == 0, fx, jnp.where(lane == 1, fy, 0.0))
    else:
        m_out, acc_out, st_out = outs
        m_out[...] = jnp.broadcast_to(peak, m_out.shape)
        acc_out[...] = acc
        st_out[...] = st


def split_bf16(x):
    hi = x.astype(jnp.bfloat16)
    return hi, (x - hi.astype(jnp.float32)).astype(jnp.bfloat16)


def positions(count, offset, width):
    index = offset + jnp.arange(count, dtype=jnp.int32)
    col_hi, col_lo = split_bf16((index % width).astype(jnp.float32) / width)
    row_hi, row_lo = split_bf16((index // width).astype(jnp.float32) / width)
    zero = jnp.zeros((count,), jnp.bfloat16)
    one = jnp.ones((count,), jnp.bfloat16)
    return jnp.stack([one, col_hi, col_lo, row_hi, row_lo, zero, zero, zero])


def match_step(queries, keys, pos, state, tq, first, last, width, slot):
    padded, chans = queries.shape
    nq = padded // tq
    tk = keys.shape[0]
    kernel = functools.partial(
        shard_kernel, scale=1.0 / math.sqrt(chans), chans=chans, first=first, last=last,
        width=width, slot=slot,
    )
    row_spec = lambda width: pl.BlockSpec((tq, width), lambda i: (i, 0))
    in_specs = [
        row_spec(chans),
        pl.BlockSpec((tk, chans), lambda i: (0, 0)),
        pl.BlockSpec(pos.shape, lambda i: (0, 0)),
    ]
    args = [queries, keys, pos]
    if not first:
        in_specs += [row_spec(128), row_spec(chans), row_spec(8)]
        args += list(state)
    if last:
        out_specs = [row_spec(chans), row_spec(128)]
        out_shape = [
            jax.ShapeDtypeStruct((padded, chans), jnp.float32),
            jax.ShapeDtypeStruct((padded, 128), jnp.float32),
        ]
    else:
        out_specs = [row_spec(128), row_spec(chans), row_spec(8)]
        out_shape = [
            jax.ShapeDtypeStruct((padded, 128), jnp.float32),
            jax.ShapeDtypeStruct((padded, chans), jnp.float32),
            jax.ShapeDtypeStruct((padded, 8), jnp.float32),
        ]
    return pl.pallas_call(
        kernel,
        grid=(nq,),
        in_specs=in_specs,
        out_specs=out_specs,
        out_shape=out_shape,
        compiler_params=pltpu.CompilerParams(dimension_semantics=("arbitrary",)),
    )(*args)


def match(queries, targets, width):
    count, chans = queries.shape
    tk = targets.shape[0]
    cap = max(8, (1024 * 2048 // tk) // 8 * 8)
    nq = -(-count // cap)
    tq = -(-(-(-count // nq)) // 8) * 8
    padded = tq * nq
    if padded != count:
        queries = jnp.pad(queries, ((0, padded - count), (0, 0)))
    n = lax.axis_size("match")
    me = lax.axis_index("match")
    shards = [(targets, me)]
    if n % 2 == 0:
        chips = n // 2
        sibling = [(j, j ^ 1) for j in range(n)]
        shards.append((lax.ppermute(targets, "match", sibling), me ^ 1))
        for shift in range(1, chips):
            hop = [(j, ((j // 2 + shift) % chips) * 2 + j % 2) for j in range(n)]
            moved = lax.ppermute(targets, "match", hop)
            owner = ((me // 2 - shift) % chips) * 2 + me % 2
            shards.append((moved, owner))
            shards.append((lax.ppermute(moved, "match", sibling), owner ^ 1))
    else:
        for shift in range(1, n):
            moved = lax.ppermute(targets, "match", [(j, (j + shift) % n) for j in range(n)])
            shards.append((moved, (me - shift) % n))
    state = None
    if tk % width == 0:
        owners = jnp.stack([owner for _, owner in shards]) * (tk // width)
        owners = jnp.pad(owners.astype(jnp.float32), (0, 128 - n))
        table = jnp.broadcast_to(owners[None, :], (8, 128))
    for step, (keys, owner) in enumerate(shards):
        if tk % width == 0:
            pos = table
            seg = width
        else:
            pos = positions(tk, owner * tk, width)
            seg = 0
        state = match_step(
            queries, keys, pos, state, tq, step == 0, step == n - 1, seg, step % 128
        )
    warped, flow = state
    return warped[:count], flow[:count, 0], flow[:count, 1]


def local(source, targets, conv_in, flow_proj, in_bias, conv_out):
    rows, cols, chans = source.shape
    all_rows = rows * lax.axis_size("space")
    width = cols * lax.axis_size("match")
    row_first = lax.axis_index("space") * rows
    col_first = lax.axis_index("match") * cols
    ext = extended(source, (("match", 1),), HALO)
    targets, ext = lax.optimization_barrier((targets, ext))
    ext = extended(ext, (("space", 0),), HALO)
    erows, ecols = rows + 2 * HALO, cols + 2 * HALO
    warped, sum_x, sum_y = match(ext.reshape(erows * ecols, chans), targets, width)
    warped = warped.reshape(erows, ecols, chans)
    grow = row_first - HALO + jnp.arange(erows, dtype=jnp.int32)
    gcol = col_first - HALO + jnp.arange(ecols, dtype=jnp.int32)
    inside = ((grow >= 0) & (grow < all_rows))[:, None] & ((gcol >= 0) & (gcol < width))[None, :]
    warped = jnp.where(inside[:, :, None], warped, 0.0)
    col_pos = gcol.astype(jnp.float32) / width
    row_pos = grow.astype(jnp.float32) / width
    flow_x = sum_x.reshape(erows, ecols) - col_pos[None, :]
    flow_y = sum_y.reshape(erows, ecols) - row_pos[:, None]

    pre = lax.conv_general_dilated(
        warped[None], conv_in.astype(jnp.float32), (1, 1), "VALID",
        dimension_numbers=("NHWC", "HWIO", "NHWC"),
        precision=lax.Precision.HIGHEST,
        preferred_element_type=jnp.float32,
    )[0]
    fx1 = flow_x[1:-1, 1:-1]
    fy1 = flow_y[1:-1, 1:-1]
    pre = pre + fx1[:, :, None] * flow_proj[0] + fy1[:, :, None] * flow_proj[1] + in_bias
    hidden = jax.nn.silu(pre).astype(jnp.bfloat16)
    hidden = jnp.where(inside[1:-1, 1:-1, None], hidden, jnp.zeros((), jnp.bfloat16))
    delta = lax.conv_general_dilated(
        hidden[None], jnp.transpose(conv_out, (1, 2, 3, 0)), (1, 1), "VALID",
        dimension_numbers=("NHWC", "HWIO", "NHWC"),
        preferred_element_type=jnp.float32,
    )[0]
    flows = jnp.stack([flow_x[HALO:-HALO, HALO:-HALO], flow_y[HALO:-HALO, HALO:-HALO]])
    return flows + jnp.transpose(delta, (2, 0, 1))


def solution(mesh):
    in_specs = (P("space", "match", None), P("match", None), P(), P(), P(), P())
    out_specs = P(None, "space", "match")
    return jax.shard_map(local, mesh=mesh, in_specs=in_specs, out_specs=out_specs, check_vma=False)
```

```python
import functools
import math

import jax
import jax.numpy as jnp
from jax import lax
from jax.experimental import pallas as pl
from jax.experimental.pallas import tpu as pltpu
from jax.sharding import PartitionSpec as P

HALO = 2


def extended(block, sides, width):
    for axis, dim in sides:
        count = lax.axis_size(axis)
        forward = [(i, i + 1) for i in range(count - 1)]
        backward = [(target, source) for source, target in forward]
        low = lax.ppermute(
            lax.slice_in_dim(block, block.shape[dim] - width, None, axis=dim), axis, forward
        )
        high = lax.ppermute(lax.slice_in_dim(block, 0, width, axis=dim), axis, backward)
        block = jnp.concatenate([low, block, high], axis=dim)
    return block


def row_sums(w, base_ref, width, slot):
    area = w[:, 0:width]
    weighted = None
    for g in range(1, w.shape[1] // width):
        part = w[:, g * width:(g + 1) * width]
        area = area + part
        weighted = part * float(g) if weighted is None else weighted + part * float(g)
    lane = lax.broadcasted_iota(jnp.int32, (1, width), 1)
    col = lane.astype(jnp.float32) / width
    total = jnp.sum(area, axis=1, keepdims=True)
    sum_x = jnp.sum(area * col, axis=1, keepdims=True)
    local = jnp.zeros_like(total) if weighted is None else jnp.sum(weighted, axis=1, keepdims=True)
    sum_y = (base_ref[0:1, slot:slot + 1] * total + local) / width
    lane8 = lax.broadcasted_iota(jnp.int32, (w.shape[0], 8), 1)
    zero = jnp.zeros((), jnp.float32)
    return jnp.where(lane8 == 0, total, jnp.where(lane8 == 1, sum_x, jnp.where(lane8 == 3, sum_y, zero)))


def shard_kernel(*refs, scale, chans, first, last, width, slot):
    if first:
        q_ref, k_ref, pos_ref = refs[:3]
        outs = refs[3:]
    else:
        q_ref, k_ref, pos_ref, m_ref, acc_ref, st_ref = refs[:6]
        outs = refs[6:]
    s = lax.dot_general(
        q_ref[...], k_ref[...], (((1,), (1,)), ((), ())),
        preferred_element_type=jnp.float32,
    ) * scale
    peak = jnp.max(s, axis=1, keepdims=True)
    if not first:
        old = m_ref[:, 0:1]
        peak = jnp.maximum(old, peak)
    w = jnp.exp(s - peak)
    hi = w.astype(jnp.bfloat16)
    if not width:
        lo = (w - hi.astype(jnp.float32)).astype(jnp.bfloat16)
    acc = jnp.dot(hi, k_ref[...], preferred_element_type=jnp.float32)
    if width:
        st = row_sums(w, pos_ref, width, slot)
    else:
        lanes = (((1,), (1,)), ((), ()))
        st = lax.dot_general(
            hi, pos_ref[...], lanes, preferred_element_type=jnp.float32
        ) + lax.dot_general(lo, pos_ref[...], lanes, preferred_element_type=jnp.float32)
    if not first:
        alpha = jnp.exp(old - peak)
        acc = acc_ref[...] * alpha + acc
        st = st_ref[...] * alpha + st
    if last:
        warped_ref, flow_ref = outs
        total = st[:, 0:1]
        warped_ref[...] = acc / total
        fx = (st[:, 1:2] + st[:, 2:3]) / total
        fy = (st[:, 3:4] + st[:, 4:5]) / total
        lane = lax.broadcasted_iota(jnp.int32, flow_ref.shape, 1)
        flow_ref[...] = jnp.where(lane == 0, fx, jnp.where(lane == 1, fy, 0.0))
    else:
        m_out, acc_out, st_out = outs
        m_out[...] = jnp.broadcast_to(peak, m_out.shape)
        acc_out[...] = acc
        st_out[...] = st


def split_bf16(x):
    hi = x.astype(jnp.bfloat16)
    return hi, (x - hi.astype(jnp.float32)).astype(jnp.bfloat16)


def positions(count, offset, width):
    index = offset + jnp.arange(count, dtype=jnp.int32)
    col_hi, col_lo = split_bf16((index % width).astype(jnp.float32) / width)
    row_hi, row_lo = split_bf16((index // width).astype(jnp.float32) / width)
    zero = jnp.zeros((count,), jnp.bfloat16)
    one = jnp.ones((count,), jnp.bfloat16)
    return jnp.stack([one, col_hi, col_lo, row_hi, row_lo, zero, zero, zero])


def match_step(queries, keys, pos, state, tq, first, last, width, slot):
    padded, chans = queries.shape
    nq = padded // tq
    tk = keys.shape[0]
    kernel = functools.partial(
        shard_kernel, scale=1.0 / math.sqrt(chans), chans=chans, first=first, last=last,
        width=width, slot=slot,
    )
    row_spec = lambda width: pl.BlockSpec((tq, width), lambda i: (i, 0))
    in_specs = [
        row_spec(chans),
        pl.BlockSpec((tk, chans), lambda i: (0, 0)),
        pl.BlockSpec(pos.shape, lambda i: (0, 0)),
    ]
    args = [queries, keys, pos]
    if not first:
        in_specs += [row_spec(128), row_spec(chans), row_spec(8)]
        args += list(state)
    if last:
        out_specs = [row_spec(chans), row_spec(128)]
        out_shape = [
            jax.ShapeDtypeStruct((padded, chans), jnp.float32),
            jax.ShapeDtypeStruct((padded, 128), jnp.float32),
        ]
    else:
        out_specs = [row_spec(128), row_spec(chans), row_spec(8)]
        out_shape = [
            jax.ShapeDtypeStruct((padded, 128), jnp.float32),
            jax.ShapeDtypeStruct((padded, chans), jnp.float32),
            jax.ShapeDtypeStruct((padded, 8), jnp.float32),
        ]
    return pl.pallas_call(
        kernel,
        grid=(nq,),
        in_specs=in_specs,
        out_specs=out_specs,
        out_shape=out_shape,
        compiler_params=pltpu.CompilerParams(dimension_semantics=("arbitrary",)),
    )(*args)


def match(queries, targets, width):
    count, chans = queries.shape
    tk = targets.shape[0]
    cap = max(8, (1024 * 2048 // tk) // 8 * 8)
    nq = -(-count // cap)
    tq = -(-(-(-count // nq)) // 8) * 8
    padded = tq * nq
    if padded != count:
        queries = jnp.pad(queries, ((0, padded - count), (0, 0)))
    n = lax.axis_size("match")
    me = lax.axis_index("match")
    shards = [(targets, me, None)]
    if n % 2 == 0:
        chips = n // 2
        sibling = [(j, j ^ 1) for j in range(n)]
        shards.append((lax.ppermute(targets, "match", sibling), me ^ 1, None))
        for shift in range(1, chips):
            hop = [(j, ((j // 2 + shift) % chips) * 2 + j % 2) for j in range(n)]
            moved = lax.ppermute(targets, "match", hop)
            owner = ((me // 2 - shift) % chips) * 2 + me % 2
            shards.append((moved, owner, sibling))
            shards.append((None, owner ^ 1, None))
    else:
        for shift in range(1, n):
            moved = lax.ppermute(targets, "match", [(j, (j + shift) % n) for j in range(n)])
            shards.append((moved, (me - shift) % n, None))
    state = None
    if tk % width == 0:
        owners = jnp.stack([owner for _, owner, _ in shards]) * (tk // width)
        owners = jnp.pad(owners.astype(jnp.float32), (0, 128 - n))
        table = jnp.broadcast_to(owners[None, :], (8, 128))
    pending = None
    for step, (keys, owner, forward) in enumerate(shards):
        if keys is None:
            keys = pending
        if forward:
            keys, state = lax.optimization_barrier((keys, state))
            pending = lax.ppermute(keys, "match", forward)
        if tk % width == 0:
            pos = table
            seg = width
        else:
            pos = positions(tk, owner * tk, width)
            seg = 0
        state = match_step(
            queries, keys, pos, state, tq, step == 0, step == n - 1, seg, step % 128
        )
    warped, flow = state
    return warped[:count], flow[:count, 0], flow[:count, 1]


def local(source, targets, conv_in, flow_proj, in_bias, conv_out):
    rows, cols, chans = source.shape
    all_rows = rows * lax.axis_size("space")
    width = cols * lax.axis_size("match")
    row_first = lax.axis_index("space") * rows
    col_first = lax.axis_index("match") * cols
    ext = extended(source, (("match", 1),), HALO)
    targets, ext = lax.optimization_barrier((targets, ext))
    ext = extended(ext, (("space", 0),), HALO)
    erows, ecols = rows + 2 * HALO, cols + 2 * HALO
    warped, sum_x, sum_y = match(ext.reshape(erows * ecols, chans), targets, width)
    warped = warped.reshape(erows, ecols, chans)
    grow = row_first - HALO + jnp.arange(erows, dtype=jnp.int32)
    gcol = col_first - HALO + jnp.arange(ecols, dtype=jnp.int32)
    inside = ((grow >= 0) & (grow < all_rows))[:, None] & ((gcol >= 0) & (gcol < width))[None, :]
    warped = jnp.where(inside[:, :, None], warped, 0.0)
    col_pos = gcol.astype(jnp.float32) / width
    row_pos = grow.astype(jnp.float32) / width
    flow_x = sum_x.reshape(erows, ecols) - col_pos[None, :]
    flow_y = sum_y.reshape(erows, ecols) - row_pos[:, None]

    pre = lax.conv_general_dilated(
        warped[None], conv_in.astype(jnp.float32), (1, 1), "VALID",
        dimension_numbers=("NHWC", "HWIO", "NHWC"),
        precision=lax.Precision.HIGHEST,
        preferred_element_type=jnp.float32,
    )[0]
    fx1 = flow_x[1:-1, 1:-1]
    fy1 = flow_y[1:-1, 1:-1]
    pre = pre + fx1[:, :, None] * flow_proj[0] + fy1[:, :, None] * flow_proj[1] + in_bias
    hidden = jax.nn.silu(pre).astype(jnp.bfloat16)
    hidden = jnp.where(inside[1:-1, 1:-1, None], hidden, jnp.zeros((), jnp.bfloat16))
    delta = lax.conv_general_dilated(
        hidden[None], jnp.transpose(conv_out, (1, 2, 3, 0)), (1, 1), "VALID",
        dimension_numbers=("NHWC", "HWIO", "NHWC"),
        preferred_element_type=jnp.float32,
    )[0]
    flows = jnp.stack([flow_x[HALO:-HALO, HALO:-HALO], flow_y[HALO:-HALO, HALO:-HALO]])
    return flows + jnp.transpose(delta, (2, 0, 1))


def solution(mesh):
    in_specs = (P("space", "match", None), P("match", None), P(), P(), P(), P())
    out_specs = P(None, "space", "match")
    return jax.shard_map(local, mesh=mesh, in_specs=in_specs, out_specs=out_specs, check_vma=False)
```

```python
import functools
import math

import jax
import jax.numpy as jnp
from jax import lax
from jax.experimental import pallas as pl
from jax.experimental.pallas import tpu as pltpu
from jax.sharding import PartitionSpec as P

HALO = 2


def extended(block, sides, width):
    for axis, dim in sides:
        count = lax.axis_size(axis)
        forward = [(i, i + 1) for i in range(count - 1)]
        backward = [(target, source) for source, target in forward]
        low = lax.ppermute(
            lax.slice_in_dim(block, block.shape[dim] - width, None, axis=dim), axis, forward
        )
        high = lax.ppermute(lax.slice_in_dim(block, 0, width, axis=dim), axis, backward)
        block = jnp.concatenate([low, block, high], axis=dim)
    return block


def row_sums(w, base_ref, width, slot):
    count = w.shape[1] // width
    parts = [w[:, g * width:(g + 1) * width] for g in range(count)]
    weighted = None
    area = parts[-1]
    for g in range(count - 1, 0, -1):
        if g < count - 1:
            area = area + parts[g]
        weighted = area if weighted is None else weighted + area
    if count > 1:
        area = area + parts[0]
    lane = lax.broadcasted_iota(jnp.int32, (1, width), 1)
    col = lane.astype(jnp.float32) / width
    total = jnp.sum(area, axis=1, keepdims=True)
    sum_x = jnp.sum(area * col, axis=1, keepdims=True)
    local = jnp.zeros_like(total) if weighted is None else jnp.sum(weighted, axis=1, keepdims=True)
    sum_y = (base_ref[0:1, slot:slot + 1] * total + local) / width
    lane8 = lax.broadcasted_iota(jnp.int32, (w.shape[0], 8), 1)
    zero = jnp.zeros((), jnp.float32)
    return jnp.where(lane8 == 0, total, jnp.where(lane8 == 1, sum_x, jnp.where(lane8 == 3, sum_y, zero)))


def shard_kernel(*refs, scale, chans, first, last, width, slot):
    if first:
        q_ref, k_ref, pos_ref = refs[:3]
        outs = refs[3:]
    else:
        q_ref, k_ref, pos_ref, m_ref, acc_ref, st_ref = refs[:6]
        outs = refs[6:]
    s = lax.dot_general(
        q_ref[...], k_ref[...], (((1,), (1,)), ((), ())),
        preferred_element_type=jnp.float32,
    )
    peak = jnp.max(s, axis=1, keepdims=True)
    if not first:
        old = m_ref[:, 0:1]
        peak = jnp.maximum(old, peak)
    rate = scale * math.log2(math.e)
    w = jnp.exp2((s - peak) * rate)
    hi = w.astype(jnp.bfloat16)
    if not width:
        lo = (w - hi.astype(jnp.float32)).astype(jnp.bfloat16)
    acc = jnp.dot(hi, k_ref[...], preferred_element_type=jnp.float32)
    if width:
        st = row_sums(w, pos_ref, width, slot)
    else:
        lanes = (((1,), (1,)), ((), ()))
        st = lax.dot_general(
            hi, pos_ref[...], lanes, preferred_element_type=jnp.float32
        ) + lax.dot_general(lo, pos_ref[...], lanes, preferred_element_type=jnp.float32)
    if not first:
        alpha = jnp.exp2((old - peak) * rate)
        acc = acc_ref[...] * alpha + acc
        st = st_ref[...] * alpha + st
    if last:
        warped_ref, flow_ref = outs
        total = st[:, 0:1]
        warped_ref[...] = acc / total
        fx = (st[:, 1:2] + st[:, 2:3]) / total
        fy = (st[:, 3:4] + st[:, 4:5]) / total
        lane = lax.broadcasted_iota(jnp.int32, flow_ref.shape, 1)
        flow_ref[...] = jnp.where(lane == 0, fx, jnp.where(lane == 1, fy, 0.0))
    else:
        m_out, acc_out, st_out = outs
        m_out[...] = jnp.broadcast_to(peak, m_out.shape)
        acc_out[...] = acc
        st_out[...] = st


def split_bf16(x):
    hi = x.astype(jnp.bfloat16)
    return hi, (x - hi.astype(jnp.float32)).astype(jnp.bfloat16)


def positions(count, offset, width):
    index = offset + jnp.arange(count, dtype=jnp.int32)
    col_hi, col_lo = split_bf16((index % width).astype(jnp.float32) / width)
    row_hi, row_lo = split_bf16((index // width).astype(jnp.float32) / width)
    zero = jnp.zeros((count,), jnp.bfloat16)
    one = jnp.ones((count,), jnp.bfloat16)
    return jnp.stack([one, col_hi, col_lo, row_hi, row_lo, zero, zero, zero])


def match_step(queries, keys, pos, state, tq, first, last, width, slot):
    padded, chans = queries.shape
    nq = padded // tq
    tk = keys.shape[0]
    kernel = functools.partial(
        shard_kernel, scale=1.0 / math.sqrt(chans), chans=chans, first=first, last=last,
        width=width, slot=slot,
    )
    row_spec = lambda width: pl.BlockSpec((tq, width), lambda i: (i, 0))
    in_specs = [
        row_spec(chans),
        pl.BlockSpec((tk, chans), lambda i: (0, 0)),
        pl.BlockSpec(pos.shape, lambda i: (0, 0)),
    ]
    args = [queries, keys, pos]
    if not first:
        in_specs += [row_spec(128), row_spec(chans), row_spec(8)]
        args += list(state)
    if last:
        out_specs = [row_spec(chans), row_spec(128)]
        out_shape = [
            jax.ShapeDtypeStruct((padded, chans), jnp.float32),
            jax.ShapeDtypeStruct((padded, 128), jnp.float32),
        ]
    else:
        out_specs = [row_spec(128), row_spec(chans), row_spec(8)]
        out_shape = [
            jax.ShapeDtypeStruct((padded, 128), jnp.float32),
            jax.ShapeDtypeStruct((padded, chans), jnp.float32),
            jax.ShapeDtypeStruct((padded, 8), jnp.float32),
        ]
    return pl.pallas_call(
        kernel,
        grid=(nq,),
        in_specs=in_specs,
        out_specs=out_specs,
        out_shape=out_shape,
        compiler_params=pltpu.CompilerParams(dimension_semantics=("arbitrary",)),
    )(*args)


def match(queries, targets, width):
    count, chans = queries.shape
    tk = targets.shape[0]
    cap = max(8, (1024 * 2048 // tk) // 8 * 8)
    nq = -(-count // cap)
    tq = -(-(-(-count // nq)) // 8) * 8
    padded = tq * nq
    if padded != count:
        queries = jnp.pad(queries, ((0, padded - count), (0, 0)))
    n = lax.axis_size("match")
    me = lax.axis_index("match")
    shards = [(targets, me, None)]
    if n % 2 == 0:
        chips = n // 2
        sibling = [(j, j ^ 1) for j in range(n)]
        shards.append((lax.ppermute(targets, "match", sibling), me ^ 1, None))
        for shift in range(1, chips):
            hop = [(j, ((j // 2 + shift) % chips) * 2 + j % 2) for j in range(n)]
            moved = lax.ppermute(targets, "match", hop)
            owner = ((me // 2 - shift) % chips) * 2 + me % 2
            shards.append((moved, owner, sibling))
            shards.append((None, owner ^ 1, None))
    else:
        for shift in range(1, n):
            moved = lax.ppermute(targets, "match", [(j, (j + shift) % n) for j in range(n)])
            shards.append((moved, (me - shift) % n, None))
    state = None
    if tk % width == 0:
        owners = jnp.stack([owner for _, owner, _ in shards]) * (tk // width)
        owners = jnp.pad(owners.astype(jnp.float32), (0, 128 - n))
        table = jnp.broadcast_to(owners[None, :], (8, 128))
    pending = None
    for step, (keys, owner, forward) in enumerate(shards):
        if keys is None:
            keys = pending
        if forward:
            keys, state = lax.optimization_barrier((keys, state))
            pending = lax.ppermute(keys, "match", forward)
        if tk % width == 0:
            pos = table
            seg = width
        else:
            pos = positions(tk, owner * tk, width)
            seg = 0
        state = match_step(
            queries, keys, pos, state, tq, step == 0, step == n - 1, seg, step % 128
        )
    warped, flow = state
    return warped[:count], flow[:count, 0], flow[:count, 1]


def local(source, targets, conv_in, flow_proj, in_bias, conv_out):
    rows, cols, chans = source.shape
    all_rows = rows * lax.axis_size("space")
    width = cols * lax.axis_size("match")
    row_first = lax.axis_index("space") * rows
    col_first = lax.axis_index("match") * cols
    ext = extended(source, (("match", 1),), HALO)
    targets, ext = lax.optimization_barrier((targets, ext))
    ext = extended(ext, (("space", 0),), HALO)
    erows, ecols = rows + 2 * HALO, cols + 2 * HALO
    warped, sum_x, sum_y = match(ext.reshape(erows * ecols, chans), targets, width)
    warped = warped.reshape(erows, ecols, chans)
    grow = row_first - HALO + jnp.arange(erows, dtype=jnp.int32)
    gcol = col_first - HALO + jnp.arange(ecols, dtype=jnp.int32)
    inside = ((grow >= 0) & (grow < all_rows))[:, None] & ((gcol >= 0) & (gcol < width))[None, :]
    warped = jnp.where(inside[:, :, None], warped, 0.0)
    col_pos = gcol.astype(jnp.float32) / width
    row_pos = grow.astype(jnp.float32) / width
    flow_x = sum_x.reshape(erows, ecols) - col_pos[None, :]
    flow_y = sum_y.reshape(erows, ecols) - row_pos[:, None]

    pre = lax.conv_general_dilated(
        warped[None], conv_in.astype(jnp.float32), (1, 1), "VALID",
        dimension_numbers=("NHWC", "HWIO", "NHWC"),
        precision=lax.Precision.HIGHEST,
        preferred_element_type=jnp.float32,
    )[0]
    fx1 = flow_x[1:-1, 1:-1]
    fy1 = flow_y[1:-1, 1:-1]
    pre = pre + fx1[:, :, None] * flow_proj[0] + fy1[:, :, None] * flow_proj[1] + in_bias
    hidden = jax.nn.silu(pre).astype(jnp.bfloat16)
    hidden = jnp.where(inside[1:-1, 1:-1, None], hidden, jnp.zeros((), jnp.bfloat16))
    delta = lax.conv_general_dilated(
        hidden[None], jnp.transpose(conv_out, (1, 2, 3, 0)), (1, 1), "VALID",
        dimension_numbers=("NHWC", "HWIO", "NHWC"),
        preferred_element_type=jnp.float32,
    )[0]
    flows = jnp.stack([flow_x[HALO:-HALO, HALO:-HALO], flow_y[HALO:-HALO, HALO:-HALO]])
    return flows + jnp.transpose(delta, (2, 0, 1))


def solution(mesh):
    in_specs = (P("space", "match", None), P("match", None), P(), P(), P(), P())
    out_specs = P(None, "space", "match")
    return jax.shard_map(local, mesh=mesh, in_specs=in_specs, out_specs=out_specs, check_vma=False)
```

```python
import functools
import itertools
import math

import jax
import jax.numpy as jnp
from jax import lax
from jax.experimental import pallas as pl
from jax.experimental.pallas import tpu as pltpu
from jax.sharding import PartitionSpec as P

HALO = 2


def extended(block, sides, width):
    for axis, dim in sides:
        count = lax.axis_size(axis)
        forward = [(i, i + 1) for i in range(count - 1)]
        backward = [(target, source) for source, target in forward]
        low = lax.ppermute(
            lax.slice_in_dim(block, block.shape[dim] - width, None, axis=dim), axis, forward
        )
        high = lax.ppermute(lax.slice_in_dim(block, 0, width, axis=dim), axis, backward)
        block = jnp.concatenate([low, block, high], axis=dim)
    return block


def row_sums(w, base_ref, width, slot):
    count = w.shape[1] // width
    parts = [w[:, g * width:(g + 1) * width] for g in range(count)]
    weighted = None
    area = parts[-1]
    for g in range(count - 1, 0, -1):
        if g < count - 1:
            area = area + parts[g]
        weighted = area if weighted is None else weighted + area
    if count > 1:
        area = area + parts[0]
    lane = lax.broadcasted_iota(jnp.int32, (1, width), 1)
    col = lane.astype(jnp.float32) / width
    total = jnp.sum(area, axis=1, keepdims=True)
    sum_x = jnp.sum(area * col, axis=1, keepdims=True)
    local = jnp.zeros_like(total) if weighted is None else jnp.sum(weighted, axis=1, keepdims=True)
    sum_y = (base_ref[0:1, slot:slot + 1] * total + local) / width
    lane8 = lax.broadcasted_iota(jnp.int32, (w.shape[0], 8), 1)
    zero = jnp.zeros((), jnp.float32)
    return jnp.where(lane8 == 0, total, jnp.where(lane8 == 1, sum_x, jnp.where(lane8 == 3, sum_y, zero)))


def halo_ring(block, width):
    rows, cols = block.shape[:2]
    counts = (lax.axis_size("space"), lax.axis_size("match"))
    pieces = {}
    for dr in (-1, 0, 1):
        for dc in (-1, 0, 1):
            if dr == 0 and dc == 0:
                continue
            part = block
            if dr:
                part = lax.slice_in_dim(part, 0 if dr > 0 else rows - width, width if dr > 0 else rows, axis=0)
            if dc:
                part = lax.slice_in_dim(part, 0 if dc > 0 else cols - width, width if dc > 0 else cols, axis=1)
            axes = [(name, step, size) for name, step, size in
                    (("space", dr, counts[0]), ("match", dc, counts[1])) if step]
            names = tuple(name for name, _, _ in axes)
            pairs = []
            grid = [range(size) for _, _, size in axes]
            for place in itertools.product(*grid):
                target = tuple(p - step for p, (_, step, _) in zip(place, axes))
                if all(0 <= t < size for t, (_, _, size) in zip(target, axes)):
                    flat = lambda idx: functools.reduce(
                        lambda acc, pair: acc * pair[1][2] + pair[0], zip(idx, axes), 0)
                    pairs.append((flat(place), flat(target)))
            name = names[0] if len(names) == 1 else names
            pieces[(dr, dc)] = lax.ppermute(part, name, pairs)
    band = lambda dr: jnp.concatenate(
        [pieces[(dr, -1)], pieces[(dr, 0)] if dr else block, pieces[(dr, 1)]], axis=1)
    return jnp.concatenate([band(-1), band(0), band(1)], axis=0)


def shard_kernel(*refs, scale, chans, first, last, width, slot):
    if first:
        q_ref, k_ref, pos_ref = refs[:3]
        outs = refs[3:]
    else:
        q_ref, k_ref, pos_ref, m_ref, acc_ref, st_ref = refs[:6]
        outs = refs[6:]
    s = lax.dot_general(
        q_ref[...], k_ref[...], (((1,), (1,)), ((), ())),
        preferred_element_type=jnp.float32,
    )
    peak = jnp.max(s, axis=1, keepdims=True)
    if not first:
        old = m_ref[:, 0:1]
        peak = jnp.maximum(old, peak)
    rate = scale * math.log2(math.e)
    w = jnp.exp2((s - peak) * rate)
    hi = w.astype(jnp.bfloat16)
    if not width:
        lo = (w - hi.astype(jnp.float32)).astype(jnp.bfloat16)
    acc = jnp.dot(hi, k_ref[...], preferred_element_type=jnp.float32)
    if width:
        st = row_sums(w, pos_ref, width, slot)
    else:
        lanes = (((1,), (1,)), ((), ()))
        st = lax.dot_general(
            hi, pos_ref[...], lanes, preferred_element_type=jnp.float32
        ) + lax.dot_general(lo, pos_ref[...], lanes, preferred_element_type=jnp.float32)
    if not first:
        alpha = jnp.exp2((old - peak) * rate)
        acc = acc_ref[...] * alpha + acc
        st = st_ref[...] * alpha + st
    if last:
        warped_ref, flow_ref = outs
        total = st[:, 0:1]
        warped_ref[...] = acc / total
        fx = (st[:, 1:2] + st[:, 2:3]) / total
        fy = (st[:, 3:4] + st[:, 4:5]) / total
        lane = lax.broadcasted_iota(jnp.int32, flow_ref.shape, 1)
        flow_ref[...] = jnp.where(lane == 0, fx, jnp.where(lane == 1, fy, 0.0))
    else:
        m_out, acc_out, st_out = outs
        m_out[...] = jnp.broadcast_to(peak, m_out.shape)
        acc_out[...] = acc
        st_out[...] = st


def split_bf16(x):
    hi = x.astype(jnp.bfloat16)
    return hi, (x - hi.astype(jnp.float32)).astype(jnp.bfloat16)


def positions(count, offset, width):
    index = offset + jnp.arange(count, dtype=jnp.int32)
    col_hi, col_lo = split_bf16((index % width).astype(jnp.float32) / width)
    row_hi, row_lo = split_bf16((index // width).astype(jnp.float32) / width)
    zero = jnp.zeros((count,), jnp.bfloat16)
    one = jnp.ones((count,), jnp.bfloat16)
    return jnp.stack([one, col_hi, col_lo, row_hi, row_lo, zero, zero, zero])


def match_step(queries, keys, pos, state, tq, first, last, width, slot):
    padded, chans = queries.shape
    nq = padded // tq
    tk = keys.shape[0]
    kernel = functools.partial(
        shard_kernel, scale=1.0 / math.sqrt(chans), chans=chans, first=first, last=last,
        width=width, slot=slot,
    )
    row_spec = lambda width: pl.BlockSpec((tq, width), lambda i: (i, 0))
    in_specs = [
        row_spec(chans),
        pl.BlockSpec((tk, chans), lambda i: (0, 0)),
        pl.BlockSpec(pos.shape, lambda i: (0, 0)),
    ]
    args = [queries, keys, pos]
    if not first:
        in_specs += [row_spec(128), row_spec(chans), row_spec(8)]
        args += list(state)
    if last:
        out_specs = [row_spec(chans), row_spec(128)]
        out_shape = [
            jax.ShapeDtypeStruct((padded, chans), jnp.float32),
            jax.ShapeDtypeStruct((padded, 128), jnp.float32),
        ]
    else:
        out_specs = [row_spec(128), row_spec(chans), row_spec(8)]
        out_shape = [
            jax.ShapeDtypeStruct((padded, 128), jnp.float32),
            jax.ShapeDtypeStruct((padded, chans), jnp.float32),
            jax.ShapeDtypeStruct((padded, 8), jnp.float32),
        ]
    return pl.pallas_call(
        kernel,
        grid=(nq,),
        in_specs=in_specs,
        out_specs=out_specs,
        out_shape=out_shape,
        compiler_params=pltpu.CompilerParams(dimension_semantics=("arbitrary",)),
    )(*args)


def match(queries, targets, width):
    count, chans = queries.shape
    tk = targets.shape[0]
    cap = max(8, (1024 * 2048 // tk) // 8 * 8)
    nq = -(-count // cap)
    tq = -(-(-(-count // nq)) // 8) * 8
    padded = tq * nq
    if padded != count:
        queries = jnp.pad(queries, ((0, padded - count), (0, 0)))
    n = lax.axis_size("match")
    me = lax.axis_index("match")
    shards = [(targets, me, None)]
    if n % 2 == 0:
        chips = n // 2
        sibling = [(j, j ^ 1) for j in range(n)]
        shards.append((lax.ppermute(targets, "match", sibling), me ^ 1, None))
        for shift in range(1, chips):
            hop = [(j, ((j // 2 + shift) % chips) * 2 + j % 2) for j in range(n)]
            moved = lax.ppermute(targets, "match", hop)
            owner = ((me // 2 - shift) % chips) * 2 + me % 2
            shards.append((moved, owner, sibling))
            shards.append((None, owner ^ 1, None))
    else:
        for shift in range(1, n):
            moved = lax.ppermute(targets, "match", [(j, (j + shift) % n) for j in range(n)])
            shards.append((moved, (me - shift) % n, None))
    state = None
    if tk % width == 0:
        owners = jnp.stack([owner for _, owner, _ in shards]) * (tk // width)
        owners = jnp.pad(owners.astype(jnp.float32), (0, 128 - n))
        table = jnp.broadcast_to(owners[None, :], (8, 128))
    pending = None
    for step, (keys, owner, forward) in enumerate(shards):
        if keys is None:
            keys = pending
        if forward:
            keys, state = lax.optimization_barrier((keys, state))
            pending = lax.ppermute(keys, "match", forward)
        if tk % width == 0:
            pos = table
            seg = width
        else:
            pos = positions(tk, owner * tk, width)
            seg = 0
        state = match_step(
            queries, keys, pos, state, tq, step == 0, step == n - 1, seg, step % 128
        )
    warped, flow = state
    return warped[:count], flow[:count, 0], flow[:count, 1]


def local(source, targets, conv_in, flow_proj, in_bias, conv_out):
    rows, cols, chans = source.shape
    all_rows = rows * lax.axis_size("space")
    width = cols * lax.axis_size("match")
    row_first = lax.axis_index("space") * rows
    col_first = lax.axis_index("match") * cols
    ext = halo_ring(source, HALO)
    targets, ext = lax.optimization_barrier((targets, ext))
    erows, ecols = rows + 2 * HALO, cols + 2 * HALO
    warped, sum_x, sum_y = match(ext.reshape(erows * ecols, chans), targets, width)
    warped = warped.reshape(erows, ecols, chans)
    grow = row_first - HALO + jnp.arange(erows, dtype=jnp.int32)
    gcol = col_first - HALO + jnp.arange(ecols, dtype=jnp.int32)
    inside = ((grow >= 0) & (grow < all_rows))[:, None] & ((gcol >= 0) & (gcol < width))[None, :]
    warped = jnp.where(inside[:, :, None], warped, 0.0)
    col_pos = gcol.astype(jnp.float32) / width
    row_pos = grow.astype(jnp.float32) / width
    flow_x = sum_x.reshape(erows, ecols) - col_pos[None, :]
    flow_y = sum_y.reshape(erows, ecols) - row_pos[:, None]

    pre = lax.conv_general_dilated(
        warped[None], conv_in.astype(jnp.float32), (1, 1), "VALID",
        dimension_numbers=("NHWC", "HWIO", "NHWC"),
        precision=lax.Precision.HIGHEST,
        preferred_element_type=jnp.float32,
    )[0]
    fx1 = flow_x[1:-1, 1:-1]
    fy1 = flow_y[1:-1, 1:-1]
    pre = pre + fx1[:, :, None] * flow_proj[0] + fy1[:, :, None] * flow_proj[1] + in_bias
    hidden = jax.nn.silu(pre).astype(jnp.bfloat16)
    hidden = jnp.where(inside[1:-1, 1:-1, None], hidden, jnp.zeros((), jnp.bfloat16))
    delta = lax.conv_general_dilated(
        hidden[None], jnp.transpose(conv_out, (1, 2, 3, 0)), (1, 1), "VALID",
        dimension_numbers=("NHWC", "HWIO", "NHWC"),
        preferred_element_type=jnp.float32,
    )[0]
    flows = jnp.stack([flow_x[HALO:-HALO, HALO:-HALO], flow_y[HALO:-HALO, HALO:-HALO]])
    return flows + jnp.transpose(delta, (2, 0, 1))


def solution(mesh):
    in_specs = (P("space", "match", None), P("match", None), P(), P(), P(), P())
    out_specs = P(None, "space", "match")
    return jax.shard_map(local, mesh=mesh, in_specs=in_specs, out_specs=out_specs, check_vma=False)
```

```python
import functools
import math

import jax
import jax.numpy as jnp
from jax import lax
from jax.experimental import pallas as pl
from jax.experimental.pallas import tpu as pltpu
from jax.sharding import PartitionSpec as P

HALO = 2


def extended(block, sides, width):
    for axis, dim in sides:
        count = lax.axis_size(axis)
        forward = [(i, i + 1) for i in range(count - 1)]
        backward = [(target, source) for source, target in forward]
        low = lax.ppermute(
            lax.slice_in_dim(block, block.shape[dim] - width, None, axis=dim), axis, forward
        )
        high = lax.ppermute(lax.slice_in_dim(block, 0, width, axis=dim), axis, backward)
        block = jnp.concatenate([low, block, high], axis=dim)
    return block


def row_sums(w, base_ref, width, slot):
    count = w.shape[1] // width
    parts = [w[:, g * width:(g + 1) * width] for g in range(count)]
    weighted = None
    area = parts[-1]
    for g in range(count - 1, 0, -1):
        if g < count - 1:
            area = area + parts[g]
        weighted = area if weighted is None else weighted + area
    if count > 1:
        area = area + parts[0]
    lane = lax.broadcasted_iota(jnp.int32, (1, width), 1)
    col = lane.astype(jnp.float32) / width
    total = jnp.sum(area, axis=1, keepdims=True)
    sum_x = jnp.sum(area * col, axis=1, keepdims=True)
    local = jnp.zeros_like(total) if weighted is None else jnp.sum(weighted, axis=1, keepdims=True)
    sum_y = (base_ref[0:1, slot:slot + 1] * total + local) / width
    lane8 = lax.broadcasted_iota(jnp.int32, (w.shape[0], 8), 1)
    zero = jnp.zeros((), jnp.float32)
    return jnp.where(lane8 == 0, total, jnp.where(lane8 == 1, sum_x, jnp.where(lane8 == 3, sum_y, zero)))


def shard_kernel(*refs, scale, chans, first, last, width, slots):
    parts = len(slots)
    q_ref = refs[0]
    k_refs = refs[1:1 + parts]
    pos_ref = refs[1 + parts]
    rest = refs[2 + parts:]
    if not first:
        m_ref, acc_ref, st_ref = rest[:3]
        rest = rest[3:]
    outs = rest
    scores = [
        lax.dot_general(
            q_ref[...], k_ref[...], (((1,), (1,)), ((), ())),
            preferred_element_type=jnp.float32,
        )
        for k_ref in k_refs
    ]
    peak = jnp.max(scores[0], axis=1, keepdims=True)
    for s in scores[1:]:
        peak = jnp.maximum(peak, jnp.max(s, axis=1, keepdims=True))
    if not first:
        old = m_ref[:, 0:1]
        peak = jnp.maximum(old, peak)
    rate = scale * math.log2(math.e)
    acc = None
    st = None
    for s, k_ref, slot in zip(scores, k_refs, slots):
        w = jnp.exp2((s - peak) * rate)
        hi = w.astype(jnp.bfloat16)
        part_acc = jnp.dot(hi, k_ref[...], preferred_element_type=jnp.float32)
        if width:
            part_st = row_sums(w, pos_ref, width, slot)
        else:
            lo = (w - hi.astype(jnp.float32)).astype(jnp.bfloat16)
            lanes = (((1,), (1,)), ((), ()))
            part_st = lax.dot_general(
                hi, pos_ref[...], lanes, preferred_element_type=jnp.float32
            ) + lax.dot_general(lo, pos_ref[...], lanes, preferred_element_type=jnp.float32)
        acc = part_acc if acc is None else acc + part_acc
        st = part_st if st is None else st + part_st
    if not first:
        alpha = jnp.exp2((old - peak) * rate)
        acc = acc_ref[...] * alpha + acc
        st = st_ref[...] * alpha + st
    if last:
        warped_ref, flow_ref = outs
        total = st[:, 0:1]
        warped_ref[...] = acc / total
        fx = (st[:, 1:2] + st[:, 2:3]) / total
        fy = (st[:, 3:4] + st[:, 4:5]) / total
        lane = lax.broadcasted_iota(jnp.int32, flow_ref.shape, 1)
        flow_ref[...] = jnp.where(lane == 0, fx, jnp.where(lane == 1, fy, 0.0))
    else:
        m_out, acc_out, st_out = outs
        m_out[...] = jnp.broadcast_to(peak, m_out.shape)
        acc_out[...] = acc
        st_out[...] = st


def split_bf16(x):
    hi = x.astype(jnp.bfloat16)
    return hi, (x - hi.astype(jnp.float32)).astype(jnp.bfloat16)


def positions(count, offset, width):
    index = offset + jnp.arange(count, dtype=jnp.int32)
    col_hi, col_lo = split_bf16((index % width).astype(jnp.float32) / width)
    row_hi, row_lo = split_bf16((index // width).astype(jnp.float32) / width)
    zero = jnp.zeros((count,), jnp.bfloat16)
    one = jnp.ones((count,), jnp.bfloat16)
    return jnp.stack([one, col_hi, col_lo, row_hi, row_lo, zero, zero, zero])


def match_step(queries, keys, pos, state, tq, first, last, width, slots):
    padded, chans = queries.shape
    nq = padded // tq
    tk = keys[0].shape[0]
    kernel = functools.partial(
        shard_kernel, scale=1.0 / math.sqrt(chans), chans=chans, first=first, last=last,
        width=width, slots=slots,
    )
    row_spec = lambda width: pl.BlockSpec((tq, width), lambda i: (i, 0))
    in_specs = [row_spec(chans)]
    in_specs += [pl.BlockSpec((tk, chans), lambda i: (0, 0)) for _ in keys]
    in_specs += [pl.BlockSpec(pos.shape, lambda i: (0, 0))]
    args = [queries, *keys, pos]
    if not first:
        in_specs += [row_spec(128), row_spec(chans), row_spec(8)]
        args += list(state)
    if last:
        out_specs = [row_spec(chans), row_spec(128)]
        out_shape = [
            jax.ShapeDtypeStruct((padded, chans), jnp.float32),
            jax.ShapeDtypeStruct((padded, 128), jnp.float32),
        ]
    else:
        out_specs = [row_spec(128), row_spec(chans), row_spec(8)]
        out_shape = [
            jax.ShapeDtypeStruct((padded, 128), jnp.float32),
            jax.ShapeDtypeStruct((padded, chans), jnp.float32),
            jax.ShapeDtypeStruct((padded, 8), jnp.float32),
        ]
    return pl.pallas_call(
        kernel,
        grid=(nq,),
        in_specs=in_specs,
        out_specs=out_specs,
        out_shape=out_shape,
        compiler_params=pltpu.CompilerParams(dimension_semantics=("arbitrary",)),
    )(*args)


def match(queries, targets, width):
    count, chans = queries.shape
    tk = targets.shape[0]
    cap = max(8, (1024 * 2048 // tk) // 8 * 8)
    nq = -(-count // cap)
    tq = -(-(-(-count // nq)) // 8) * 8
    padded = tq * nq
    if padded != count:
        queries = jnp.pad(queries, ((0, padded - count), (0, 0)))
    n = lax.axis_size("match")
    me = lax.axis_index("match")
    shards = [(targets, me, None)]
    if n % 2 == 0:
        chips = n // 2
        sibling = [(j, j ^ 1) for j in range(n)]
        shards.append((lax.ppermute(targets, "match", sibling), me ^ 1, None))
        for shift in range(1, chips):
            hop = [(j, ((j // 2 + shift) % chips) * 2 + j % 2) for j in range(n)]
            moved = lax.ppermute(targets, "match", hop)
            owner = ((me // 2 - shift) % chips) * 2 + me % 2
            shards.append((moved, owner, sibling))
            shards.append((None, owner ^ 1, None))
    else:
        for shift in range(1, n):
            moved = lax.ppermute(targets, "match", [(j, (j + shift) % n) for j in range(n)])
            shards.append((moved, (me - shift) % n, None))
    state = None
    if tk % width == 0:
        owners = jnp.stack([owner for _, owner, _ in shards]) * (tk // width)
        owners = jnp.pad(owners.astype(jnp.float32), (0, 128 - n))
        table = jnp.broadcast_to(owners[None, :], (8, 128))
    pending = None
    whole_rows = tk % width == 0
    if whole_rows and n > 1:
        groups = [[0, 1]] + [[i] for i in range(2, n)]
    else:
        groups = [[i] for i in range(n)]
    for group in groups:
        keys = []
        for step in group:
            key, owner, forward = shards[step]
            if key is None:
                key = pending
            if forward:
                key, state = lax.optimization_barrier((key, state))
                pending = lax.ppermute(key, "match", forward)
            keys.append(key)
        if tk % width == 0:
            pos = table
            seg = width
        else:
            pos = positions(tk, shards[group[0]][1] * tk, width)
            seg = 0
        state = match_step(
            queries, keys, pos, state, tq, group[0] == 0, group[-1] == n - 1, seg,
            tuple(step % 128 for step in group),
        )
    warped, flow = state
    return warped[:count], flow[:count, 0], flow[:count, 1]


def local(source, targets, conv_in, flow_proj, in_bias, conv_out):
    rows, cols, chans = source.shape
    all_rows = rows * lax.axis_size("space")
    width = cols * lax.axis_size("match")
    row_first = lax.axis_index("space") * rows
    col_first = lax.axis_index("match") * cols
    ext = extended(source, (("match", 1),), HALO)
    targets, ext = lax.optimization_barrier((targets, ext))
    ext = extended(ext, (("space", 0),), HALO)
    erows, ecols = rows + 2 * HALO, cols + 2 * HALO
    warped, sum_x, sum_y = match(ext.reshape(erows * ecols, chans), targets, width)
    warped = warped.reshape(erows, ecols, chans)
    grow = row_first - HALO + jnp.arange(erows, dtype=jnp.int32)
    gcol = col_first - HALO + jnp.arange(ecols, dtype=jnp.int32)
    inside = ((grow >= 0) & (grow < all_rows))[:, None] & ((gcol >= 0) & (gcol < width))[None, :]
    warped = jnp.where(inside[:, :, None], warped, 0.0)
    col_pos = gcol.astype(jnp.float32) / width
    row_pos = grow.astype(jnp.float32) / width
    flow_x = sum_x.reshape(erows, ecols) - col_pos[None, :]
    flow_y = sum_y.reshape(erows, ecols) - row_pos[:, None]

    pre = lax.conv_general_dilated(
        warped[None], conv_in.astype(jnp.float32), (1, 1), "VALID",
        dimension_numbers=("NHWC", "HWIO", "NHWC"),
        precision=lax.Precision.HIGHEST,
        preferred_element_type=jnp.float32,
    )[0]
    fx1 = flow_x[1:-1, 1:-1]
    fy1 = flow_y[1:-1, 1:-1]
    pre = pre + fx1[:, :, None] * flow_proj[0] + fy1[:, :, None] * flow_proj[1] + in_bias
    hidden = jax.nn.silu(pre).astype(jnp.bfloat16)
    hidden = jnp.where(inside[1:-1, 1:-1, None], hidden, jnp.zeros((), jnp.bfloat16))
    delta = lax.conv_general_dilated(
        hidden[None], jnp.transpose(conv_out, (1, 2, 3, 0)), (1, 1), "VALID",
        dimension_numbers=("NHWC", "HWIO", "NHWC"),
        preferred_element_type=jnp.float32,
    )[0]
    flows = jnp.stack([flow_x[HALO:-HALO, HALO:-HALO], flow_y[HALO:-HALO, HALO:-HALO]])
    return flows + jnp.transpose(delta, (2, 0, 1))


def solution(mesh):
    in_specs = (P("space", "match", None), P("match", None), P(), P(), P(), P())
    out_specs = P(None, "space", "match")
    return jax.shard_map(local, mesh=mesh, in_specs=in_specs, out_specs=out_specs, check_vma=False)
```

```python
import functools
import math

import jax
import jax.numpy as jnp
from jax import lax
from jax.experimental import pallas as pl
from jax.experimental.pallas import tpu as pltpu
from jax.sharding import PartitionSpec as P

HALO = 2


def extended(block, sides, width):
    for axis, dim in sides:
        count = lax.axis_size(axis)
        forward = [(i, i + 1) for i in range(count - 1)]
        backward = [(target, source) for source, target in forward]
        low = lax.ppermute(
            lax.slice_in_dim(block, block.shape[dim] - width, None, axis=dim), axis, forward
        )
        high = lax.ppermute(lax.slice_in_dim(block, 0, width, axis=dim), axis, backward)
        block = jnp.concatenate([low, block, high], axis=dim)
    return block


def row_sums(w, base_ref, width, slot):
    count = w.shape[1] // width
    parts = [w[:, g * width:(g + 1) * width] for g in range(count)]
    weighted = None
    area = parts[-1]
    for g in range(count - 1, 0, -1):
        if g < count - 1:
            area = area + parts[g]
        weighted = area if weighted is None else weighted + area
    if count > 1:
        area = area + parts[0]
    lane = lax.broadcasted_iota(jnp.int32, (1, width), 1)
    col = lane.astype(jnp.float32) / width
    total = jnp.sum(area, axis=1, keepdims=True)
    sum_x = jnp.sum(area * col, axis=1, keepdims=True)
    local = jnp.zeros_like(total) if weighted is None else jnp.sum(weighted, axis=1, keepdims=True)
    sum_y = (base_ref[0:1, slot:slot + 1] * total + local) / width
    lane8 = lax.broadcasted_iota(jnp.int32, (w.shape[0], 8), 1)
    zero = jnp.zeros((), jnp.float32)
    return jnp.where(lane8 == 0, total, jnp.where(lane8 == 1, sum_x, jnp.where(lane8 == 3, sum_y, zero)))


def shard_kernel(*refs, scale, chans, first, last, width, slots):
    parts = len(slots)
    q_ref = refs[0]
    k_refs = refs[1:1 + parts]
    pos_ref = refs[1 + parts]
    rest = refs[2 + parts:]
    if not first:
        m_ref, acc_ref, st_ref = rest[:3]
        rest = rest[3:]
    outs = rest
    scores = [
        lax.dot_general(
            q_ref[...], k_ref[...], (((1,), (1,)), ((), ())),
            preferred_element_type=jnp.float32,
        )
        for k_ref in k_refs
    ]
    peak = jnp.max(scores[0], axis=1, keepdims=True)
    for s in scores[1:]:
        peak = jnp.maximum(peak, jnp.max(s, axis=1, keepdims=True))
    if not first:
        old = m_ref[:, 0:1]
        peak = jnp.maximum(old, peak)
    rate = scale * math.log2(math.e)
    acc = None
    st = None
    for s, k_ref, slot in zip(scores, k_refs, slots):
        w = jnp.exp2((s - peak) * rate)
        hi = w.astype(jnp.bfloat16)
        part_acc = jnp.dot(hi, k_ref[...], preferred_element_type=jnp.float32)
        if width:
            part_st = row_sums(w, pos_ref, width, slot)
        else:
            lo = (w - hi.astype(jnp.float32)).astype(jnp.bfloat16)
            lanes = (((1,), (1,)), ((), ()))
            part_st = lax.dot_general(
                hi, pos_ref[...], lanes, preferred_element_type=jnp.float32
            ) + lax.dot_general(lo, pos_ref[...], lanes, preferred_element_type=jnp.float32)
        acc = part_acc if acc is None else acc + part_acc
        st = part_st if st is None else st + part_st
    if not first:
        alpha = jnp.exp2((old - peak) * rate)
        acc = acc_ref[...] * alpha + acc
        st = st_ref[...] * alpha + st
    if last:
        warped_ref, flow_ref = outs
        total = st[:, 0:1]
        warped_ref[...] = acc / total
        fx = (st[:, 1:2] + st[:, 2:3]) / total
        fy = (st[:, 3:4] + st[:, 4:5]) / total
        lane = lax.broadcasted_iota(jnp.int32, flow_ref.shape, 1)
        flow_ref[...] = jnp.where(lane == 0, fx, jnp.where(lane == 1, fy, 0.0))
    else:
        m_out, acc_out, st_out = outs
        m_out[...] = jnp.broadcast_to(peak, m_out.shape)
        acc_out[...] = acc
        st_out[...] = st


def split_bf16(x):
    hi = x.astype(jnp.bfloat16)
    return hi, (x - hi.astype(jnp.float32)).astype(jnp.bfloat16)


def positions(count, offset, width):
    index = offset + jnp.arange(count, dtype=jnp.int32)
    col_hi, col_lo = split_bf16((index % width).astype(jnp.float32) / width)
    row_hi, row_lo = split_bf16((index // width).astype(jnp.float32) / width)
    zero = jnp.zeros((count,), jnp.bfloat16)
    one = jnp.ones((count,), jnp.bfloat16)
    return jnp.stack([one, col_hi, col_lo, row_hi, row_lo, zero, zero, zero])


def match_step(queries, keys, pos, state, tq, first, last, width, slots):
    padded, chans = queries.shape
    nq = padded // tq
    tk = keys[0].shape[0]
    kernel = functools.partial(
        shard_kernel, scale=1.0 / math.sqrt(chans), chans=chans, first=first, last=last,
        width=width, slots=slots,
    )
    row_spec = lambda width: pl.BlockSpec((tq, width), lambda i: (i, 0))
    in_specs = [row_spec(chans)]
    in_specs += [pl.BlockSpec((tk, chans), lambda i: (0, 0)) for _ in keys]
    in_specs += [pl.BlockSpec(pos.shape, lambda i: (0, 0))]
    args = [queries, *keys, pos]
    if not first:
        in_specs += [row_spec(128), row_spec(chans), row_spec(8)]
        args += list(state)
    if last:
        out_specs = [row_spec(chans), row_spec(128)]
        out_shape = [
            jax.ShapeDtypeStruct((padded, chans), jnp.float32),
            jax.ShapeDtypeStruct((padded, 128), jnp.float32),
        ]
    else:
        out_specs = [row_spec(128), row_spec(chans), row_spec(8)]
        out_shape = [
            jax.ShapeDtypeStruct((padded, 128), jnp.float32),
            jax.ShapeDtypeStruct((padded, chans), jnp.float32),
            jax.ShapeDtypeStruct((padded, 8), jnp.float32),
        ]
    return pl.pallas_call(
        kernel,
        grid=(nq,),
        in_specs=in_specs,
        out_specs=out_specs,
        out_shape=out_shape,
        compiler_params=pltpu.CompilerParams(dimension_semantics=("arbitrary",)),
    )(*args)


def match(queries, targets, width):
    count, chans = queries.shape
    tk = targets.shape[0]
    cap = max(8, (1024 * 2048 // tk) // 8 * 8)
    nq = -(-count // cap)
    tq = -(-(-(-count // nq)) // 8) * 8
    padded = tq * nq
    if padded != count:
        queries = jnp.pad(queries, ((0, padded - count), (0, 0)))
    n = lax.axis_size("match")
    me = lax.axis_index("match")
    shards = [(targets, me, None)]
    if n % 2 == 0:
        chips = n // 2
        sibling = [(j, j ^ 1) for j in range(n)]
        shards.append((lax.ppermute(targets, "match", sibling), me ^ 1, None))
        for shift in range(1, chips):
            hop = [(j, ((j // 2 + shift) % chips) * 2 + j % 2) for j in range(n)]
            moved = lax.ppermute(targets, "match", hop)
            owner = ((me // 2 - shift) % chips) * 2 + me % 2
            shards.append((moved, owner, sibling))
            shards.append((None, owner ^ 1, None))
    else:
        for shift in range(1, n):
            moved = lax.ppermute(targets, "match", [(j, (j + shift) % n) for j in range(n)])
            shards.append((moved, (me - shift) % n, None))
    state = None
    if tk % width == 0:
        owners = jnp.stack([owner for _, owner, _ in shards]) * (tk // width)
        owners = jnp.pad(owners.astype(jnp.float32), (0, 128 - n))
        table = jnp.broadcast_to(owners[None, :], (8, 128))
    pending = None
    whole_rows = tk % width == 0
    if whole_rows and n > 1:
        groups = [[0]] + ([[1, 2]] if n > 2 else [[1]]) + [[i] for i in range(3, n)]
    else:
        groups = [[i] for i in range(n)]
    for group in groups:
        keys = []
        for step in group:
            key, owner, forward = shards[step]
            if key is None:
                key = pending
            if forward:
                key, state = lax.optimization_barrier((key, state))
                pending = lax.ppermute(key, "match", forward)
            keys.append(key)
        if tk % width == 0:
            pos = table
            seg = width
        else:
            pos = positions(tk, shards[group[0]][1] * tk, width)
            seg = 0
        state = match_step(
            queries, keys, pos, state, tq, group[0] == 0, group[-1] == n - 1, seg,
            tuple(step % 128 for step in group),
        )
    warped, flow = state
    return warped[:count], flow[:count, 0], flow[:count, 1]


def local(source, targets, conv_in, flow_proj, in_bias, conv_out):
    rows, cols, chans = source.shape
    all_rows = rows * lax.axis_size("space")
    width = cols * lax.axis_size("match")
    row_first = lax.axis_index("space") * rows
    col_first = lax.axis_index("match") * cols
    ext = extended(source, (("match", 1),), HALO)
    targets, ext = lax.optimization_barrier((targets, ext))
    ext = extended(ext, (("space", 0),), HALO)
    erows, ecols = rows + 2 * HALO, cols + 2 * HALO
    warped, sum_x, sum_y = match(ext.reshape(erows * ecols, chans), targets, width)
    warped = warped.reshape(erows, ecols, chans)
    grow = row_first - HALO + jnp.arange(erows, dtype=jnp.int32)
    gcol = col_first - HALO + jnp.arange(ecols, dtype=jnp.int32)
    inside = ((grow >= 0) & (grow < all_rows))[:, None] & ((gcol >= 0) & (gcol < width))[None, :]
    warped = jnp.where(inside[:, :, None], warped, 0.0)
    col_pos = gcol.astype(jnp.float32) / width
    row_pos = grow.astype(jnp.float32) / width
    flow_x = sum_x.reshape(erows, ecols) - col_pos[None, :]
    flow_y = sum_y.reshape(erows, ecols) - row_pos[:, None]

    pre = lax.conv_general_dilated(
        warped[None], conv_in.astype(jnp.float32), (1, 1), "VALID",
        dimension_numbers=("NHWC", "HWIO", "NHWC"),
        precision=lax.Precision.HIGHEST,
        preferred_element_type=jnp.float32,
    )[0]
    fx1 = flow_x[1:-1, 1:-1]
    fy1 = flow_y[1:-1, 1:-1]
    pre = pre + fx1[:, :, None] * flow_proj[0] + fy1[:, :, None] * flow_proj[1] + in_bias
    hidden = jax.nn.silu(pre).astype(jnp.bfloat16)
    hidden = jnp.where(inside[1:-1, 1:-1, None], hidden, jnp.zeros((), jnp.bfloat16))
    delta = lax.conv_general_dilated(
        hidden[None], jnp.transpose(conv_out, (1, 2, 3, 0)), (1, 1), "VALID",
        dimension_numbers=("NHWC", "HWIO", "NHWC"),
        preferred_element_type=jnp.float32,
    )[0]
    flows = jnp.stack([flow_x[HALO:-HALO, HALO:-HALO], flow_y[HALO:-HALO, HALO:-HALO]])
    return flows + jnp.transpose(delta, (2, 0, 1))


def solution(mesh):
    in_specs = (P("space", "match", None), P("match", None), P(), P(), P(), P())
    out_specs = P(None, "space", "match")
    return jax.shard_map(local, mesh=mesh, in_specs=in_specs, out_specs=out_specs, check_vma=False)
```

```python
import functools
import math

import jax
import jax.numpy as jnp
from jax import lax
from jax.experimental import pallas as pl
from jax.experimental.pallas import tpu as pltpu
from jax.sharding import PartitionSpec as P

HALO = 2


def extended(block, sides, width):
    for axis, dim in sides:
        count = lax.axis_size(axis)
        forward = [(i, i + 1) for i in range(count - 1)]
        backward = [(target, source) for source, target in forward]
        low = lax.ppermute(
            lax.slice_in_dim(block, block.shape[dim] - width, None, axis=dim), axis, forward
        )
        high = lax.ppermute(lax.slice_in_dim(block, 0, width, axis=dim), axis, backward)
        block = jnp.concatenate([low, block, high], axis=dim)
    return block


def row_sums(w, base_ref, width, slot):
    count = w.shape[1] // width
    parts = [w[:, g * width:(g + 1) * width] for g in range(count)]
    weighted = None
    area = parts[-1]
    for g in range(count - 1, 0, -1):
        if g < count - 1:
            area = area + parts[g]
        weighted = area if weighted is None else weighted + area
    if count > 1:
        area = area + parts[0]
    lane = lax.broadcasted_iota(jnp.int32, (1, width), 1)
    col = lane.astype(jnp.float32) / width
    total = jnp.sum(area, axis=1, keepdims=True)
    sum_x = jnp.sum(area * col, axis=1, keepdims=True)
    local = jnp.zeros_like(total) if weighted is None else jnp.sum(weighted, axis=1, keepdims=True)
    sum_y = (base_ref[0:1, slot:slot + 1] * total + local) / width
    lane8 = lax.broadcasted_iota(jnp.int32, (w.shape[0], 8), 1)
    zero = jnp.zeros((), jnp.float32)
    return jnp.where(lane8 == 0, total, jnp.where(lane8 == 1, sum_x, jnp.where(lane8 == 3, sum_y, zero)))


def shard_kernel(*refs, scale, chans, first, last, width, slots):
    parts = len(slots)
    q_ref = refs[0]
    k_refs = refs[1:1 + parts]
    pos_ref = refs[1 + parts]
    rest = refs[2 + parts:]
    if not first:
        m_ref, acc_ref, st_ref = rest[:3]
        rest = rest[3:]
    outs = rest
    scores = [
        lax.dot_general(
            q_ref[...], k_ref[...], (((1,), (1,)), ((), ())),
            preferred_element_type=jnp.float32,
        )
        for k_ref in k_refs
    ]
    peak = jnp.max(scores[0], axis=1, keepdims=True)
    for s in scores[1:]:
        peak = jnp.maximum(peak, jnp.max(s, axis=1, keepdims=True))
    if not first:
        old = m_ref[:, 0:1]
        peak = jnp.maximum(old, peak)
    rate = scale * math.log2(math.e)
    acc = None
    st = None
    for s, k_ref, slot in zip(scores, k_refs, slots):
        w = jnp.exp2((s - peak) * rate)
        hi = w.astype(jnp.bfloat16)
        part_acc = jnp.dot(hi, k_ref[...], preferred_element_type=jnp.float32)
        if width:
            part_st = row_sums(w, pos_ref, width, slot)
        else:
            lo = (w - hi.astype(jnp.float32)).astype(jnp.bfloat16)
            lanes = (((1,), (1,)), ((), ()))
            part_st = lax.dot_general(
                hi, pos_ref[...], lanes, preferred_element_type=jnp.float32
            ) + lax.dot_general(lo, pos_ref[...], lanes, preferred_element_type=jnp.float32)
        acc = part_acc if acc is None else acc + part_acc
        st = part_st if st is None else st + part_st
    if not first:
        alpha = jnp.exp2((old - peak) * rate)
        acc = acc_ref[...] * alpha + acc
        st = st_ref[...] * alpha + st
    if last:
        warped_ref, flow_ref = outs
        total = st[:, 0:1]
        warped_ref[...] = acc / total
        fx = (st[:, 1:2] + st[:, 2:3]) / total
        fy = (st[:, 3:4] + st[:, 4:5]) / total
        lane = lax.broadcasted_iota(jnp.int32, flow_ref.shape, 1)
        flow_ref[...] = jnp.where(lane == 0, fx, jnp.where(lane == 1, fy, 0.0))
    else:
        m_out, acc_out, st_out = outs
        m_out[...] = jnp.broadcast_to(peak, m_out.shape)
        acc_out[...] = acc
        st_out[...] = st


def split_bf16(x):
    hi = x.astype(jnp.bfloat16)
    return hi, (x - hi.astype(jnp.float32)).astype(jnp.bfloat16)


def positions(count, offset, width):
    index = offset + jnp.arange(count, dtype=jnp.int32)
    col_hi, col_lo = split_bf16((index % width).astype(jnp.float32) / width)
    row_hi, row_lo = split_bf16((index // width).astype(jnp.float32) / width)
    zero = jnp.zeros((count,), jnp.bfloat16)
    one = jnp.ones((count,), jnp.bfloat16)
    return jnp.stack([one, col_hi, col_lo, row_hi, row_lo, zero, zero, zero])


def match_step(queries, keys, pos, state, tq, first, last, width, slots):
    padded, chans = queries.shape
    nq = padded // tq
    tk = keys[0].shape[0]
    kernel = functools.partial(
        shard_kernel, scale=1.0 / math.sqrt(chans), chans=chans, first=first, last=last,
        width=width, slots=slots,
    )
    row_spec = lambda width: pl.BlockSpec((tq, width), lambda i: (i, 0))
    in_specs = [row_spec(chans)]
    in_specs += [pl.BlockSpec((tk, chans), lambda i: (0, 0)) for _ in keys]
    in_specs += [pl.BlockSpec(pos.shape, lambda i: (0, 0))]
    args = [queries, *keys, pos]
    if not first:
        in_specs += [row_spec(128), row_spec(chans), row_spec(8)]
        args += list(state)
    if last:
        out_specs = [row_spec(chans), row_spec(128)]
        out_shape = [
            jax.ShapeDtypeStruct((padded, chans), jnp.float32),
            jax.ShapeDtypeStruct((padded, 128), jnp.float32),
        ]
    else:
        out_specs = [row_spec(128), row_spec(chans), row_spec(8)]
        out_shape = [
            jax.ShapeDtypeStruct((padded, 128), jnp.float32),
            jax.ShapeDtypeStruct((padded, chans), jnp.float32),
            jax.ShapeDtypeStruct((padded, 8), jnp.float32),
        ]
    return pl.pallas_call(
        kernel,
        grid=(nq,),
        in_specs=in_specs,
        out_specs=out_specs,
        out_shape=out_shape,
        compiler_params=pltpu.CompilerParams(dimension_semantics=("arbitrary",)),
    )(*args)


def match(queries, targets, width):
    count, chans = queries.shape
    tk = targets.shape[0]
    cap = max(8, (1024 * 2048 // tk) // 8 * 8)
    nq = -(-count // cap)
    tq = -(-(-(-count // nq)) // 8) * 8
    padded = tq * nq
    if padded != count:
        queries = jnp.pad(queries, ((0, padded - count), (0, 0)))
    n = lax.axis_size("match")
    me = lax.axis_index("match")
    shards = [(targets, me, None)]
    if n % 2 == 0:
        chips = n // 2
        sibling = [(j, j ^ 1) for j in range(n)]
        shards.append((lax.ppermute(targets, "match", sibling), me ^ 1, None))
        for shift in range(1, chips):
            hop = [(j, ((j // 2 + shift) % chips) * 2 + j % 2) for j in range(n)]
            moved = lax.ppermute(targets, "match", hop)
            owner = ((me // 2 - shift) % chips) * 2 + me % 2
            shards.append((moved, owner, sibling))
            shards.append((None, owner ^ 1, None))
    else:
        for shift in range(1, n):
            moved = lax.ppermute(targets, "match", [(j, (j + shift) % n) for j in range(n)])
            shards.append((moved, (me - shift) % n, None))
    state = None
    if tk % width == 0:
        owners = jnp.stack([owner for _, owner, _ in shards]) * (tk // width)
        owners = jnp.pad(owners.astype(jnp.float32), (0, 128 - n))
        table = jnp.broadcast_to(owners[None, :], (8, 128))
    pending = None
    whole_rows = tk % width == 0
    if whole_rows and n > 1:
        groups = [[0]] + ([[1, 2]] if n > 2 else [[1]]) + [[i] for i in range(3, n)]
    else:
        groups = [[i] for i in range(n)]
    for group in groups:
        keys = []
        for step in group:
            key, owner, forward = shards[step]
            if key is None:
                key = pending
            if forward:
                key, state = lax.optimization_barrier((key, state))
                pending = lax.ppermute(key, "match", forward)
            keys.append(key)
        if tk % width == 0:
            pos = table
            seg = width
        else:
            pos = positions(tk, shards[group[0]][1] * tk, width)
            seg = 0
        state = match_step(
            queries, keys, pos, state, tq, group[0] == 0, group[-1] == n - 1, seg,
            tuple(step % 128 for step in group),
        )
    warped, flow = state
    return warped[:count], flow[:count, 0], flow[:count, 1]


def local(source, targets, conv_in, flow_proj, in_bias, conv_out):
    rows, cols, chans = source.shape
    all_rows = rows * lax.axis_size("space")
    width = cols * lax.axis_size("match")
    row_first = lax.axis_index("space") * rows
    col_first = lax.axis_index("match") * cols
    ext = extended(source, (("match", 1),), HALO)
    targets, ext, conv_in, flow_proj, in_bias, conv_out = lax.optimization_barrier(
        (targets, ext, conv_in, flow_proj, in_bias, conv_out)
    )
    ext = extended(ext, (("space", 0),), HALO)
    erows, ecols = rows + 2 * HALO, cols + 2 * HALO
    warped, sum_x, sum_y = match(ext.reshape(erows * ecols, chans), targets, width)
    warped = warped.reshape(erows, ecols, chans)
    grow = row_first - HALO + jnp.arange(erows, dtype=jnp.int32)
    gcol = col_first - HALO + jnp.arange(ecols, dtype=jnp.int32)
    inside = ((grow >= 0) & (grow < all_rows))[:, None] & ((gcol >= 0) & (gcol < width))[None, :]
    warped = jnp.where(inside[:, :, None], warped, 0.0)
    col_pos = gcol.astype(jnp.float32) / width
    row_pos = grow.astype(jnp.float32) / width
    flow_x = sum_x.reshape(erows, ecols) - col_pos[None, :]
    flow_y = sum_y.reshape(erows, ecols) - row_pos[:, None]

    pre = lax.conv_general_dilated(
        warped[None], conv_in.astype(jnp.float32), (1, 1), "VALID",
        dimension_numbers=("NHWC", "HWIO", "NHWC"),
        precision=lax.Precision.HIGHEST,
        preferred_element_type=jnp.float32,
    )[0]
    fx1 = flow_x[1:-1, 1:-1]
    fy1 = flow_y[1:-1, 1:-1]
    pre = pre + fx1[:, :, None] * flow_proj[0] + fy1[:, :, None] * flow_proj[1] + in_bias
    hidden = jax.nn.silu(pre).astype(jnp.bfloat16)
    hidden = jnp.where(inside[1:-1, 1:-1, None], hidden, jnp.zeros((), jnp.bfloat16))
    taps = jnp.transpose(conv_out, (3, 0, 1, 2)).reshape(chans, -1)
    proj = jnp.einsum("hwc,ck->hwk", hidden, taps, preferred_element_type=jnp.float32)
    delta = None
    for tap_a in range(3):
        for tap_b in range(3):
            part = proj[tap_a:tap_a + rows, tap_b:tap_b + cols]
            part = jnp.stack([part[..., o * 9 + tap_a * 3 + tap_b] for o in range(2)])
            delta = part if delta is None else delta + part
    flows = jnp.stack([flow_x[HALO:-HALO, HALO:-HALO], flow_y[HALO:-HALO, HALO:-HALO]])
    return flows + delta


def solution(mesh):
    in_specs = (P("space", "match", None), P("match", None), P(), P(), P(), P())
    out_specs = P(None, "space", "match")
    return jax.shard_map(local, mesh=mesh, in_specs=in_specs, out_specs=out_specs, check_vma=False)
```

```python
import functools
import math

import jax
import jax.numpy as jnp
from jax import lax
from jax.experimental import pallas as pl
from jax.experimental.pallas import tpu as pltpu
from jax.sharding import PartitionSpec as P

HALO = 2


def extended(block, sides, width):
    for axis, dim in sides:
        count = lax.axis_size(axis)
        forward = [(i, i + 1) for i in range(count - 1)]
        backward = [(target, source) for source, target in forward]
        low = lax.ppermute(
            lax.slice_in_dim(block, block.shape[dim] - width, None, axis=dim), axis, forward
        )
        high = lax.ppermute(lax.slice_in_dim(block, 0, width, axis=dim), axis, backward)
        block = jnp.concatenate([low, block, high], axis=dim)
    return block


def row_sums(w, base_ref, width, slot):
    count = w.shape[1] // width
    parts = [w[:, g * width:(g + 1) * width] for g in range(count)]
    weighted = None
    area = parts[-1]
    for g in range(count - 1, 0, -1):
        if g < count - 1:
            area = area + parts[g]
        weighted = area if weighted is None else weighted + area
    if count > 1:
        area = area + parts[0]
    lane = lax.broadcasted_iota(jnp.int32, (1, width), 1)
    col = lane.astype(jnp.float32) / width
    total = jnp.sum(area, axis=1, keepdims=True)
    sum_x = jnp.sum(area * col, axis=1, keepdims=True)
    local = jnp.zeros_like(total) if weighted is None else jnp.sum(weighted, axis=1, keepdims=True)
    sum_y = (base_ref[0:1, slot:slot + 1] * total + local) / width
    lane8 = lax.broadcasted_iota(jnp.int32, (w.shape[0], 8), 1)
    zero = jnp.zeros((), jnp.float32)
    return jnp.where(lane8 == 0, total, jnp.where(lane8 == 1, sum_x, jnp.where(lane8 == 3, sum_y, zero)))


def shard_kernel(*refs, scale, chans, first, last, width, slots):
    parts = len(slots)
    q_ref = refs[0]
    k_refs = refs[1:1 + parts]
    pos_ref = refs[1 + parts]
    rest = refs[2 + parts:]
    if not first:
        m_ref, acc_ref, st_ref = rest[:3]
        rest = rest[3:]
    outs = rest
    scores = [
        lax.dot_general(
            q_ref[...], k_ref[...], (((1,), (1,)), ((), ())),
            preferred_element_type=jnp.float32,
        )
        for k_ref in k_refs
    ]
    peak = jnp.max(scores[0], axis=1, keepdims=True)
    for s in scores[1:]:
        peak = jnp.maximum(peak, jnp.max(s, axis=1, keepdims=True))
    if not first:
        old = m_ref[:, 0:1]
        peak = jnp.maximum(old, peak)
    rate = scale * math.log2(math.e)
    acc = None
    st = None
    for s, k_ref, slot in zip(scores, k_refs, slots):
        w = jnp.exp2((s - peak) * rate)
        hi = w.astype(jnp.bfloat16)
        part_acc = jnp.dot(hi, k_ref[...], preferred_element_type=jnp.float32)
        if width:
            part_st = row_sums(w, pos_ref, width, slot)
        else:
            lo = (w - hi.astype(jnp.float32)).astype(jnp.bfloat16)
            lanes = (((1,), (1,)), ((), ()))
            part_st = lax.dot_general(
                hi, pos_ref[...], lanes, preferred_element_type=jnp.float32
            ) + lax.dot_general(lo, pos_ref[...], lanes, preferred_element_type=jnp.float32)
        acc = part_acc if acc is None else acc + part_acc
        st = part_st if st is None else st + part_st
    if not first:
        alpha = jnp.exp2((old - peak) * rate)
        acc = acc_ref[...] * alpha + acc
        st = st_ref[...] * alpha + st
    if last:
        warped_ref, flow_ref = outs
        total = st[:, 0:1]
        warped_ref[...] = acc / total
        fx = (st[:, 1:2] + st[:, 2:3]) / total
        fy = (st[:, 3:4] + st[:, 4:5]) / total
        lane = lax.broadcasted_iota(jnp.int32, flow_ref.shape, 1)
        flow_ref[...] = jnp.where(lane == 0, fx, jnp.where(lane == 1, fy, 0.0))
    else:
        m_out, acc_out, st_out = outs
        m_out[...] = jnp.broadcast_to(peak, m_out.shape)
        acc_out[...] = acc
        st_out[...] = st


def split_bf16(x):
    hi = x.astype(jnp.bfloat16)
    return hi, (x - hi.astype(jnp.float32)).astype(jnp.bfloat16)


def positions(count, offset, width):
    index = offset + jnp.arange(count, dtype=jnp.int32)
    col_hi, col_lo = split_bf16((index % width).astype(jnp.float32) / width)
    row_hi, row_lo = split_bf16((index // width).astype(jnp.float32) / width)
    zero = jnp.zeros((count,), jnp.bfloat16)
    one = jnp.ones((count,), jnp.bfloat16)
    return jnp.stack([one, col_hi, col_lo, row_hi, row_lo, zero, zero, zero])


def match_step(queries, keys, pos, state, tq, first, last, width, slots):
    padded, chans = queries.shape
    nq = padded // tq
    tk = keys[0].shape[0]
    kernel = functools.partial(
        shard_kernel, scale=1.0 / math.sqrt(chans), chans=chans, first=first, last=last,
        width=width, slots=slots,
    )
    row_spec = lambda width: pl.BlockSpec((tq, width), lambda i: (i, 0))
    in_specs = [row_spec(chans)]
    in_specs += [pl.BlockSpec((tk, chans), lambda i: (0, 0)) for _ in keys]
    in_specs += [pl.BlockSpec(pos.shape, lambda i: (0, 0))]
    args = [queries, *keys, pos]
    if not first:
        in_specs += [row_spec(8), row_spec(chans), row_spec(8)]
        args += list(state)
    if last:
        out_specs = [row_spec(chans), row_spec(8)]
        out_shape = [
            jax.ShapeDtypeStruct((padded, chans), jnp.float32),
            jax.ShapeDtypeStruct((padded, 8), jnp.float32),
        ]
    else:
        out_specs = [row_spec(8), row_spec(chans), row_spec(8)]
        out_shape = [
            jax.ShapeDtypeStruct((padded, 8), jnp.float32),
            jax.ShapeDtypeStruct((padded, chans), jnp.float32),
            jax.ShapeDtypeStruct((padded, 8), jnp.float32),
        ]
    return pl.pallas_call(
        kernel,
        grid=(nq,),
        in_specs=in_specs,
        out_specs=out_specs,
        out_shape=out_shape,
        compiler_params=pltpu.CompilerParams(dimension_semantics=("arbitrary",)),
    )(*args)


def match(queries, targets, width):
    count, chans = queries.shape
    tk = targets.shape[0]
    cap = max(8, (1024 * 2048 // tk) // 8 * 8)
    nq = -(-count // cap)
    tq = -(-(-(-count // nq)) // 8) * 8
    padded = tq * nq
    if padded != count:
        queries = jnp.pad(queries, ((0, padded - count), (0, 0)))
    n = lax.axis_size("match")
    me = lax.axis_index("match")
    shards = [(targets, me, None)]
    if n % 2 == 0:
        chips = n // 2
        sibling = [(j, j ^ 1) for j in range(n)]
        shards.append((lax.ppermute(targets, "match", sibling), me ^ 1, None))
        for shift in range(1, chips):
            hop = [(j, ((j // 2 + shift) % chips) * 2 + j % 2) for j in range(n)]
            moved = lax.ppermute(targets, "match", hop)
            owner = ((me // 2 - shift) % chips) * 2 + me % 2
            shards.append((moved, owner, sibling))
            shards.append((None, owner ^ 1, None))
    else:
        for shift in range(1, n):
            moved = lax.ppermute(targets, "match", [(j, (j + shift) % n) for j in range(n)])
            shards.append((moved, (me - shift) % n, None))
    state = None
    if tk % width == 0:
        owners = jnp.stack([owner for _, owner, _ in shards]) * (tk // width)
        owners = jnp.pad(owners.astype(jnp.float32), (0, 128 - n))
        table = jnp.broadcast_to(owners[None, :], (8, 128))
    pending = None
    whole_rows = tk % width == 0
    if whole_rows and n > 1:
        groups = [[0]] + ([[1, 2]] if n > 2 else [[1]]) + [[i] for i in range(3, n)]
    else:
        groups = [[i] for i in range(n)]
    for group in groups:
        keys = []
        for step in group:
            key, owner, forward = shards[step]
            if key is None:
                key = pending
            if forward:
                key, state = lax.optimization_barrier((key, state))
                pending = lax.ppermute(key, "match", forward)
            keys.append(key)
        if tk % width == 0:
            pos = table
            seg = width
        else:
            pos = positions(tk, shards[group[0]][1] * tk, width)
            seg = 0
        state = match_step(
            queries, keys, pos, state, tq, group[0] == 0, group[-1] == n - 1, seg,
            tuple(step % 128 for step in group),
        )
    warped, flow = state
    return warped[:count], flow[:count, 0], flow[:count, 1]


def local(source, targets, conv_in, flow_proj, in_bias, conv_out):
    rows, cols, chans = source.shape
    all_rows = rows * lax.axis_size("space")
    width = cols * lax.axis_size("match")
    row_first = lax.axis_index("space") * rows
    col_first = lax.axis_index("match") * cols
    ext = extended(source, (("match", 1),), HALO)
    targets, ext, conv_in, flow_proj, in_bias, conv_out = lax.optimization_barrier(
        (targets, ext, conv_in, flow_proj, in_bias, conv_out)
    )
    ext = extended(ext, (("space", 0),), HALO)
    erows, ecols = rows + 2 * HALO, cols + 2 * HALO
    warped, sum_x, sum_y = match(ext.reshape(erows * ecols, chans), targets, width)
    warped = warped.reshape(erows, ecols, chans)
    grow = row_first - HALO + jnp.arange(erows, dtype=jnp.int32)
    gcol = col_first - HALO + jnp.arange(ecols, dtype=jnp.int32)
    inside = ((grow >= 0) & (grow < all_rows))[:, None] & ((gcol >= 0) & (gcol < width))[None, :]
    warped = jnp.where(inside[:, :, None], warped, 0.0)
    col_pos = gcol.astype(jnp.float32) / width
    row_pos = grow.astype(jnp.float32) / width
    flow_x = sum_x.reshape(erows, ecols) - col_pos[None, :]
    flow_y = sum_y.reshape(erows, ecols) - row_pos[:, None]

    pre = lax.conv_general_dilated(
        warped[None], conv_in.astype(jnp.float32), (1, 1), "VALID",
        dimension_numbers=("NHWC", "HWIO", "NHWC"),
        precision=lax.Precision.HIGHEST,
        preferred_element_type=jnp.float32,
    )[0]
    fx1 = flow_x[1:-1, 1:-1]
    fy1 = flow_y[1:-1, 1:-1]
    pre = pre + fx1[:, :, None] * flow_proj[0] + fy1[:, :, None] * flow_proj[1] + in_bias
    hidden = jax.nn.silu(pre).astype(jnp.bfloat16)
    hidden = jnp.where(inside[1:-1, 1:-1, None], hidden, jnp.zeros((), jnp.bfloat16))
    taps = jnp.transpose(conv_out, (3, 0, 1, 2)).reshape(chans, -1)
    proj = jnp.einsum("hwc,ck->hwk", hidden, taps, preferred_element_type=jnp.float32)
    delta = None
    for tap_a in range(3):
        for tap_b in range(3):
            part = proj[tap_a:tap_a + rows, tap_b:tap_b + cols]
            part = jnp.stack([part[..., o * 9 + tap_a * 3 + tap_b] for o in range(2)])
            delta = part if delta is None else delta + part
    flows = jnp.stack([flow_x[HALO:-HALO, HALO:-HALO], flow_y[HALO:-HALO, HALO:-HALO]])
    return flows + delta


def solution(mesh):
    in_specs = (P("space", "match", None), P("match", None), P(), P(), P(), P())
    out_specs = P(None, "space", "match")
    return jax.shard_map(local, mesh=mesh, in_specs=in_specs, out_specs=out_specs, check_vma=False)
```

```python
import functools
import math

import jax
import jax.numpy as jnp
from jax import lax
from jax.experimental import pallas as pl
from jax.experimental.pallas import tpu as pltpu
from jax.sharding import PartitionSpec as P

HALO = 2


def extended(block, sides, width):
    for axis, dim in sides:
        count = lax.axis_size(axis)
        forward = [(i, i + 1) for i in range(count - 1)]
        backward = [(target, source) for source, target in forward]
        low = lax.ppermute(
            lax.slice_in_dim(block, block.shape[dim] - width, None, axis=dim), axis, forward
        )
        high = lax.ppermute(lax.slice_in_dim(block, 0, width, axis=dim), axis, backward)
        block = jnp.concatenate([low, block, high], axis=dim)
    return block


def row_sums(w, base, width):
    count = w.shape[1] // width
    parts = [w[:, g * width:(g + 1) * width] for g in range(count)]
    weighted = None
    area = parts[-1]
    for g in range(count - 1, 0, -1):
        if g < count - 1:
            area = area + parts[g]
        weighted = area if weighted is None else weighted + area
    if count > 1:
        area = area + parts[0]
    lane = lax.broadcasted_iota(jnp.int32, (1, width), 1)
    col = lane.astype(jnp.float32) / width
    total = jnp.sum(area, axis=1, keepdims=True)
    sum_x = jnp.sum(area * col, axis=1, keepdims=True)
    local = jnp.zeros_like(total) if weighted is None else jnp.sum(weighted, axis=1, keepdims=True)
    sum_y = (base * total + local) / width
    lane8 = lax.broadcasted_iota(jnp.int32, (w.shape[0], 8), 1)
    zero = jnp.zeros((), jnp.float32)
    return jnp.where(lane8 == 0, total, jnp.where(lane8 == 1, sum_x, jnp.where(lane8 == 3, sum_y, zero)))


def shard_kernel(*refs, scale, chans, first, last, width, slots):
    parts = len(slots)
    q_ref = refs[0]
    k_refs = refs[1:1 + parts]
    if width:
        pos_ref = None
        rest = refs[1 + parts:]
        me = lax.axis_index("match")
    else:
        pos_ref = refs[1 + parts]
        rest = refs[2 + parts:]
    if not first:
        m_ref, acc_ref, st_ref = rest[:3]
        rest = rest[3:]
    outs = rest
    scores = [
        lax.dot_general(
            q_ref[...], k_ref[...], (((1,), (1,)), ((), ())),
            preferred_element_type=jnp.float32,
        )
        for k_ref in k_refs
    ]
    peak = jnp.max(scores[0], axis=1, keepdims=True)
    for s in scores[1:]:
        peak = jnp.maximum(peak, jnp.max(s, axis=1, keepdims=True))
    if not first:
        old = m_ref[:, 0:1]
        peak = jnp.maximum(old, peak)
    rate = scale * math.log2(math.e)
    acc = None
    st = None
    for s, k_ref, slot in zip(scores, k_refs, slots):
        w = jnp.exp2((s - peak) * rate)
        hi = w.astype(jnp.bfloat16)
        part_acc = jnp.dot(hi, k_ref[...], preferred_element_type=jnp.float32)
        if width:
            base = jnp.float32(0.0)
            for device, rows_first in enumerate(slot):
                base = jnp.where(me == device, jnp.float32(rows_first), base)
            part_st = row_sums(w, base, width)
        else:
            lo = (w - hi.astype(jnp.float32)).astype(jnp.bfloat16)
            lanes = (((1,), (1,)), ((), ()))
            part_st = lax.dot_general(
                hi, pos_ref[...], lanes, preferred_element_type=jnp.float32
            ) + lax.dot_general(lo, pos_ref[...], lanes, preferred_element_type=jnp.float32)
        acc = part_acc if acc is None else acc + part_acc
        st = part_st if st is None else st + part_st
    if not first:
        alpha = jnp.exp2((old - peak) * rate)
        acc = acc_ref[...] * alpha + acc
        st = st_ref[...] * alpha + st
    if last:
        warped_ref, flow_ref = outs
        total = st[:, 0:1]
        warped_ref[...] = acc / total
        fx = (st[:, 1:2] + st[:, 2:3]) / total
        fy = (st[:, 3:4] + st[:, 4:5]) / total
        lane = lax.broadcasted_iota(jnp.int32, flow_ref.shape, 1)
        flow_ref[...] = jnp.where(lane == 0, fx, jnp.where(lane == 1, fy, 0.0))
    else:
        m_out, acc_out, st_out = outs
        m_out[...] = jnp.broadcast_to(peak, m_out.shape)
        acc_out[...] = acc
        st_out[...] = st


def split_bf16(x):
    hi = x.astype(jnp.bfloat16)
    return hi, (x - hi.astype(jnp.float32)).astype(jnp.bfloat16)


def positions(count, offset, width):
    index = offset + jnp.arange(count, dtype=jnp.int32)
    col_hi, col_lo = split_bf16((index % width).astype(jnp.float32) / width)
    row_hi, row_lo = split_bf16((index // width).astype(jnp.float32) / width)
    zero = jnp.zeros((count,), jnp.bfloat16)
    one = jnp.ones((count,), jnp.bfloat16)
    return jnp.stack([one, col_hi, col_lo, row_hi, row_lo, zero, zero, zero])


def match_step(queries, keys, pos, state, tq, first, last, width, slots):
    padded, chans = queries.shape
    nq = padded // tq
    tk = keys[0].shape[0]
    kernel = functools.partial(
        shard_kernel, scale=1.0 / math.sqrt(chans), chans=chans, first=first, last=last,
        width=width, slots=slots,
    )
    row_spec = lambda width: pl.BlockSpec((tq, width), lambda i: (i, 0))
    in_specs = [row_spec(chans)]
    in_specs += [pl.BlockSpec((tk, chans), lambda i: (0, 0)) for _ in keys]
    args = [queries, *keys]
    if pos is not None:
        in_specs += [pl.BlockSpec(pos.shape, lambda i: (0, 0))]
        args.append(pos)
    if not first:
        in_specs += [row_spec(8), row_spec(chans), row_spec(8)]
        args += list(state)
    if last:
        out_specs = [row_spec(chans), row_spec(8)]
        out_shape = [
            jax.ShapeDtypeStruct((padded, chans), jnp.float32),
            jax.ShapeDtypeStruct((padded, 8), jnp.float32),
        ]
    else:
        out_specs = [row_spec(8), row_spec(chans), row_spec(8)]
        out_shape = [
            jax.ShapeDtypeStruct((padded, 8), jnp.float32),
            jax.ShapeDtypeStruct((padded, chans), jnp.float32),
            jax.ShapeDtypeStruct((padded, 8), jnp.float32),
        ]
    return pl.pallas_call(
        kernel,
        grid=(nq,),
        in_specs=in_specs,
        out_specs=out_specs,
        out_shape=out_shape,
        compiler_params=pltpu.CompilerParams(dimension_semantics=("arbitrary",)),
    )(*args)


def match(queries, targets, width):
    count, chans = queries.shape
    tk = targets.shape[0]
    cap = max(8, (1024 * 2048 // tk) // 8 * 8)
    nq = -(-count // cap)
    tq = -(-(-(-count // nq)) // 8) * 8
    padded = tq * nq
    if padded != count:
        queries = jnp.pad(queries, ((0, padded - count), (0, 0)))
    n = lax.axis_size("match")
    me = lax.axis_index("match")
    chips = n // 2
    if n % 2 == 0:
        rules = [lambda m: m, lambda m: m ^ 1]
        for shift in range(1, chips):
            rules.append(lambda m, s=shift: ((m // 2 - s) % chips) * 2 + m % 2)
            rules.append(lambda m, s=shift: (((m // 2 - s) % chips) * 2 + m % 2) ^ 1)
    else:
        rules = [lambda m, s=shift: (m - s) % n for shift in range(n)]
    shards = [(targets, me, None)]
    if n % 2 == 0:
        chips = n // 2
        sibling = [(j, j ^ 1) for j in range(n)]
        shards.append((lax.ppermute(targets, "match", sibling), me ^ 1, None))
        for shift in range(1, chips):
            hop = [(j, ((j // 2 + shift) % chips) * 2 + j % 2) for j in range(n)]
            moved = lax.ppermute(targets, "match", hop)
            owner = ((me // 2 - shift) % chips) * 2 + me % 2
            shards.append((moved, owner, sibling))
            shards.append((None, owner ^ 1, None))
    else:
        for shift in range(1, n):
            moved = lax.ppermute(targets, "match", [(j, (j + shift) % n) for j in range(n)])
            shards.append((moved, (me - shift) % n, None))
    state = None
    pending = None
    whole_rows = tk % width == 0
    if whole_rows and n > 1:
        groups = [[0]] + ([[1, 2]] if n > 2 else [[1]]) + [[i] for i in range(3, n)]
    else:
        groups = [[i] for i in range(n)]
    for group in groups:
        keys = []
        for step in group:
            key, owner, forward = shards[step]
            if key is None:
                key = pending
            if forward:
                key, state = lax.optimization_barrier((key, state))
                pending = lax.ppermute(key, "match", forward)
            keys.append(key)
        if tk % width == 0:
            pos = None
            seg = width
        else:
            pos = positions(tk, shards[group[0]][1] * tk, width)
            seg = 0
        state = match_step(
            queries, keys, pos, state, tq, group[0] == 0, group[-1] == n - 1, seg,
            tuple(tuple(rules[step](m) * (tk // width) for m in range(n)) for step in group),
        )
    warped, flow = state
    return warped[:count], flow[:count, 0], flow[:count, 1]


def local(source, targets, conv_in, flow_proj, in_bias, conv_out):
    rows, cols, chans = source.shape
    all_rows = rows * lax.axis_size("space")
    width = cols * lax.axis_size("match")
    row_first = lax.axis_index("space") * rows
    col_first = lax.axis_index("match") * cols
    ext = extended(source, (("match", 1),), HALO)
    targets, ext, conv_in, flow_proj, in_bias, conv_out = lax.optimization_barrier(
        (targets, ext, conv_in, flow_proj, in_bias, conv_out)
    )
    ext = extended(ext, (("space", 0),), HALO)
    erows, ecols = rows + 2 * HALO, cols + 2 * HALO
    warped, sum_x, sum_y = match(ext.reshape(erows * ecols, chans), targets, width)
    warped = warped.reshape(erows, ecols, chans)
    grow = row_first - HALO + jnp.arange(erows, dtype=jnp.int32)
    gcol = col_first - HALO + jnp.arange(ecols, dtype=jnp.int32)
    inside = ((grow >= 0) & (grow < all_rows))[:, None] & ((gcol >= 0) & (gcol < width))[None, :]
    warped = jnp.where(inside[:, :, None], warped, 0.0)
    col_pos = gcol.astype(jnp.float32) / width
    row_pos = grow.astype(jnp.float32) / width
    flow_x = sum_x.reshape(erows, ecols) - col_pos[None, :]
    flow_y = sum_y.reshape(erows, ecols) - row_pos[:, None]

    pre = lax.conv_general_dilated(
        warped[None], conv_in.astype(jnp.float32), (1, 1), "VALID",
        dimension_numbers=("NHWC", "HWIO", "NHWC"),
        precision=lax.Precision.HIGHEST,
        preferred_element_type=jnp.float32,
    )[0]
    fx1 = flow_x[1:-1, 1:-1]
    fy1 = flow_y[1:-1, 1:-1]
    pre = pre + fx1[:, :, None] * flow_proj[0] + fy1[:, :, None] * flow_proj[1] + in_bias
    hidden = jax.nn.silu(pre).astype(jnp.bfloat16)
    hidden = jnp.where(inside[1:-1, 1:-1, None], hidden, jnp.zeros((), jnp.bfloat16))
    taps = jnp.transpose(conv_out, (3, 0, 1, 2)).reshape(chans, -1)
    proj = jnp.einsum("hwc,ck->hwk", hidden, taps, preferred_element_type=jnp.float32)
    delta = None
    for tap_a in range(3):
        for tap_b in range(3):
            part = proj[tap_a:tap_a + rows, tap_b:tap_b + cols]
            part = jnp.stack([part[..., o * 9 + tap_a * 3 + tap_b] for o in range(2)])
            delta = part if delta is None else delta + part
    flows = jnp.stack([flow_x[HALO:-HALO, HALO:-HALO], flow_y[HALO:-HALO, HALO:-HALO]])
    return flows + delta


def solution(mesh):
    in_specs = (P("space", "match", None), P("match", None), P(), P(), P(), P())
    out_specs = P(None, "space", "match")
    return jax.shard_map(local, mesh=mesh, in_specs=in_specs, out_specs=out_specs, check_vma=False)
```

```python
import functools
import math

import jax
import jax.numpy as jnp
from jax import lax
from jax.experimental import pallas as pl
from jax.experimental.pallas import tpu as pltpu
from jax.sharding import PartitionSpec as P

HALO = 2


def extended(block, sides, width):
    for axis, dim in sides:
        count = lax.axis_size(axis)
        forward = [(i, i + 1) for i in range(count - 1)]
        backward = [(target, source) for source, target in forward]
        low = lax.ppermute(
            lax.slice_in_dim(block, block.shape[dim] - width, None, axis=dim), axis, forward
        )
        high = lax.ppermute(lax.slice_in_dim(block, 0, width, axis=dim), axis, backward)
        block = jnp.concatenate([low, block, high], axis=dim)
    return block


def row_sums(w, base_ref, width, slot):
    count = w.shape[1] // width
    parts = [w[:, g * width:(g + 1) * width] for g in range(count)]
    weighted = None
    area = parts[-1]
    for g in range(count - 1, 0, -1):
        if g < count - 1:
            area = area + parts[g]
        weighted = area if weighted is None else weighted + area
    if count > 1:
        area = area + parts[0]
    lane = lax.broadcasted_iota(jnp.int32, (1, width), 1)
    col = lane.astype(jnp.float32) / width
    total = jnp.sum(area, axis=1, keepdims=True)
    sum_x = jnp.sum(area * col, axis=1, keepdims=True)
    local = jnp.zeros_like(total) if weighted is None else jnp.sum(weighted, axis=1, keepdims=True)
    sum_y = (base_ref[0:1, slot:slot + 1] * total + local) / width
    lane8 = lax.broadcasted_iota(jnp.int32, (w.shape[0], 8), 1)
    zero = jnp.zeros((), jnp.float32)
    return jnp.where(lane8 == 0, total, jnp.where(lane8 == 1, sum_x, jnp.where(lane8 == 3, sum_y, zero)))


def shard_kernel(*refs, scale, chans, first, last, width, slots):
    parts = len(slots)
    q_ref = refs[0]
    k_refs = refs[1:1 + parts]
    pos_ref = refs[1 + parts]
    rest = refs[2 + parts:]
    if not first:
        m_ref, acc_ref, st_ref = rest[:3]
        rest = rest[3:]
    outs = rest
    scores = [
        lax.dot_general(
            q_ref[...], k_ref[...], (((1,), (1,)), ((), ())),
            preferred_element_type=jnp.float32,
        )
        for k_ref in k_refs
    ]
    peak = jnp.max(scores[0], axis=1, keepdims=True)
    for s in scores[1:]:
        peak = jnp.maximum(peak, jnp.max(s, axis=1, keepdims=True))
    if not first:
        old = m_ref[:, 0:1]
        peak = jnp.maximum(old, peak)
    rate = scale * math.log2(math.e)
    acc = None
    st = None
    for s, k_ref, slot in zip(scores, k_refs, slots):
        w = jnp.exp2((s - peak) * rate)
        hi = w.astype(jnp.bfloat16)
        part_acc = jnp.dot(hi, k_ref[...], preferred_element_type=jnp.float32)
        if width:
            part_st = row_sums(w, pos_ref, width, slot)
        else:
            lo = (w - hi.astype(jnp.float32)).astype(jnp.bfloat16)
            lanes = (((1,), (1,)), ((), ()))
            part_st = lax.dot_general(
                hi, pos_ref[...], lanes, preferred_element_type=jnp.float32
            ) + lax.dot_general(lo, pos_ref[...], lanes, preferred_element_type=jnp.float32)
        acc = part_acc if acc is None else acc + part_acc
        st = part_st if st is None else st + part_st
    if not first:
        alpha = jnp.exp2((old - peak) * rate)
        acc = acc_ref[...] * alpha + acc
        st = st_ref[...] * alpha + st
    if last:
        warped_ref, flow_ref = outs
        total = st[:, 0:1]
        warped_ref[...] = acc / total
        fx = (st[:, 1:2] + st[:, 2:3]) / total
        fy = (st[:, 3:4] + st[:, 4:5]) / total
        lane = lax.broadcasted_iota(jnp.int32, flow_ref.shape, 1)
        flow_ref[...] = jnp.where(lane == 0, fx, jnp.where(lane == 1, fy, 0.0))
    else:
        m_out, acc_out, st_out = outs
        m_out[...] = jnp.broadcast_to(peak, m_out.shape)
        acc_out[...] = acc
        st_out[...] = st


def split_bf16(x):
    hi = x.astype(jnp.bfloat16)
    return hi, (x - hi.astype(jnp.float32)).astype(jnp.bfloat16)


def positions(count, offset, width):
    index = offset + jnp.arange(count, dtype=jnp.int32)
    col_hi, col_lo = split_bf16((index % width).astype(jnp.float32) / width)
    row_hi, row_lo = split_bf16((index // width).astype(jnp.float32) / width)
    zero = jnp.zeros((count,), jnp.bfloat16)
    one = jnp.ones((count,), jnp.bfloat16)
    return jnp.stack([one, col_hi, col_lo, row_hi, row_lo, zero, zero, zero])


def match_step(queries, keys, pos, state, tq, first, last, width, slots):
    padded, chans = queries.shape
    nq = padded // tq
    tk = keys[0].shape[0]
    kernel = functools.partial(
        shard_kernel, scale=1.0 / math.sqrt(chans), chans=chans, first=first, last=last,
        width=width, slots=slots,
    )
    row_spec = lambda width: pl.BlockSpec((tq, width), lambda i: (i, 0))
    in_specs = [row_spec(chans)]
    in_specs += [pl.BlockSpec((tk, chans), lambda i: (0, 0)) for _ in keys]
    in_specs += [pl.BlockSpec(pos.shape, lambda i: (0, 0))]
    args = [queries, *keys, pos]
    if not first:
        in_specs += [row_spec(8), row_spec(chans), row_spec(8)]
        args += list(state)
    if last:
        out_specs = [row_spec(chans), row_spec(8)]
        out_shape = [
            jax.ShapeDtypeStruct((padded, chans), jnp.float32),
            jax.ShapeDtypeStruct((padded, 8), jnp.float32),
        ]
    else:
        out_specs = [row_spec(8), row_spec(chans), row_spec(8)]
        out_shape = [
            jax.ShapeDtypeStruct((padded, 8), jnp.float32),
            jax.ShapeDtypeStruct((padded, chans), jnp.float32),
            jax.ShapeDtypeStruct((padded, 8), jnp.float32),
        ]
    return pl.pallas_call(
        kernel,
        grid=(nq,),
        in_specs=in_specs,
        out_specs=out_specs,
        out_shape=out_shape,
        compiler_params=pltpu.CompilerParams(dimension_semantics=("arbitrary",)),
    )(*args)


def match(queries, targets, width):
    count, chans = queries.shape
    tk = targets.shape[0]
    cap = max(8, (1024 * 2048 // tk) // 8 * 8)
    nq = -(-count // cap)
    tq = -(-(-(-count // nq)) // 8) * 8
    padded = tq * nq
    if padded != count:
        queries = jnp.pad(queries, ((0, padded - count), (0, 0)))
    n = lax.axis_size("match")
    me = lax.axis_index("match")
    shards = [(targets, me, None)]
    if n % 2 == 0:
        chips = n // 2
        sibling = [(j, j ^ 1) for j in range(n)]
        shards.append((lax.ppermute(targets, "match", sibling), me ^ 1, None))
        for shift in range(1, chips):
            hop = [(j, ((j // 2 + shift) % chips) * 2 + j % 2) for j in range(n)]
            moved = lax.ppermute(targets, "match", hop)
            owner = ((me // 2 - shift) % chips) * 2 + me % 2
            shards.append((moved, owner, sibling))
            shards.append((None, owner ^ 1, None))
    else:
        for shift in range(1, n):
            moved = lax.ppermute(targets, "match", [(j, (j + shift) % n) for j in range(n)])
            shards.append((moved, (me - shift) % n, None))
    state = None
    if tk % width == 0:
        owners = jnp.stack([owner for _, owner, _ in shards]) * (tk // width)
        owners = jnp.pad(owners.astype(jnp.float32), (0, 128 - n))
        table = jnp.broadcast_to(owners[None, :], (8, 128))
    pending = None
    whole_rows = tk % width == 0
    if whole_rows and n > 1:
        groups = [[0]] + ([[1, 2]] if n > 2 else [[1]]) + [[i] for i in range(3, n)]
    else:
        groups = [[i] for i in range(n)]
    for group in groups:
        keys = []
        for step in group:
            key, owner, forward = shards[step]
            if key is None:
                key = pending
            if forward:
                key, state = lax.optimization_barrier((key, state))
                pending = lax.ppermute(key, "match", forward)
            keys.append(key)
        if tk % width == 0:
            pos = table
            seg = width
        else:
            pos = positions(tk, shards[group[0]][1] * tk, width)
            seg = 0
        state = match_step(
            queries, keys, pos, state, tq, group[0] == 0, group[-1] == n - 1, seg,
            tuple(step % 128 for step in group),
        )
    warped, flow = state
    return warped[:count], flow[:count, 0], flow[:count, 1]


def local(source, targets, conv_in, flow_proj, in_bias, conv_out):
    rows, cols, chans = source.shape
    all_rows = rows * lax.axis_size("space")
    width = cols * lax.axis_size("match")
    row_first = lax.axis_index("space") * rows
    col_first = lax.axis_index("match") * cols
    ext = extended(source, (("match", 1),), HALO)
    small = jnp.concatenate([flow_proj, in_bias[None, :]], axis=0)
    taps = jnp.transpose(conv_out, (3, 0, 1, 2)).reshape(chans, -1)
    targets, ext, conv_in, small, taps = lax.optimization_barrier(
        (targets, ext, conv_in, small, taps)
    )
    ext = extended(ext, (("space", 0),), HALO)
    erows, ecols = rows + 2 * HALO, cols + 2 * HALO
    warped, sum_x, sum_y = match(ext.reshape(erows * ecols, chans), targets, width)
    warped = warped.reshape(erows, ecols, chans)
    grow = row_first - HALO + jnp.arange(erows, dtype=jnp.int32)
    gcol = col_first - HALO + jnp.arange(ecols, dtype=jnp.int32)
    inside = ((grow >= 0) & (grow < all_rows))[:, None] & ((gcol >= 0) & (gcol < width))[None, :]
    warped = jnp.where(inside[:, :, None], warped, 0.0)
    col_pos = gcol.astype(jnp.float32) / width
    row_pos = grow.astype(jnp.float32) / width
    flow_x = sum_x.reshape(erows, ecols) - col_pos[None, :]
    flow_y = sum_y.reshape(erows, ecols) - row_pos[:, None]

    pre = lax.conv_general_dilated(
        warped[None], conv_in.astype(jnp.float32), (1, 1), "VALID",
        dimension_numbers=("NHWC", "HWIO", "NHWC"),
        precision=lax.Precision.HIGHEST,
        preferred_element_type=jnp.float32,
    )[0]
    fx1 = flow_x[1:-1, 1:-1]
    fy1 = flow_y[1:-1, 1:-1]
    pre = pre + fx1[:, :, None] * small[0] + fy1[:, :, None] * small[1] + small[2]
    hidden = jax.nn.silu(pre).astype(jnp.bfloat16)
    hidden = jnp.where(inside[1:-1, 1:-1, None], hidden, jnp.zeros((), jnp.bfloat16))
    proj = jnp.einsum("hwc,ck->hwk", hidden, taps, preferred_element_type=jnp.float32)
    delta = None
    for tap_a in range(3):
        for tap_b in range(3):
            part = proj[tap_a:tap_a + rows, tap_b:tap_b + cols]
            part = jnp.stack([part[..., o * 9 + tap_a * 3 + tap_b] for o in range(2)])
            delta = part if delta is None else delta + part
    flows = jnp.stack([flow_x[HALO:-HALO, HALO:-HALO], flow_y[HALO:-HALO, HALO:-HALO]])
    return flows + delta


def solution(mesh):
    in_specs = (P("space", "match", None), P("match", None), P(), P(), P(), P())
    out_specs = P(None, "space", "match")
    return jax.shard_map(local, mesh=mesh, in_specs=in_specs, out_specs=out_specs, check_vma=False)
```

```python
import functools
import math

import jax
import jax.numpy as jnp
from jax import lax
from jax.experimental import pallas as pl
from jax.experimental.pallas import tpu as pltpu
from jax.sharding import PartitionSpec as P

HALO = 2


def extended(block, sides, width):
    for axis, dim in sides:
        count = lax.axis_size(axis)
        forward = [(i, i + 1) for i in range(count - 1)]
        backward = [(target, source) for source, target in forward]
        low = lax.ppermute(
            lax.slice_in_dim(block, block.shape[dim] - width, None, axis=dim), axis, forward
        )
        high = lax.ppermute(lax.slice_in_dim(block, 0, width, axis=dim), axis, backward)
        block = jnp.concatenate([low, block, high], axis=dim)
    return block


def row_sums(w, base_ref, width, slot):
    count = w.shape[1] // width
    parts = [w[:, g * width:(g + 1) * width] for g in range(count)]
    weighted = None
    area = parts[-1]
    for g in range(count - 1, 0, -1):
        if g < count - 1:
            area = area + parts[g]
        weighted = area if weighted is None else weighted + area
    if count > 1:
        area = area + parts[0]
    lane = lax.broadcasted_iota(jnp.int32, (1, width), 1)
    col = lane.astype(jnp.float32) / width
    total = jnp.sum(area, axis=1, keepdims=True)
    sum_x = jnp.sum(area * col, axis=1, keepdims=True)
    local = jnp.zeros_like(total) if weighted is None else jnp.sum(weighted, axis=1, keepdims=True)
    sum_y = (base_ref[0:1, slot:slot + 1] * total + local) / width
    lane8 = lax.broadcasted_iota(jnp.int32, (w.shape[0], 8), 1)
    zero = jnp.zeros((), jnp.float32)
    return jnp.where(lane8 == 0, total, jnp.where(lane8 == 1, sum_x, jnp.where(lane8 == 3, sum_y, zero)))


def shard_kernel(*refs, scale, chans, first, last, width, slots):
    parts = len(slots)
    q_ref = refs[0]
    k_refs = refs[1:1 + parts]
    pos_ref = refs[1 + parts]
    rest = refs[2 + parts:]
    if not first:
        m_ref, acc_ref, st_ref = rest[:3]
        rest = rest[3:]
    outs = rest
    scores = [
        lax.dot_general(
            q_ref[...], k_ref[...], (((1,), (1,)), ((), ())),
            preferred_element_type=jnp.float32,
        )
        for k_ref in k_refs
    ]
    peak = jnp.max(scores[0], axis=1, keepdims=True)
    for s in scores[1:]:
        peak = jnp.maximum(peak, jnp.max(s, axis=1, keepdims=True))
    if not first:
        old = m_ref[:, 0:1]
        peak = jnp.maximum(old, peak)
    rate = scale * math.log2(math.e)
    acc = None
    st = None
    for s, k_ref, slot in zip(scores, k_refs, slots):
        w = jnp.exp2((s - peak) * rate)
        hi = w.astype(jnp.bfloat16)
        part_acc = jnp.dot(hi, k_ref[...], preferred_element_type=jnp.float32)
        if width:
            part_st = row_sums(w, pos_ref, width, slot)
        else:
            lo = (w - hi.astype(jnp.float32)).astype(jnp.bfloat16)
            lanes = (((1,), (1,)), ((), ()))
            part_st = lax.dot_general(
                hi, pos_ref[...], lanes, preferred_element_type=jnp.float32
            ) + lax.dot_general(lo, pos_ref[...], lanes, preferred_element_type=jnp.float32)
        acc = part_acc if acc is None else acc + part_acc
        st = part_st if st is None else st + part_st
    if not first:
        alpha = jnp.exp2((old - peak) * rate)
        acc = acc_ref[...] * alpha + acc
        st = st_ref[...] * alpha + st
    if last:
        warped_ref, flow_ref = outs
        total = st[:, 0:1]
        warped_ref[...] = acc / total
        fx = (st[:, 1:2] + st[:, 2:3]) / total
        fy = (st[:, 3:4] + st[:, 4:5]) / total
        lane = lax.broadcasted_iota(jnp.int32, flow_ref.shape, 1)
        flow_ref[...] = jnp.where(lane == 0, fx, jnp.where(lane == 1, fy, 0.0))
    else:
        m_out, acc_out, st_out = outs
        m_out[...] = jnp.broadcast_to(peak, m_out.shape)
        acc_out[...] = acc
        st_out[...] = st


def split_bf16(x):
    hi = x.astype(jnp.bfloat16)
    return hi, (x - hi.astype(jnp.float32)).astype(jnp.bfloat16)


def positions(count, offset, width):
    index = offset + jnp.arange(count, dtype=jnp.int32)
    col_hi, col_lo = split_bf16((index % width).astype(jnp.float32) / width)
    row_hi, row_lo = split_bf16((index // width).astype(jnp.float32) / width)
    zero = jnp.zeros((count,), jnp.bfloat16)
    one = jnp.ones((count,), jnp.bfloat16)
    return jnp.stack([one, col_hi, col_lo, row_hi, row_lo, zero, zero, zero])


def match_step(queries, keys, pos, state, tq, first, last, width, slots):
    padded, chans = queries.shape
    nq = padded // tq
    tk = keys[0].shape[0]
    kernel = functools.partial(
        shard_kernel, scale=1.0 / math.sqrt(chans), chans=chans, first=first, last=last,
        width=width, slots=slots,
    )
    row_spec = lambda width: pl.BlockSpec((tq, width), lambda i: (i, 0))
    in_specs = [row_spec(chans)]
    in_specs += [pl.BlockSpec((tk, chans), lambda i: (0, 0)) for _ in keys]
    in_specs += [pl.BlockSpec(pos.shape, lambda i: (0, 0))]
    args = [queries, *keys, pos]
    if not first:
        in_specs += [row_spec(8), row_spec(chans), row_spec(8)]
        args += list(state)
    if last:
        out_specs = [row_spec(chans), row_spec(8)]
        out_shape = [
            jax.ShapeDtypeStruct((padded, chans), jnp.float32),
            jax.ShapeDtypeStruct((padded, 8), jnp.float32),
        ]
    else:
        out_specs = [row_spec(8), row_spec(chans), row_spec(8)]
        out_shape = [
            jax.ShapeDtypeStruct((padded, 8), jnp.float32),
            jax.ShapeDtypeStruct((padded, chans), jnp.float32),
            jax.ShapeDtypeStruct((padded, 8), jnp.float32),
        ]
    return pl.pallas_call(
        kernel,
        grid=(nq,),
        in_specs=in_specs,
        out_specs=out_specs,
        out_shape=out_shape,
        compiler_params=pltpu.CompilerParams(dimension_semantics=("arbitrary",)),
    )(*args)


def match(queries, targets, width):
    count, chans = queries.shape
    tk = targets.shape[0]
    cap = max(8, (1024 * 2048 // tk) // 8 * 8)
    nq = -(-count // cap)
    tq = -(-(-(-count // nq)) // 8) * 8
    padded = tq * nq
    if padded != count:
        queries = jnp.pad(queries, ((0, padded - count), (0, 0)))
    n = lax.axis_size("match")
    me = lax.axis_index("match")
    shards = [(targets, me, None)]
    if n % 2 == 0:
        chips = n // 2
        sibling = [(j, j ^ 1) for j in range(n)]
        shards.append((lax.ppermute(targets, "match", sibling), me ^ 1, None))
        for shift in range(1, chips):
            hop = [(j, ((j // 2 + shift) % chips) * 2 + j % 2) for j in range(n)]
            moved = lax.ppermute(targets, "match", hop)
            owner = ((me // 2 - shift) % chips) * 2 + me % 2
            shards.append((moved, owner, sibling))
            shards.append((None, owner ^ 1, None))
    else:
        for shift in range(1, n):
            moved = lax.ppermute(targets, "match", [(j, (j + shift) % n) for j in range(n)])
            shards.append((moved, (me - shift) % n, None))
    state = None
    if tk % width == 0:
        owners = jnp.stack([owner for _, owner, _ in shards]) * (tk // width)
        owners = jnp.pad(owners.astype(jnp.float32), (0, 128 - n))
        table = jnp.broadcast_to(owners[None, :], (8, 128))
    pending = None
    whole_rows = tk % width == 0
    if whole_rows and n > 1:
        groups = [[i, i + 1] for i in range(0, n, 2)]
    else:
        groups = [[i] for i in range(n)]
    for group in groups:
        keys = []
        for step in group:
            key, owner, forward = shards[step]
            if key is None:
                key = pending
            if forward:
                key, state = lax.optimization_barrier((key, state))
                pending = lax.ppermute(key, "match", forward)
            keys.append(key)
        if tk % width == 0:
            pos = table
            seg = width
        else:
            pos = positions(tk, shards[group[0]][1] * tk, width)
            seg = 0
        state = match_step(
            queries, keys, pos, state, tq, group[0] == 0, group[-1] == n - 1, seg,
            tuple(step % 128 for step in group),
        )
    warped, flow = state
    return warped[:count], flow[:count, 0], flow[:count, 1]


def local(source, targets, conv_in, flow_proj, in_bias, conv_out):
    rows, cols, chans = source.shape
    all_rows = rows * lax.axis_size("space")
    width = cols * lax.axis_size("match")
    row_first = lax.axis_index("space") * rows
    col_first = lax.axis_index("match") * cols
    ext = extended(source, (("match", 1),), HALO)
    small = jnp.concatenate([flow_proj, in_bias[None, :]], axis=0)
    taps = jnp.transpose(conv_out, (3, 0, 1, 2)).reshape(chans, -1)
    targets, ext, conv_in, small, taps = lax.optimization_barrier(
        (targets, ext, conv_in, small, taps)
    )
    ext = extended(ext, (("space", 0),), HALO)
    erows, ecols = rows + 2 * HALO, cols + 2 * HALO
    warped, sum_x, sum_y = match(ext.reshape(erows * ecols, chans), targets, width)
    warped = warped.reshape(erows, ecols, chans)
    grow = row_first - HALO + jnp.arange(erows, dtype=jnp.int32)
    gcol = col_first - HALO + jnp.arange(ecols, dtype=jnp.int32)
    inside = ((grow >= 0) & (grow < all_rows))[:, None] & ((gcol >= 0) & (gcol < width))[None, :]
    warped = jnp.where(inside[:, :, None], warped, 0.0)
    col_pos = gcol.astype(jnp.float32) / width
    row_pos = grow.astype(jnp.float32) / width
    flow_x = sum_x.reshape(erows, ecols) - col_pos[None, :]
    flow_y = sum_y.reshape(erows, ecols) - row_pos[:, None]

    pre = lax.conv_general_dilated(
        warped[None], conv_in.astype(jnp.float32), (1, 1), "VALID",
        dimension_numbers=("NHWC", "HWIO", "NHWC"),
        precision=lax.Precision.HIGHEST,
        preferred_element_type=jnp.float32,
    )[0]
    fx1 = flow_x[1:-1, 1:-1]
    fy1 = flow_y[1:-1, 1:-1]
    pre = pre + fx1[:, :, None] * small[0] + fy1[:, :, None] * small[1] + small[2]
    hidden = jax.nn.silu(pre).astype(jnp.bfloat16)
    hidden = jnp.where(inside[1:-1, 1:-1, None], hidden, jnp.zeros((), jnp.bfloat16))
    proj = jnp.einsum("hwc,ck->hwk", hidden, taps, preferred_element_type=jnp.float32)
    delta = None
    for tap_a in range(3):
        for tap_b in range(3):
            part = proj[tap_a:tap_a + rows, tap_b:tap_b + cols]
            part = jnp.stack([part[..., o * 9 + tap_a * 3 + tap_b] for o in range(2)])
            delta = part if delta is None else delta + part
    flows = jnp.stack([flow_x[HALO:-HALO, HALO:-HALO], flow_y[HALO:-HALO, HALO:-HALO]])
    return flows + delta


def solution(mesh):
    in_specs = (P("space", "match", None), P("match", None), P(), P(), P(), P())
    out_specs = P(None, "space", "match")
    return jax.shard_map(local, mesh=mesh, in_specs=in_specs, out_specs=out_specs, check_vma=False)
```

```python
import functools
import math

import jax
import jax.numpy as jnp
from jax import lax
from jax.experimental import pallas as pl
from jax.experimental.pallas import tpu as pltpu
from jax.sharding import PartitionSpec as P

HALO = 2


def extended(block, sides, width):
    for axis, dim in sides:
        count = lax.axis_size(axis)
        forward = [(i, i + 1) for i in range(count - 1)]
        backward = [(target, source) for source, target in forward]
        low = lax.ppermute(
            lax.slice_in_dim(block, block.shape[dim] - width, None, axis=dim), axis, forward
        )
        high = lax.ppermute(lax.slice_in_dim(block, 0, width, axis=dim), axis, backward)
        block = jnp.concatenate([low, block, high], axis=dim)
    return block


def row_sums(w, base_ref, width, slot):
    count = w.shape[1] // width
    parts = [w[:, g * width:(g + 1) * width] for g in range(count)]
    weighted = None
    area = parts[-1]
    for g in range(count - 1, 0, -1):
        if g < count - 1:
            area = area + parts[g]
        weighted = area if weighted is None else weighted + area
    if count > 1:
        area = area + parts[0]
    lane = lax.broadcasted_iota(jnp.int32, (1, width), 1)
    col = lane.astype(jnp.float32) / width
    total = jnp.sum(area, axis=1, keepdims=True)
    sum_x = jnp.sum(area * col, axis=1, keepdims=True)
    local = jnp.zeros_like(total) if weighted is None else jnp.sum(weighted, axis=1, keepdims=True)
    sum_y = (base_ref[0:1, slot:slot + 1] * total + local) / width
    lane8 = lax.broadcasted_iota(jnp.int32, (w.shape[0], 8), 1)
    zero = jnp.zeros((), jnp.float32)
    return jnp.where(lane8 == 0, total, jnp.where(lane8 == 1, sum_x, jnp.where(lane8 == 3, sum_y, zero)))


def shard_kernel(*refs, scale, chans, first, last, width, slots):
    parts = len(slots)
    q_ref = refs[0]
    k_refs = refs[1:1 + parts]
    pos_ref = refs[1 + parts]
    rest = refs[2 + parts:]
    if not first:
        m_ref, acc_ref, st_ref = rest[:3]
        rest = rest[3:]
    outs = rest
    scores = [
        lax.dot_general(
            q_ref[...], k_ref[...], (((1,), (1,)), ((), ())),
            preferred_element_type=jnp.float32,
        )
        for k_ref in k_refs
    ]
    peak = jnp.max(scores[0], axis=1, keepdims=True)
    for s in scores[1:]:
        peak = jnp.maximum(peak, jnp.max(s, axis=1, keepdims=True))
    if not first:
        old = m_ref[:, 0:1]
        peak = jnp.maximum(old, peak)
    rate = scale * math.log2(math.e)
    acc = None
    st = None
    for s, k_ref, slot in zip(scores, k_refs, slots):
        w = jnp.exp2((s - peak) * rate)
        hi = w.astype(jnp.bfloat16)
        part_acc = jnp.dot(hi, k_ref[...], preferred_element_type=jnp.float32)
        if width:
            part_st = row_sums(w, pos_ref, width, slot)
        else:
            lo = (w - hi.astype(jnp.float32)).astype(jnp.bfloat16)
            lanes = (((1,), (1,)), ((), ()))
            part_st = lax.dot_general(
                hi, pos_ref[...], lanes, preferred_element_type=jnp.float32
            ) + lax.dot_general(lo, pos_ref[...], lanes, preferred_element_type=jnp.float32)
        acc = part_acc if acc is None else acc + part_acc
        st = part_st if st is None else st + part_st
    if not first:
        alpha = jnp.exp2((old - peak) * rate)
        acc = acc_ref[...] * alpha + acc
        st = st_ref[...] * alpha + st
    if last:
        warped_ref, flow_ref = outs
        total = st[:, 0:1]
        warped_ref[...] = acc / total
        fx = (st[:, 1:2] + st[:, 2:3]) / total
        fy = (st[:, 3:4] + st[:, 4:5]) / total
        lane = lax.broadcasted_iota(jnp.int32, flow_ref.shape, 1)
        flow_ref[...] = jnp.where(lane == 0, fx, jnp.where(lane == 1, fy, 0.0))
    else:
        m_out, acc_out, st_out = outs
        m_out[...] = jnp.broadcast_to(peak, m_out.shape)
        acc_out[...] = acc
        st_out[...] = st


def split_bf16(x):
    hi = x.astype(jnp.bfloat16)
    return hi, (x - hi.astype(jnp.float32)).astype(jnp.bfloat16)


def positions(count, offset, width):
    index = offset + jnp.arange(count, dtype=jnp.int32)
    col_hi, col_lo = split_bf16((index % width).astype(jnp.float32) / width)
    row_hi, row_lo = split_bf16((index // width).astype(jnp.float32) / width)
    zero = jnp.zeros((count,), jnp.bfloat16)
    one = jnp.ones((count,), jnp.bfloat16)
    return jnp.stack([one, col_hi, col_lo, row_hi, row_lo, zero, zero, zero])


def match_step(queries, keys, pos, state, tq, first, last, width, slots):
    padded, chans = queries.shape
    nq = padded // tq
    tk = keys[0].shape[0]
    kernel = functools.partial(
        shard_kernel, scale=1.0 / math.sqrt(chans), chans=chans, first=first, last=last,
        width=width, slots=slots,
    )
    row_spec = lambda width: pl.BlockSpec((tq, width), lambda i: (i, 0))
    in_specs = [row_spec(chans)]
    in_specs += [pl.BlockSpec((tk, chans), lambda i: (0, 0)) for _ in keys]
    in_specs += [pl.BlockSpec(pos.shape, lambda i: (0, 0))]
    args = [queries, *keys, pos]
    if not first:
        in_specs += [row_spec(8), row_spec(chans), row_spec(8)]
        args += list(state)
    if last:
        out_specs = [row_spec(chans), row_spec(8)]
        out_shape = [
            jax.ShapeDtypeStruct((padded, chans), jnp.float32),
            jax.ShapeDtypeStruct((padded, 8), jnp.float32),
        ]
    else:
        out_specs = [row_spec(8), row_spec(chans), row_spec(8)]
        out_shape = [
            jax.ShapeDtypeStruct((padded, 8), jnp.float32),
            jax.ShapeDtypeStruct((padded, chans), jnp.float32),
            jax.ShapeDtypeStruct((padded, 8), jnp.float32),
        ]
    return pl.pallas_call(
        kernel,
        grid=(nq,),
        in_specs=in_specs,
        out_specs=out_specs,
        out_shape=out_shape,
        compiler_params=pltpu.CompilerParams(dimension_semantics=("arbitrary",)),
    )(*args)


def shard_owners(n, me):
    if n % 2:
        return [(me - shift) % n for shift in range(n)]
    chips = n // 2
    owners = [me, me ^ 1]
    for shift in range(1, chips):
        owner = ((me // 2 - shift) % chips) * 2 + me % 2
        owners += [owner, owner ^ 1]
    return owners


def row_table(targets, width):
    n = lax.axis_size("match")
    tk = targets.shape[0]
    if tk % width:
        return None
    owners = jnp.stack(shard_owners(n, lax.axis_index("match"))) * (tk // width)
    owners = jnp.pad(owners.astype(jnp.float32), (0, 128 - n))
    return jnp.broadcast_to(owners[None, :], (8, 128))


def match(queries, targets, width, table):
    count, chans = queries.shape
    tk = targets.shape[0]
    cap = max(8, (1024 * 2048 // tk) // 8 * 8)
    nq = -(-count // cap)
    tq = -(-(-(-count // nq)) // 8) * 8
    padded = tq * nq
    if padded != count:
        queries = jnp.pad(queries, ((0, padded - count), (0, 0)))
    n = lax.axis_size("match")
    me = lax.axis_index("match")
    shards = [(targets, me, None)]
    if n % 2 == 0:
        chips = n // 2
        sibling = [(j, j ^ 1) for j in range(n)]
        shards.append((lax.ppermute(targets, "match", sibling), me ^ 1, None))
        for shift in range(1, chips):
            hop = [(j, ((j // 2 + shift) % chips) * 2 + j % 2) for j in range(n)]
            moved = lax.ppermute(targets, "match", hop)
            owner = ((me // 2 - shift) % chips) * 2 + me % 2
            shards.append((moved, owner, sibling))
            shards.append((None, owner ^ 1, None))
    else:
        for shift in range(1, n):
            moved = lax.ppermute(targets, "match", [(j, (j + shift) % n) for j in range(n)])
            shards.append((moved, (me - shift) % n, None))
    state = None
    pending = None
    whole_rows = tk % width == 0
    if whole_rows and n > 1:
        groups = [[i, i + 1] for i in range(0, n, 2)]
    else:
        groups = [[i] for i in range(n)]
    for group in groups:
        keys = []
        for step in group:
            key, owner, forward = shards[step]
            if key is None:
                key = pending
            if forward:
                key, state = lax.optimization_barrier((key, state))
                pending = lax.ppermute(key, "match", forward)
            keys.append(key)
        if tk % width == 0:
            pos = table
            seg = width
        else:
            pos = positions(tk, shards[group[0]][1] * tk, width)
            seg = 0
        state = match_step(
            queries, keys, pos, state, tq, group[0] == 0, group[-1] == n - 1, seg,
            tuple(step % 128 for step in group),
        )
    warped, flow = state
    return warped[:count], flow[:count, 0], flow[:count, 1]


def local(source, targets, conv_in, flow_proj, in_bias, conv_out):
    rows, cols, chans = source.shape
    all_rows = rows * lax.axis_size("space")
    width = cols * lax.axis_size("match")
    row_first = lax.axis_index("space") * rows
    col_first = lax.axis_index("match") * cols
    ext = extended(source, (("match", 1),), HALO)
    small = jnp.concatenate([flow_proj, in_bias[None, :]], axis=0)
    taps = jnp.transpose(conv_out, (3, 0, 1, 2)).reshape(chans, -1)
    table = row_table(targets, width)
    targets, ext, conv_in, small, taps, table = lax.optimization_barrier(
        (targets, ext, conv_in, small, taps, table)
    )
    ext = extended(ext, (("space", 0),), HALO)
    erows, ecols = rows + 2 * HALO, cols + 2 * HALO
    warped, sum_x, sum_y = match(ext.reshape(erows * ecols, chans), targets, width, table)
    warped = warped.reshape(erows, ecols, chans)
    grow = row_first - HALO + jnp.arange(erows, dtype=jnp.int32)
    gcol = col_first - HALO + jnp.arange(ecols, dtype=jnp.int32)
    inside = ((grow >= 0) & (grow < all_rows))[:, None] & ((gcol >= 0) & (gcol < width))[None, :]
    warped = jnp.where(inside[:, :, None], warped, 0.0)
    col_pos = gcol.astype(jnp.float32) / width
    row_pos = grow.astype(jnp.float32) / width
    flow_x = sum_x.reshape(erows, ecols) - col_pos[None, :]
    flow_y = sum_y.reshape(erows, ecols) - row_pos[:, None]

    pre = lax.conv_general_dilated(
        warped[None], conv_in.astype(jnp.float32), (1, 1), "VALID",
        dimension_numbers=("NHWC", "HWIO", "NHWC"),
        precision=lax.Precision.HIGHEST,
        preferred_element_type=jnp.float32,
    )[0]
    fx1 = flow_x[1:-1, 1:-1]
    fy1 = flow_y[1:-1, 1:-1]
    pre = pre + fx1[:, :, None] * small[0] + fy1[:, :, None] * small[1] + small[2]
    hidden = jax.nn.silu(pre).astype(jnp.bfloat16)
    hidden = jnp.where(inside[1:-1, 1:-1, None], hidden, jnp.zeros((), jnp.bfloat16))
    proj = jnp.einsum("hwc,ck->hwk", hidden, taps, preferred_element_type=jnp.float32)
    delta = None
    for tap_a in range(3):
        for tap_b in range(3):
            part = proj[tap_a:tap_a + rows, tap_b:tap_b + cols]
            part = jnp.stack([part[..., o * 9 + tap_a * 3 + tap_b] for o in range(2)])
            delta = part if delta is None else delta + part
    flows = jnp.stack([flow_x[HALO:-HALO, HALO:-HALO], flow_y[HALO:-HALO, HALO:-HALO]])
    return flows + delta


def solution(mesh):
    in_specs = (P("space", "match", None), P("match", None), P(), P(), P(), P())
    out_specs = P(None, "space", "match")
    return jax.shard_map(local, mesh=mesh, in_specs=in_specs, out_specs=out_specs, check_vma=False)
```

```python
import functools
import math

import jax
import jax.numpy as jnp
from jax import lax
from jax.experimental import pallas as pl
from jax.experimental.pallas import tpu as pltpu
from jax.sharding import PartitionSpec as P

HALO = 2


def extended(block, sides, width):
    for axis, dim in sides:
        count = lax.axis_size(axis)
        forward = [(i, i + 1) for i in range(count - 1)]
        backward = [(target, source) for source, target in forward]
        low = lax.ppermute(
            lax.slice_in_dim(block, block.shape[dim] - width, None, axis=dim), axis, forward
        )
        high = lax.ppermute(lax.slice_in_dim(block, 0, width, axis=dim), axis, backward)
        block = jnp.concatenate([low, block, high], axis=dim)
    return block


def row_sums(w, base_ref, width, slot):
    count = w.shape[1] // width
    parts = [w[:, g * width:(g + 1) * width] for g in range(count)]
    weighted = None
    area = parts[-1]
    for g in range(count - 1, 0, -1):
        if g < count - 1:
            area = area + parts[g]
        weighted = area if weighted is None else weighted + area
    if count > 1:
        area = area + parts[0]
    lane = lax.broadcasted_iota(jnp.int32, (1, width), 1)
    col = lane.astype(jnp.float32) / width
    total = jnp.sum(area, axis=1, keepdims=True)
    sum_x = jnp.sum(area * col, axis=1, keepdims=True)
    local = jnp.zeros_like(total) if weighted is None else jnp.sum(weighted, axis=1, keepdims=True)
    sum_y = (base_ref[0:1, slot:slot + 1] * total + local) / width
    lane8 = lax.broadcasted_iota(jnp.int32, (w.shape[0], 8), 1)
    zero = jnp.zeros((), jnp.float32)
    return jnp.where(lane8 == 0, total, jnp.where(lane8 == 1, sum_x, jnp.where(lane8 == 3, sum_y, zero)))


def shard_kernel(*refs, scale, chans, first, last, width, slots):
    parts = len(slots)
    q_ref = refs[0]
    k_refs = refs[1:1 + parts]
    pos_ref = refs[1 + parts]
    rest = refs[2 + parts:]
    if not first:
        m_ref, acc_ref, st_ref = rest[:3]
        rest = rest[3:]
    outs = rest
    scores = [
        lax.dot_general(
            q_ref[...], k_ref[...], (((1,), (1,)), ((), ())),
            preferred_element_type=jnp.float32,
        )
        for k_ref in k_refs
    ]
    peak = jnp.max(scores[0], axis=1, keepdims=True)
    for s in scores[1:]:
        peak = jnp.maximum(peak, jnp.max(s, axis=1, keepdims=True))
    if not first:
        old = m_ref[:, 0:1]
        peak = jnp.maximum(old, peak)
    rate = scale * math.log2(math.e)
    acc = None
    st = None
    for s, k_ref, slot in zip(scores, k_refs, slots):
        w = jnp.exp2((s - peak) * rate)
        hi = w.astype(jnp.bfloat16)
        part_acc = jnp.dot(hi, k_ref[...], preferred_element_type=jnp.float32)
        if width:
            part_st = row_sums(w, pos_ref, width, slot)
        else:
            lo = (w - hi.astype(jnp.float32)).astype(jnp.bfloat16)
            lanes = (((1,), (1,)), ((), ()))
            part_st = lax.dot_general(
                hi, pos_ref[...], lanes, preferred_element_type=jnp.float32
            ) + lax.dot_general(lo, pos_ref[...], lanes, preferred_element_type=jnp.float32)
        acc = part_acc if acc is None else acc + part_acc
        st = part_st if st is None else st + part_st
    if not first:
        alpha = jnp.exp2((old - peak) * rate)
        acc = acc_ref[...] * alpha + acc
        st = st_ref[...] * alpha + st
    if last:
        warped_ref, flow_ref = outs
        total = st[:, 0:1]
        warped_ref[...] = acc / total
        fx = (st[:, 1:2] + st[:, 2:3]) / total
        fy = (st[:, 3:4] + st[:, 4:5]) / total
        lane = lax.broadcasted_iota(jnp.int32, flow_ref.shape, 1)
        flow_ref[...] = jnp.where(lane == 0, fx, jnp.where(lane == 1, fy, 0.0))
    else:
        m_out, acc_out, st_out = outs
        m_out[...] = jnp.broadcast_to(peak, m_out.shape)
        acc_out[...] = acc
        st_out[...] = st


def split_bf16(x):
    hi = x.astype(jnp.bfloat16)
    return hi, (x - hi.astype(jnp.float32)).astype(jnp.bfloat16)


def positions(count, offset, width):
    index = offset + jnp.arange(count, dtype=jnp.int32)
    col_hi, col_lo = split_bf16((index % width).astype(jnp.float32) / width)
    row_hi, row_lo = split_bf16((index // width).astype(jnp.float32) / width)
    zero = jnp.zeros((count,), jnp.bfloat16)
    one = jnp.ones((count,), jnp.bfloat16)
    return jnp.stack([one, col_hi, col_lo, row_hi, row_lo, zero, zero, zero])


def match_step(queries, keys, pos, state, tq, first, last, width, slots):
    padded, chans = queries.shape
    nq = padded // tq
    tk = keys[0].shape[0]
    kernel = functools.partial(
        shard_kernel, scale=1.0 / math.sqrt(chans), chans=chans, first=first, last=last,
        width=width, slots=slots,
    )
    row_spec = lambda width: pl.BlockSpec((tq, width), lambda i: (i, 0))
    in_specs = [row_spec(chans)]
    in_specs += [pl.BlockSpec((tk, chans), lambda i: (0, 0)) for _ in keys]
    in_specs += [pl.BlockSpec(pos.shape, lambda i: (0, 0))]
    args = [queries, *keys, pos]
    if not first:
        in_specs += [row_spec(8), row_spec(chans), row_spec(8)]
        args += list(state)
    if last:
        out_specs = [row_spec(chans), row_spec(8)]
        out_shape = [
            jax.ShapeDtypeStruct((padded, chans), jnp.float32),
            jax.ShapeDtypeStruct((padded, 8), jnp.float32),
        ]
    else:
        out_specs = [row_spec(8), row_spec(chans), row_spec(8)]
        out_shape = [
            jax.ShapeDtypeStruct((padded, 8), jnp.float32),
            jax.ShapeDtypeStruct((padded, chans), jnp.float32),
            jax.ShapeDtypeStruct((padded, 8), jnp.float32),
        ]
    return pl.pallas_call(
        kernel,
        grid=(nq,),
        in_specs=in_specs,
        out_specs=out_specs,
        out_shape=out_shape,
        compiler_params=pltpu.CompilerParams(dimension_semantics=("arbitrary",)),
    )(*args)


def match(queries, targets, width):
    count, chans = queries.shape
    tk = targets.shape[0]
    cap = max(8, (1024 * 2048 // tk) // 8 * 8)
    nq = -(-count // cap)
    tq = -(-(-(-count // nq)) // 8) * 8
    padded = tq * nq
    if padded != count:
        queries = jnp.pad(queries, ((0, padded - count), (0, 0)))
    n = lax.axis_size("match")
    me = lax.axis_index("match")
    shards = [(targets, me, None)]
    if n % 2 == 0:
        chips = n // 2
        sibling = [(j, j ^ 1) for j in range(n)]
        shards.append((lax.ppermute(targets, "match", sibling), me ^ 1, None))
        for shift in range(1, chips):
            hop = [(j, ((j // 2 + shift) % chips) * 2 + j % 2) for j in range(n)]
            moved = lax.ppermute(targets, "match", hop)
            owner = ((me // 2 - shift) % chips) * 2 + me % 2
            shards.append((moved, owner, sibling))
            shards.append((None, owner ^ 1, None))
    else:
        for shift in range(1, n):
            moved = lax.ppermute(targets, "match", [(j, (j + shift) % n) for j in range(n)])
            shards.append((moved, (me - shift) % n, None))
    state = None
    if tk % width == 0:
        owners = jnp.stack([owner for _, owner, _ in shards]) * (tk // width)
        owners = jnp.pad(owners.astype(jnp.float32), (0, 128 - n))
        table = jnp.broadcast_to(owners[None, :], (8, 128))
    pending = None
    whole_rows = tk % width == 0
    if whole_rows and n > 1:
        groups = [[i, i + 1] for i in range(0, n, 2)]
    else:
        groups = [[i] for i in range(n)]
    for group in groups:
        keys = []
        for step in group:
            key, owner, forward = shards[step]
            if key is None:
                key = pending
            if forward:
                key, state = lax.optimization_barrier((key, state))
                pending = lax.ppermute(key, "match", forward)
            keys.append(key)
        if tk % width == 0:
            pos = table
            seg = width
        else:
            pos = positions(tk, shards[group[0]][1] * tk, width)
            seg = 0
        state = match_step(
            queries, keys, pos, state, tq, group[0] == 0, group[-1] == n - 1, seg,
            tuple(step % 128 for step in group),
        )
    warped, flow = state
    return warped[:count], flow[:count, 0], flow[:count, 1]


def local(source, targets, conv_in, flow_proj, in_bias, conv_out):
    rows, cols, chans = source.shape
    all_rows = rows * lax.axis_size("space")
    width = cols * lax.axis_size("match")
    row_first = lax.axis_index("space") * rows
    col_first = lax.axis_index("match") * cols
    ext = extended(source, (("match", 1),), HALO)
    ext = ext.reshape(rows * (cols + 2 * HALO), chans)
    small = jnp.concatenate([flow_proj, in_bias[None, :]], axis=0)
    taps = jnp.transpose(conv_out, (3, 0, 1, 2)).reshape(chans, -1)
    targets, ext, conv_in, small, taps = lax.optimization_barrier(
        (targets, ext, conv_in, small, taps)
    )
    ext = extended(ext, (("space", 0),), HALO * (cols + 2 * HALO))
    erows, ecols = rows + 2 * HALO, cols + 2 * HALO
    warped, sum_x, sum_y = match(ext, targets, width)
    warped = warped.reshape(erows, ecols, chans)
    grow = row_first - HALO + jnp.arange(erows, dtype=jnp.int32)
    gcol = col_first - HALO + jnp.arange(ecols, dtype=jnp.int32)
    inside = ((grow >= 0) & (grow < all_rows))[:, None] & ((gcol >= 0) & (gcol < width))[None, :]
    warped = jnp.where(inside[:, :, None], warped, 0.0)
    col_pos = gcol.astype(jnp.float32) / width
    row_pos = grow.astype(jnp.float32) / width
    flow_x = sum_x.reshape(erows, ecols) - col_pos[None, :]
    flow_y = sum_y.reshape(erows, ecols) - row_pos[:, None]

    pre = lax.conv_general_dilated(
        warped[None], conv_in.astype(jnp.float32), (1, 1), "VALID",
        dimension_numbers=("NHWC", "HWIO", "NHWC"),
        precision=lax.Precision.HIGHEST,
        preferred_element_type=jnp.float32,
    )[0]
    fx1 = flow_x[1:-1, 1:-1]
    fy1 = flow_y[1:-1, 1:-1]
    pre = pre + fx1[:, :, None] * small[0] + fy1[:, :, None] * small[1] + small[2]
    hidden = jax.nn.silu(pre).astype(jnp.bfloat16)
    hidden = jnp.where(inside[1:-1, 1:-1, None], hidden, jnp.zeros((), jnp.bfloat16))
    proj = jnp.einsum("hwc,ck->hwk", hidden, taps, preferred_element_type=jnp.float32)
    delta = None
    for tap_a in range(3):
        for tap_b in range(3):
            part = proj[tap_a:tap_a + rows, tap_b:tap_b + cols]
            part = jnp.stack([part[..., o * 9 + tap_a * 3 + tap_b] for o in range(2)])
            delta = part if delta is None else delta + part
    flows = jnp.stack([flow_x[HALO:-HALO, HALO:-HALO], flow_y[HALO:-HALO, HALO:-HALO]])
    return flows + delta


def solution(mesh):
    in_specs = (P("space", "match", None), P("match", None), P(), P(), P(), P())
    out_specs = P(None, "space", "match")
    return jax.shard_map(local, mesh=mesh, in_specs=in_specs, out_specs=out_specs, check_vma=False)
```

```python
import functools
import math

import jax
import jax.numpy as jnp
from jax import lax
from jax.experimental import pallas as pl
from jax.experimental.pallas import tpu as pltpu
from jax.sharding import PartitionSpec as P

HALO = 2


def extended(block, sides, width):
    for axis, dim in sides:
        count = lax.axis_size(axis)
        forward = [(i, i + 1) for i in range(count - 1)]
        backward = [(target, source) for source, target in forward]
        low = lax.ppermute(
            lax.slice_in_dim(block, block.shape[dim] - width, None, axis=dim), axis, forward
        )
        high = lax.ppermute(lax.slice_in_dim(block, 0, width, axis=dim), axis, backward)
        block = jnp.concatenate([low, block, high], axis=dim)
    return block


def row_sums(w, base_ref, width, slot):
    count = w.shape[1] // width
    parts = [w[:, g * width:(g + 1) * width] for g in range(count)]
    weighted = None
    area = parts[-1]
    for g in range(count - 1, 0, -1):
        if g < count - 1:
            area = area + parts[g]
        weighted = area if weighted is None else weighted + area
    if count > 1:
        area = area + parts[0]
    lane = lax.broadcasted_iota(jnp.int32, (1, width), 1)
    col = lane.astype(jnp.float32) / width
    total = jnp.sum(area, axis=1, keepdims=True)
    sum_x = jnp.sum(area * col, axis=1, keepdims=True)
    local = jnp.zeros_like(total) if weighted is None else jnp.sum(weighted, axis=1, keepdims=True)
    sum_y = (base_ref[0:1, slot:slot + 1] * total + local) / width
    lane8 = lax.broadcasted_iota(jnp.int32, (w.shape[0], 8), 1)
    zero = jnp.zeros((), jnp.float32)
    return jnp.where(lane8 == 0, total, jnp.where(lane8 == 1, sum_x, jnp.where(lane8 == 3, sum_y, zero)))


def shard_kernel(*refs, scale, chans, first, last, width, slots, flip):
    parts = len(slots)
    q_ref = refs[0]
    k_refs = refs[1:1 + parts]
    pos_ref = refs[1 + parts]
    rest = refs[2 + parts:]
    if not first:
        m_ref, acc_ref, st_ref = rest[:3]
        rest = rest[3:]
    outs = rest
    scores = [
        lax.dot_general(
            q_ref[...], k_ref[...], (((1,), (1,)), ((), ())),
            preferred_element_type=jnp.float32,
        )
        for k_ref in k_refs
    ]
    peak = jnp.max(scores[0], axis=1, keepdims=True)
    for s in scores[1:]:
        peak = jnp.maximum(peak, jnp.max(s, axis=1, keepdims=True))
    if not first:
        old = m_ref[:, 0:1]
        peak = jnp.maximum(old, peak)
    rate = scale * math.log2(math.e)
    acc = None
    st = None
    for s, k_ref, slot in zip(scores, k_refs, slots):
        w = jnp.exp2((s - peak) * rate)
        hi = w.astype(jnp.bfloat16)
        part_acc = jnp.dot(hi, k_ref[...], preferred_element_type=jnp.float32)
        if width:
            part_st = row_sums(w, pos_ref, width, slot)
        else:
            lo = (w - hi.astype(jnp.float32)).astype(jnp.bfloat16)
            lanes = (((1,), (1,)), ((), ()))
            part_st = lax.dot_general(
                hi, pos_ref[...], lanes, preferred_element_type=jnp.float32
            ) + lax.dot_general(lo, pos_ref[...], lanes, preferred_element_type=jnp.float32)
        acc = part_acc if acc is None else acc + part_acc
        st = part_st if st is None else st + part_st
    if not first:
        alpha = jnp.exp2((old - peak) * rate)
        acc = acc_ref[...] * alpha + acc
        st = st_ref[...] * alpha + st
    if last and flip:
        warped_ref, flow_ref = outs
        total = st[:, 0:1]
        warped_ref[...] = acc / total
        fx = (st[:, 1:2] + st[:, 2:3]) / total
        fy = (st[:, 3:4] + st[:, 4:5]) / total
        lane = lax.broadcasted_iota(jnp.int32, (st.shape[0], 128), 1)
        flow = jnp.where(lane == 0, fx, jnp.where(lane == 1, fy, 0.0))
        eye = (lax.broadcasted_iota(jnp.int32, (8, 128), 0)
               == lax.broadcasted_iota(jnp.int32, (8, 128), 1)).astype(jnp.bfloat16)
        flipped = None
        for _ in range(3):
            piece = flow.astype(jnp.bfloat16)
            flow = flow - piece.astype(jnp.float32)
            part = lax.dot_general(eye, piece, (((1,), (1,)), ((), ())),
                                   preferred_element_type=jnp.float32)
            flipped = part if flipped is None else flipped + part
        flow_ref[...] = flipped
    elif last:
        warped_ref, flow_ref = outs
        total = st[:, 0:1]
        warped_ref[...] = acc / total
        fx = (st[:, 1:2] + st[:, 2:3]) / total
        fy = (st[:, 3:4] + st[:, 4:5]) / total
        lane = lax.broadcasted_iota(jnp.int32, flow_ref.shape, 1)
        flow_ref[...] = jnp.where(lane == 0, fx, jnp.where(lane == 1, fy, 0.0))
    else:
        m_out, acc_out, st_out = outs
        m_out[...] = jnp.broadcast_to(peak, m_out.shape)
        acc_out[...] = acc
        st_out[...] = st


def split_bf16(x):
    hi = x.astype(jnp.bfloat16)
    return hi, (x - hi.astype(jnp.float32)).astype(jnp.bfloat16)


def positions(count, offset, width):
    index = offset + jnp.arange(count, dtype=jnp.int32)
    col_hi, col_lo = split_bf16((index % width).astype(jnp.float32) / width)
    row_hi, row_lo = split_bf16((index // width).astype(jnp.float32) / width)
    zero = jnp.zeros((count,), jnp.bfloat16)
    one = jnp.ones((count,), jnp.bfloat16)
    return jnp.stack([one, col_hi, col_lo, row_hi, row_lo, zero, zero, zero])


def match_step(queries, keys, pos, state, tq, first, last, width, slots):
    padded, chans = queries.shape
    nq = padded // tq
    tk = keys[0].shape[0]
    kernel = functools.partial(
        shard_kernel, scale=1.0 / math.sqrt(chans), chans=chans, first=first, last=last,
        width=width, slots=slots, flip=nq == 1,
    )
    row_spec = lambda width: pl.BlockSpec((tq, width), lambda i: (i, 0))
    in_specs = [row_spec(chans)]
    in_specs += [pl.BlockSpec((tk, chans), lambda i: (0, 0)) for _ in keys]
    in_specs += [pl.BlockSpec(pos.shape, lambda i: (0, 0))]
    args = [queries, *keys, pos]
    if not first:
        in_specs += [row_spec(8), row_spec(chans), row_spec(8)]
        args += list(state)
    if last and nq == 1:
        out_specs = [row_spec(chans), pl.BlockSpec((8, tq), lambda i: (0, i))]
        out_shape = [
            jax.ShapeDtypeStruct((padded, chans), jnp.float32),
            jax.ShapeDtypeStruct((8, padded), jnp.float32),
        ]
    elif last:
        out_specs = [row_spec(chans), row_spec(8)]
        out_shape = [
            jax.ShapeDtypeStruct((padded, chans), jnp.float32),
            jax.ShapeDtypeStruct((padded, 8), jnp.float32),
        ]
    else:
        out_specs = [row_spec(8), row_spec(chans), row_spec(8)]
        out_shape = [
            jax.ShapeDtypeStruct((padded, 8), jnp.float32),
            jax.ShapeDtypeStruct((padded, chans), jnp.float32),
            jax.ShapeDtypeStruct((padded, 8), jnp.float32),
        ]
    return pl.pallas_call(
        kernel,
        grid=(nq,),
        in_specs=in_specs,
        out_specs=out_specs,
        out_shape=out_shape,
        compiler_params=pltpu.CompilerParams(dimension_semantics=("arbitrary",)),
    )(*args)


def match(queries, targets, width):
    count, chans = queries.shape
    tk = targets.shape[0]
    cap = max(8, (1024 * 2048 // tk) // 8 * 8)
    nq = -(-count // cap)
    tq = -(-(-(-count // nq)) // 8) * 8
    padded = tq * nq
    if padded != count:
        queries = jnp.pad(queries, ((0, padded - count), (0, 0)))
    n = lax.axis_size("match")
    me = lax.axis_index("match")
    shards = [(targets, me, None)]
    if n % 2 == 0:
        chips = n // 2
        sibling = [(j, j ^ 1) for j in range(n)]
        shards.append((lax.ppermute(targets, "match", sibling), me ^ 1, None))
        for shift in range(1, chips):
            hop = [(j, ((j // 2 + shift) % chips) * 2 + j % 2) for j in range(n)]
            moved = lax.ppermute(targets, "match", hop)
            owner = ((me // 2 - shift) % chips) * 2 + me % 2
            shards.append((moved, owner, sibling))
            shards.append((None, owner ^ 1, None))
    else:
        for shift in range(1, n):
            moved = lax.ppermute(targets, "match", [(j, (j + shift) % n) for j in range(n)])
            shards.append((moved, (me - shift) % n, None))
    state = None
    if tk % width == 0:
        owners = jnp.stack([owner for _, owner, _ in shards]) * (tk // width)
        owners = jnp.pad(owners.astype(jnp.float32), (0, 128 - n))
        table = jnp.broadcast_to(owners[None, :], (8, 128))
    pending = None
    whole_rows = tk % width == 0
    if whole_rows and n > 1:
        groups = [[i, i + 1] for i in range(0, n, 2)]
    else:
        groups = [[i] for i in range(n)]
    for group in groups:
        keys = []
        for step in group:
            key, owner, forward = shards[step]
            if key is None:
                key = pending
            if forward:
                key, state = lax.optimization_barrier((key, state))
                pending = lax.ppermute(key, "match", forward)
            keys.append(key)
        if tk % width == 0:
            pos = table
            seg = width
        else:
            pos = positions(tk, shards[group[0]][1] * tk, width)
            seg = 0
        state = match_step(
            queries, keys, pos, state, tq, group[0] == 0, group[-1] == n - 1, seg,
            tuple(step % 128 for step in group),
        )
    warped, flow = state
    if nq == 1:
        return warped[:count], flow[0, :count], flow[1, :count]
    return warped[:count], flow[:count, 0], flow[:count, 1]


def local(source, targets, conv_in, flow_proj, in_bias, conv_out):
    rows, cols, chans = source.shape
    all_rows = rows * lax.axis_size("space")
    width = cols * lax.axis_size("match")
    row_first = lax.axis_index("space") * rows
    col_first = lax.axis_index("match") * cols
    ext = extended(source, (("match", 1),), HALO)
    ext = ext.reshape(rows * (cols + 2 * HALO), chans)
    small = jnp.concatenate([flow_proj, in_bias[None, :]], axis=0)
    taps = jnp.transpose(conv_out, (3, 0, 1, 2)).reshape(chans, -1)
    targets, ext, conv_in, small, taps = lax.optimization_barrier(
        (targets, ext, conv_in, small, taps)
    )
    ext = extended(ext, (("space", 0),), HALO * (cols + 2 * HALO))
    erows, ecols = rows + 2 * HALO, cols + 2 * HALO
    warped, sum_x, sum_y = match(ext, targets, width)
    warped = warped.reshape(erows, ecols, chans)
    grow = row_first - HALO + jnp.arange(erows, dtype=jnp.int32)
    gcol = col_first - HALO + jnp.arange(ecols, dtype=jnp.int32)
    inside = ((grow >= 0) & (grow < all_rows))[:, None] & ((gcol >= 0) & (gcol < width))[None, :]
    warped = jnp.where(inside[:, :, None], warped, 0.0)
    col_pos = gcol.astype(jnp.float32) / width
    row_pos = grow.astype(jnp.float32) / width
    flow_x = sum_x.reshape(erows, ecols) - col_pos[None, :]
    flow_y = sum_y.reshape(erows, ecols) - row_pos[:, None]

    pre = lax.conv_general_dilated(
        warped[None], conv_in.astype(jnp.float32), (1, 1), "VALID",
        dimension_numbers=("NHWC", "HWIO", "NHWC"),
        precision=lax.Precision.HIGHEST,
        preferred_element_type=jnp.float32,
    )[0]
    fx1 = flow_x[1:-1, 1:-1]
    fy1 = flow_y[1:-1, 1:-1]
    pre = pre + fx1[:, :, None] * small[0] + fy1[:, :, None] * small[1] + small[2]
    hidden = jax.nn.silu(pre).astype(jnp.bfloat16)
    hidden = jnp.where(inside[1:-1, 1:-1, None], hidden, jnp.zeros((), jnp.bfloat16))
    proj = jnp.einsum("hwc,ck->hwk", hidden, taps, preferred_element_type=jnp.float32)
    delta = None
    for tap_a in range(3):
        for tap_b in range(3):
            part = proj[tap_a:tap_a + rows, tap_b:tap_b + cols]
            part = jnp.stack([part[..., o * 9 + tap_a * 3 + tap_b] for o in range(2)])
            delta = part if delta is None else delta + part
    flows = jnp.stack([flow_x[HALO:-HALO, HALO:-HALO], flow_y[HALO:-HALO, HALO:-HALO]])
    return flows + delta


def solution(mesh):
    in_specs = (P("space", "match", None), P("match", None), P(), P(), P(), P())
    out_specs = P(None, "space", "match")
    return jax.shard_map(local, mesh=mesh, in_specs=in_specs, out_specs=out_specs, check_vma=False)
```

```python
import functools
import math

import jax
import jax.numpy as jnp
from jax import lax
from jax.experimental import pallas as pl
from jax.experimental.pallas import tpu as pltpu
from jax.sharding import PartitionSpec as P

HALO = 2


def extended(block, sides, width):
    for axis, dim in sides:
        count = lax.axis_size(axis)
        forward = [(i, i + 1) for i in range(count - 1)]
        backward = [(target, source) for source, target in forward]
        low = lax.ppermute(
            lax.slice_in_dim(block, block.shape[dim] - width, None, axis=dim), axis, forward
        )
        high = lax.ppermute(lax.slice_in_dim(block, 0, width, axis=dim), axis, backward)
        block = jnp.concatenate([low, block, high], axis=dim)
    return block


def row_sums(w, base_ref, width, slot):
    count = w.shape[1] // width
    parts = [w[:, g * width:(g + 1) * width] for g in range(count)]
    weighted = None
    area = parts[-1]
    for g in range(count - 1, 0, -1):
        if g < count - 1:
            area = area + parts[g]
        weighted = area if weighted is None else weighted + area
    if count > 1:
        area = area + parts[0]
    lane = lax.broadcasted_iota(jnp.int32, (1, width), 1)
    col = lane.astype(jnp.float32) / width
    total = jnp.sum(area, axis=1, keepdims=True)
    sum_x = jnp.sum(area * col, axis=1, keepdims=True)
    local = jnp.zeros_like(total) if weighted is None else jnp.sum(weighted, axis=1, keepdims=True)
    sum_y = (base_ref[0:1, slot:slot + 1] * total + local) / width
    lane8 = lax.broadcasted_iota(jnp.int32, (w.shape[0], 8), 1)
    zero = jnp.zeros((), jnp.float32)
    return jnp.where(lane8 == 0, total, jnp.where(lane8 == 1, sum_x, jnp.where(lane8 == 3, sum_y, zero)))


def shard_kernel(*refs, scale, chans, first, last, width, slots):
    parts = len(slots)
    q_ref = refs[0]
    k_refs = refs[1:1 + parts]
    pos_ref = refs[1 + parts]
    rest = refs[2 + parts:]
    if not first:
        m_ref, acc_ref, st_ref = rest[:3]
        rest = rest[3:]
    outs = rest
    scores = [
        lax.dot_general(
            q_ref[...], k_ref[...], (((1,), (1,)), ((), ())),
            preferred_element_type=jnp.float32,
        )
        for k_ref in k_refs
    ]
    peak = jnp.max(scores[0], axis=1, keepdims=True)
    for s in scores[1:]:
        peak = jnp.maximum(peak, jnp.max(s, axis=1, keepdims=True))
    if not first:
        old = m_ref[:, 0:1]
        peak = jnp.maximum(old, peak)
    rate = scale * math.log2(math.e)
    acc = None
    st = None
    for s, k_ref, slot in zip(scores, k_refs, slots):
        w = jnp.exp2((s - peak) * rate)
        hi = w.astype(jnp.bfloat16)
        part_acc = jnp.dot(hi, k_ref[...], preferred_element_type=jnp.float32)
        if width:
            part_st = row_sums(w, pos_ref, width, slot)
        else:
            lo = (w - hi.astype(jnp.float32)).astype(jnp.bfloat16)
            lanes = (((1,), (1,)), ((), ()))
            part_st = lax.dot_general(
                hi, pos_ref[...], lanes, preferred_element_type=jnp.float32
            ) + lax.dot_general(lo, pos_ref[...], lanes, preferred_element_type=jnp.float32)
        acc = part_acc if acc is None else acc + part_acc
        st = part_st if st is None else st + part_st
    if not first:
        alpha = jnp.exp2((old - peak) * rate)
        acc = acc_ref[...] * alpha + acc
        st = st_ref[...] * alpha + st
    if last:
        warped_ref, flow_ref = outs
        total = st[:, 0:1]
        warped_ref[...] = acc / total
        fx = (st[:, 1:2] + st[:, 2:3]) / total
        fy = (st[:, 3:4] + st[:, 4:5]) / total
        lane = lax.broadcasted_iota(jnp.int32, flow_ref.shape, 1)
        flow_ref[...] = jnp.where(lane == 0, fx, jnp.where(lane == 1, fy, 0.0))
    else:
        m_out, acc_out, st_out = outs
        m_out[...] = jnp.broadcast_to(peak, m_out.shape)
        acc_out[...] = acc
        st_out[...] = st


def split_bf16(x):
    hi = x.astype(jnp.bfloat16)
    return hi, (x - hi.astype(jnp.float32)).astype(jnp.bfloat16)


def positions(count, offset, width):
    index = offset + jnp.arange(count, dtype=jnp.int32)
    col_hi, col_lo = split_bf16((index % width).astype(jnp.float32) / width)
    row_hi, row_lo = split_bf16((index // width).astype(jnp.float32) / width)
    zero = jnp.zeros((count,), jnp.bfloat16)
    one = jnp.ones((count,), jnp.bfloat16)
    return jnp.stack([one, col_hi, col_lo, row_hi, row_lo, zero, zero, zero])


def match_step(queries, keys, pos, state, tq, first, last, width, slots):
    padded, chans = queries.shape
    nq = padded // tq
    tk = keys[0].shape[0]
    kernel = functools.partial(
        shard_kernel, scale=1.0 / math.sqrt(chans), chans=chans, first=first, last=last,
        width=width, slots=slots,
    )
    row_spec = lambda width: pl.BlockSpec((tq, width), lambda i: (i, 0))
    in_specs = [row_spec(chans)]
    in_specs += [pl.BlockSpec((tk, chans), lambda i: (0, 0)) for _ in keys]
    in_specs += [pl.BlockSpec(pos.shape, lambda i: (0, 0))]
    args = [queries, *keys, pos]
    if not first:
        in_specs += [row_spec(8), row_spec(chans), row_spec(8)]
        args += list(state)
    if last:
        out_specs = [row_spec(chans), row_spec(8)]
        out_shape = [
            jax.ShapeDtypeStruct((padded, chans), jnp.float32),
            jax.ShapeDtypeStruct((padded, 8), jnp.float32),
        ]
    else:
        out_specs = [row_spec(8), row_spec(chans), row_spec(8)]
        out_shape = [
            jax.ShapeDtypeStruct((padded, 8), jnp.float32),
            jax.ShapeDtypeStruct((padded, chans), jnp.float32),
            jax.ShapeDtypeStruct((padded, 8), jnp.float32),
        ]
    return pl.pallas_call(
        kernel,
        grid=(nq,),
        in_specs=in_specs,
        out_specs=out_specs,
        out_shape=out_shape,
        compiler_params=pltpu.CompilerParams(dimension_semantics=("arbitrary",)),
    )(*args)


def shard_owners(n, me):
    if n % 2:
        return [(me - shift) % n for shift in range(n)]
    chips = n // 2
    owners = [me, me ^ 1]
    for shift in range(1, chips):
        owner = ((me // 2 - shift) % chips) * 2 + me % 2
        owners += [owner, owner ^ 1]
    return owners


def row_table(targets, width):
    n = lax.axis_size("match")
    tk = targets.shape[0]
    if tk % width:
        return None
    owners = jnp.stack(shard_owners(n, lax.axis_index("match"))) * (tk // width)
    owners = jnp.pad(owners.astype(jnp.float32), (0, 128 - n))
    return jnp.broadcast_to(owners[None, :], (8, 128))


def match(queries, targets, width, table):
    count, chans = queries.shape
    tk = targets.shape[0]
    cap = max(8, (1024 * 2048 // tk) // 8 * 8)
    nq = -(-count // cap)
    tq = -(-(-(-count // nq)) // 8) * 8
    padded = tq * nq
    if padded != count:
        queries = jnp.pad(queries, ((0, padded - count), (0, 0)))
    n = lax.axis_size("match")
    me = lax.axis_index("match")
    shards = [(targets, me, None)]
    if n % 2 == 0:
        chips = n // 2
        sibling = [(j, j ^ 1) for j in range(n)]
        shards.append((lax.ppermute(targets, "match", sibling), me ^ 1, None))
        for shift in range(1, chips):
            hop = [(j, ((j // 2 + shift) % chips) * 2 + j % 2) for j in range(n)]
            moved = lax.ppermute(targets, "match", hop)
            owner = ((me // 2 - shift) % chips) * 2 + me % 2
            shards.append((moved, owner, sibling))
            shards.append((None, owner ^ 1, None))
    else:
        for shift in range(1, n):
            moved = lax.ppermute(targets, "match", [(j, (j + shift) % n) for j in range(n)])
            shards.append((moved, (me - shift) % n, None))
    state = None
    pending = None
    whole_rows = tk % width == 0
    if whole_rows and n > 1:
        groups = [[i, i + 1] for i in range(0, n, 2)]
    else:
        groups = [[i] for i in range(n)]
    for group in groups:
        keys = []
        for step in group:
            key, owner, forward = shards[step]
            if key is None:
                key = pending
            if forward:
                key, state = lax.optimization_barrier((key, state))
                pending = lax.ppermute(key, "match", forward)
            keys.append(key)
        if tk % width == 0:
            pos = table
            seg = width
        else:
            pos = positions(tk, shards[group[0]][1] * tk, width)
            seg = 0
        state = match_step(
            queries, keys, pos, state, tq, group[0] == 0, group[-1] == n - 1, seg,
            tuple(step % 128 for step in group),
        )
    warped, flow = state
    return warped[:count], flow[:count, 0], flow[:count, 1]


def local(source, targets, conv_in, flow_proj, in_bias, conv_out):
    rows, cols, chans = source.shape
    all_rows = rows * lax.axis_size("space")
    width = cols * lax.axis_size("match")
    row_first = lax.axis_index("space") * rows
    col_first = lax.axis_index("match") * cols
    ext = extended(source, (("match", 1),), HALO)
    ext = ext.reshape(rows * (cols + 2 * HALO), chans)
    small = jnp.concatenate([flow_proj, in_bias[None, :]], axis=0)
    taps = jnp.transpose(conv_out, (3, 0, 1, 2)).reshape(chans, -1)
    table = row_table(targets, width)
    targets, ext, conv_in, small, taps, table = lax.optimization_barrier(
        (targets, ext, conv_in, small, taps, table)
    )
    ext = extended(ext, (("space", 0),), HALO * (cols + 2 * HALO))
    erows, ecols = rows + 2 * HALO, cols + 2 * HALO
    warped, sum_x, sum_y = match(ext, targets, width, table)
    warped = warped.reshape(erows, ecols, chans)
    grow = row_first - HALO + jnp.arange(erows, dtype=jnp.int32)
    gcol = col_first - HALO + jnp.arange(ecols, dtype=jnp.int32)
    inside = ((grow >= 0) & (grow < all_rows))[:, None] & ((gcol >= 0) & (gcol < width))[None, :]
    warped = jnp.where(inside[:, :, None], warped, 0.0)
    col_pos = gcol.astype(jnp.float32) / width
    row_pos = grow.astype(jnp.float32) / width
    flow_x = sum_x.reshape(erows, ecols) - col_pos[None, :]
    flow_y = sum_y.reshape(erows, ecols) - row_pos[:, None]

    pre = lax.conv_general_dilated(
        warped[None], conv_in.astype(jnp.float32), (1, 1), "VALID",
        dimension_numbers=("NHWC", "HWIO", "NHWC"),
        precision=lax.Precision.HIGHEST,
        preferred_element_type=jnp.float32,
    )[0]
    fx1 = flow_x[1:-1, 1:-1]
    fy1 = flow_y[1:-1, 1:-1]
    pre = pre + fx1[:, :, None] * small[0] + fy1[:, :, None] * small[1] + small[2]
    hidden = jax.nn.silu(pre).astype(jnp.bfloat16)
    hidden = jnp.where(inside[1:-1, 1:-1, None], hidden, jnp.zeros((), jnp.bfloat16))
    proj = jnp.einsum("hwc,ck->hwk", hidden, taps, preferred_element_type=jnp.float32)
    delta = None
    for tap_a in range(3):
        for tap_b in range(3):
            part = proj[tap_a:tap_a + rows, tap_b:tap_b + cols]
            part = jnp.stack([part[..., o * 9 + tap_a * 3 + tap_b] for o in range(2)])
            delta = part if delta is None else delta + part
    flows = jnp.stack([flow_x[HALO:-HALO, HALO:-HALO], flow_y[HALO:-HALO, HALO:-HALO]])
    return flows + delta


def solution(mesh):
    in_specs = (P("space", "match", None), P("match", None), P(), P(), P(), P())
    out_specs = P(None, "space", "match")
    return jax.shard_map(local, mesh=mesh, in_specs=in_specs, out_specs=out_specs, check_vma=False)
```

```python
import functools
import math

import jax
import jax.numpy as jnp
from jax import lax
from jax.experimental import pallas as pl
from jax.experimental.pallas import tpu as pltpu
from jax.sharding import PartitionSpec as P

HALO = 2


def extended(block, sides, width):
    for axis, dim in sides:
        count = lax.axis_size(axis)
        forward = [(i, i + 1) for i in range(count - 1)]
        backward = [(target, source) for source, target in forward]
        low = lax.ppermute(
            lax.slice_in_dim(block, block.shape[dim] - width, None, axis=dim), axis, forward
        )
        high = lax.ppermute(lax.slice_in_dim(block, 0, width, axis=dim), axis, backward)
        block = jnp.concatenate([low, block, high], axis=dim)
    return block


def row_sums(w, base_ref, width, slot):
    count = w.shape[1] // width
    parts = [w[:, g * width:(g + 1) * width] for g in range(count)]
    weighted = None
    area = parts[-1]
    for g in range(count - 1, 0, -1):
        if g < count - 1:
            area = area + parts[g]
        weighted = area if weighted is None else weighted + area
    if count > 1:
        area = area + parts[0]
    lane = lax.broadcasted_iota(jnp.int32, (1, width), 1)
    col = lane.astype(jnp.float32) / width
    total = jnp.sum(area, axis=1, keepdims=True)
    sum_x = jnp.sum(area * col, axis=1, keepdims=True)
    local = jnp.zeros_like(total) if weighted is None else jnp.sum(weighted, axis=1, keepdims=True)
    sum_y = (base_ref[0:1, slot:slot + 1] * total + local) / width
    lane8 = lax.broadcasted_iota(jnp.int32, (w.shape[0], 8), 1)
    zero = jnp.zeros((), jnp.float32)
    return jnp.where(lane8 == 0, total, jnp.where(lane8 == 1, sum_x, jnp.where(lane8 == 3, sum_y, zero)))


def shard_kernel(*refs, scale, chans, first, last, width, slots):
    parts = len(slots)
    q_ref = refs[0]
    k_refs = refs[1:1 + parts]
    pos_ref = refs[1 + parts]
    rest = refs[2 + parts:]
    if not first:
        m_ref, acc_ref, st_ref = rest[:3]
        rest = rest[3:]
    outs = rest
    scores = [
        lax.dot_general(
            q_ref[...], k_ref[...], (((1,), (1,)), ((), ())),
            preferred_element_type=jnp.float32,
        )
        for k_ref in k_refs
    ]
    peak = jnp.max(scores[0], axis=1, keepdims=True)
    for s in scores[1:]:
        peak = jnp.maximum(peak, jnp.max(s, axis=1, keepdims=True))
    if not first:
        old = m_ref[:, 0:1]
        peak = jnp.maximum(old, peak)
    rate = scale * math.log2(math.e)
    acc = None
    st = None
    for s, k_ref, slot in zip(scores, k_refs, slots):
        w = jnp.exp2((s - peak) * rate)
        hi = w.astype(jnp.bfloat16)
        part_acc = jnp.dot(hi, k_ref[...], preferred_element_type=jnp.float32)
        if width:
            part_st = row_sums(w, pos_ref, width, slot)
        else:
            lo = (w - hi.astype(jnp.float32)).astype(jnp.bfloat16)
            lanes = (((1,), (1,)), ((), ()))
            part_st = lax.dot_general(
                hi, pos_ref[...], lanes, preferred_element_type=jnp.float32
            ) + lax.dot_general(lo, pos_ref[...], lanes, preferred_element_type=jnp.float32)
        acc = part_acc if acc is None else acc + part_acc
        st = part_st if st is None else st + part_st
    if not first:
        alpha = jnp.exp2((old - peak) * rate)
        acc = acc_ref[...] * alpha + acc
        st = st_ref[...] * alpha + st
    if last:
        warped_ref, flow_ref = outs
        total = st[:, 0:1]
        warped_ref[...] = acc / total
        fx = (st[:, 1:2] + st[:, 2:3]) / total
        fy = (st[:, 3:4] + st[:, 4:5]) / total
        lane = lax.broadcasted_iota(jnp.int32, flow_ref.shape, 1)
        flow_ref[...] = jnp.where(lane == 0, fx, jnp.where(lane == 1, fy, 0.0))
    else:
        m_out, acc_out, st_out = outs
        m_out[...] = jnp.broadcast_to(peak, m_out.shape)
        acc_out[...] = acc
        st_out[...] = st


def split_bf16(x):
    hi = x.astype(jnp.bfloat16)
    return hi, (x - hi.astype(jnp.float32)).astype(jnp.bfloat16)


def positions(count, offset, width):
    index = offset + jnp.arange(count, dtype=jnp.int32)
    col_hi, col_lo = split_bf16((index % width).astype(jnp.float32) / width)
    row_hi, row_lo = split_bf16((index // width).astype(jnp.float32) / width)
    zero = jnp.zeros((count,), jnp.bfloat16)
    one = jnp.ones((count,), jnp.bfloat16)
    return jnp.stack([one, col_hi, col_lo, row_hi, row_lo, zero, zero, zero])


def match_step(queries, keys, pos, state, tq, first, last, width, slots):
    padded, chans = queries.shape
    nq = padded // tq
    tk = keys[0].shape[0]
    kernel = functools.partial(
        shard_kernel, scale=1.0 / math.sqrt(chans), chans=chans, first=first, last=last,
        width=width, slots=slots,
    )
    row_spec = lambda width: pl.BlockSpec((tq, width), lambda i: (i, 0))
    in_specs = [row_spec(chans)]
    in_specs += [pl.BlockSpec((tk, chans), lambda i: (0, 0)) for _ in keys]
    in_specs += [pl.BlockSpec(pos.shape, lambda i: (0, 0))]
    args = [queries, *keys, pos]
    if not first:
        in_specs += [row_spec(8), row_spec(chans), row_spec(8)]
        args += list(state)
    if last:
        out_specs = [row_spec(chans), row_spec(8)]
        out_shape = [
            jax.ShapeDtypeStruct((padded, chans), jnp.float32),
            jax.ShapeDtypeStruct((padded, 8), jnp.float32),
        ]
    else:
        out_specs = [row_spec(8), row_spec(chans), row_spec(8)]
        out_shape = [
            jax.ShapeDtypeStruct((padded, 8), jnp.float32),
            jax.ShapeDtypeStruct((padded, chans), jnp.float32),
            jax.ShapeDtypeStruct((padded, 8), jnp.float32),
        ]
    return pl.pallas_call(
        kernel,
        grid=(nq,),
        in_specs=in_specs,
        out_specs=out_specs,
        out_shape=out_shape,
        compiler_params=pltpu.CompilerParams(dimension_semantics=("arbitrary",)),
    )(*args)


def match(queries, targets, width):
    count, chans = queries.shape
    tk = targets.shape[0]
    cap = max(8, (1024 * 2048 // tk) // 8 * 8)
    nq = -(-count // cap)
    tq = -(-(-(-count // nq)) // 8) * 8
    padded = tq * nq
    if padded != count:
        queries = jnp.pad(queries, ((0, padded - count), (0, 0)))
    n = lax.axis_size("match")
    me = lax.axis_index("match")
    shards = [(targets, me, None)]
    if n % 2 == 0:
        chips = n // 2
        sibling = [(j, j ^ 1) for j in range(n)]
        shards.append((lax.ppermute(targets, "match", sibling), me ^ 1, None))
        for shift in range(1, chips):
            hop = [(j, ((j // 2 + shift) % chips) * 2 + j % 2) for j in range(n)]
            moved = lax.ppermute(targets, "match", hop)
            owner = ((me // 2 - shift) % chips) * 2 + me % 2
            shards.append((moved, owner, sibling))
            shards.append((None, owner ^ 1, None))
    else:
        for shift in range(1, n):
            moved = lax.ppermute(targets, "match", [(j, (j + shift) % n) for j in range(n)])
            shards.append((moved, (me - shift) % n, None))
    state = None
    if tk % width == 0:
        owners = jnp.stack([owner for _, owner, _ in shards]) * (tk // width)
        owners = jnp.pad(owners.astype(jnp.float32), (0, 128 - n))
        table = owners[None, :]
    pending = None
    whole_rows = tk % width == 0
    if whole_rows and n > 1:
        groups = [[i, i + 1] for i in range(0, n, 2)]
    else:
        groups = [[i] for i in range(n)]
    for group in groups:
        keys = []
        for step in group:
            key, owner, forward = shards[step]
            if key is None:
                key = pending
            if forward:
                key, state = lax.optimization_barrier((key, state))
                pending = lax.ppermute(key, "match", forward)
            keys.append(key)
        if tk % width == 0:
            pos = table
            seg = width
        else:
            pos = positions(tk, shards[group[0]][1] * tk, width)
            seg = 0
        state = match_step(
            queries, keys, pos, state, tq, group[0] == 0, group[-1] == n - 1, seg,
            tuple(step % 128 for step in group),
        )
    warped, flow = state
    return warped[:count], flow[:count, 0], flow[:count, 1]


def local(source, targets, conv_in, flow_proj, in_bias, conv_out):
    rows, cols, chans = source.shape
    all_rows = rows * lax.axis_size("space")
    width = cols * lax.axis_size("match")
    row_first = lax.axis_index("space") * rows
    col_first = lax.axis_index("match") * cols
    ext = extended(source, (("match", 1),), HALO)
    ext = ext.reshape(rows * (cols + 2 * HALO), chans)
    small = jnp.concatenate([flow_proj, in_bias[None, :]], axis=0)
    taps = jnp.transpose(conv_out, (3, 0, 1, 2)).reshape(chans, -1)
    targets, ext, conv_in, small, taps = lax.optimization_barrier(
        (targets, ext, conv_in, small, taps)
    )
    ext = extended(ext, (("space", 0),), HALO * (cols + 2 * HALO))
    erows, ecols = rows + 2 * HALO, cols + 2 * HALO
    warped, sum_x, sum_y = match(ext, targets, width)
    warped = warped.reshape(erows, ecols, chans)
    grow = row_first - HALO + jnp.arange(erows, dtype=jnp.int32)
    gcol = col_first - HALO + jnp.arange(ecols, dtype=jnp.int32)
    inside = ((grow >= 0) & (grow < all_rows))[:, None] & ((gcol >= 0) & (gcol < width))[None, :]
    warped = jnp.where(inside[:, :, None], warped, 0.0)
    col_pos = gcol.astype(jnp.float32) / width
    row_pos = grow.astype(jnp.float32) / width
    flow_x = sum_x.reshape(erows, ecols) - col_pos[None, :]
    flow_y = sum_y.reshape(erows, ecols) - row_pos[:, None]

    pre = lax.conv_general_dilated(
        warped[None], conv_in.astype(jnp.float32), (1, 1), "VALID",
        dimension_numbers=("NHWC", "HWIO", "NHWC"),
        precision=lax.Precision.HIGHEST,
        preferred_element_type=jnp.float32,
    )[0]
    fx1 = flow_x[1:-1, 1:-1]
    fy1 = flow_y[1:-1, 1:-1]
    pre = pre + fx1[:, :, None] * small[0] + fy1[:, :, None] * small[1] + small[2]
    hidden = jax.nn.silu(pre).astype(jnp.bfloat16)
    hidden = jnp.where(inside[1:-1, 1:-1, None], hidden, jnp.zeros((), jnp.bfloat16))
    proj = jnp.einsum("hwc,ck->hwk", hidden, taps, preferred_element_type=jnp.float32)
    delta = None
    for tap_a in range(3):
        for tap_b in range(3):
            part = proj[tap_a:tap_a + rows, tap_b:tap_b + cols]
            part = jnp.stack([part[..., o * 9 + tap_a * 3 + tap_b] for o in range(2)])
            delta = part if delta is None else delta + part
    flows = jnp.stack([flow_x[HALO:-HALO, HALO:-HALO], flow_y[HALO:-HALO, HALO:-HALO]])
    return flows + delta


def solution(mesh):
    in_specs = (P("space", "match", None), P("match", None), P(), P(), P(), P())
    out_specs = P(None, "space", "match")
    return jax.shard_map(local, mesh=mesh, in_specs=in_specs, out_specs=out_specs, check_vma=False)
```

```python
import functools
import math

import jax
import jax.numpy as jnp
from jax import lax
from jax.experimental import pallas as pl
from jax.experimental.pallas import tpu as pltpu
from jax.sharding import PartitionSpec as P

HALO = 2


def extended(block, sides, width):
    for axis, dim in sides:
        count = lax.axis_size(axis)
        forward = [(i, i + 1) for i in range(count - 1)]
        backward = [(target, source) for source, target in forward]
        low = lax.ppermute(
            lax.slice_in_dim(block, block.shape[dim] - width, None, axis=dim), axis, forward
        )
        high = lax.ppermute(lax.slice_in_dim(block, 0, width, axis=dim), axis, backward)
        block = jnp.concatenate([low, block, high], axis=dim)
    return block


def row_sums(w, base_ref, width, slot):
    count = w.shape[1] // width
    parts = [w[:, g * width:(g + 1) * width] for g in range(count)]
    weighted = None
    area = parts[-1]
    for g in range(count - 1, 0, -1):
        if g < count - 1:
            area = area + parts[g]
        weighted = area if weighted is None else weighted + area
    if count > 1:
        area = area + parts[0]
    lane = lax.broadcasted_iota(jnp.int32, (1, width), 1)
    col = lane.astype(jnp.float32) / width
    total = jnp.sum(area, axis=1, keepdims=True)
    sum_x = jnp.sum(area * col, axis=1, keepdims=True)
    local = jnp.zeros_like(total) if weighted is None else jnp.sum(weighted, axis=1, keepdims=True)
    sum_y = (base_ref[0:1, slot:slot + 1] * total + local) / width
    lane8 = lax.broadcasted_iota(jnp.int32, (w.shape[0], 8), 1)
    zero = jnp.zeros((), jnp.float32)
    return jnp.where(lane8 == 0, total, jnp.where(lane8 == 1, sum_x, jnp.where(lane8 == 3, sum_y, zero)))


def shard_kernel(*refs, scale, chans, first, last, width, slots):
    parts = len(slots)
    q_ref = refs[0]
    k_refs = refs[1:1 + parts]
    pos_ref = refs[1 + parts]
    rest = refs[2 + parts:]
    if not first:
        m_ref, acc_ref, st_ref = rest[:3]
        rest = rest[3:]
    outs = rest
    scores = [
        lax.dot_general(
            q_ref[...], k_ref[...], (((1,), (1,)), ((), ())),
            preferred_element_type=jnp.float32,
        )
        for k_ref in k_refs
    ]
    peak = jnp.max(scores[0], axis=1, keepdims=True)
    for s in scores[1:]:
        peak = jnp.maximum(peak, jnp.max(s, axis=1, keepdims=True))
    if not first:
        old = m_ref[:, 0:1]
        peak = jnp.maximum(old, peak)
    rate = scale * math.log2(math.e)
    acc = None
    st = None
    for s, k_ref, slot in zip(scores, k_refs, slots):
        w = jnp.exp2((s - peak) * rate)
        hi = w.astype(jnp.bfloat16)
        part_acc = jnp.dot(hi, k_ref[...], preferred_element_type=jnp.float32)
        if width:
            part_st = row_sums(w, pos_ref, width, slot)
        else:
            lo = (w - hi.astype(jnp.float32)).astype(jnp.bfloat16)
            lanes = (((1,), (1,)), ((), ()))
            part_st = lax.dot_general(
                hi, pos_ref[...], lanes, preferred_element_type=jnp.float32
            ) + lax.dot_general(lo, pos_ref[...], lanes, preferred_element_type=jnp.float32)
        acc = part_acc if acc is None else acc + part_acc
        st = part_st if st is None else st + part_st
    if not first:
        alpha = jnp.exp2((old - peak) * rate)
        acc = acc_ref[...] * alpha + acc
        st = st_ref[...] * alpha + st
    if last:
        warped_ref, flow_ref = outs
        total = st[:, 0:1]
        warped_ref[...] = acc / total
        fx = (st[:, 1:2] + st[:, 2:3]) / total
        fy = (st[:, 3:4] + st[:, 4:5]) / total
        lane = lax.broadcasted_iota(jnp.int32, flow_ref.shape, 1)
        flow_ref[...] = jnp.where(lane == 0, fx, jnp.where(lane == 1, fy, 0.0))
    else:
        m_out, acc_out, st_out = outs
        m_out[...] = jnp.broadcast_to(peak, m_out.shape)
        acc_out[...] = acc
        st_out[...] = st


def split_bf16(x):
    hi = x.astype(jnp.bfloat16)
    return hi, (x - hi.astype(jnp.float32)).astype(jnp.bfloat16)


def positions(count, offset, width):
    index = offset + jnp.arange(count, dtype=jnp.int32)
    col_hi, col_lo = split_bf16((index % width).astype(jnp.float32) / width)
    row_hi, row_lo = split_bf16((index // width).astype(jnp.float32) / width)
    zero = jnp.zeros((count,), jnp.bfloat16)
    one = jnp.ones((count,), jnp.bfloat16)
    return jnp.stack([one, col_hi, col_lo, row_hi, row_lo, zero, zero, zero])


def match_step(queries, keys, pos, state, tq, first, last, width, slots):
    padded, chans = queries.shape
    nq = padded // tq
    tk = keys[0].shape[0]
    kernel = functools.partial(
        shard_kernel, scale=1.0 / math.sqrt(chans), chans=chans, first=first, last=last,
        width=width, slots=slots,
    )
    row_spec = lambda width: pl.BlockSpec((tq, width), lambda i: (i, 0))
    in_specs = [row_spec(chans)]
    in_specs += [pl.BlockSpec((tk, chans), lambda i: (0, 0)) for _ in keys]
    in_specs += [pl.BlockSpec(pos.shape, lambda i: (0, 0))]
    args = [queries, *keys, pos]
    if not first:
        in_specs += [row_spec(8), row_spec(chans), row_spec(8)]
        args += list(state)
    if last:
        out_specs = [row_spec(chans), row_spec(8)]
        out_shape = [
            jax.ShapeDtypeStruct((padded, chans), jnp.float32),
            jax.ShapeDtypeStruct((padded, 8), jnp.float32),
        ]
    else:
        out_specs = [row_spec(8), row_spec(chans), row_spec(8)]
        out_shape = [
            jax.ShapeDtypeStruct((padded, 8), jnp.float32),
            jax.ShapeDtypeStruct((padded, chans), jnp.float32),
            jax.ShapeDtypeStruct((padded, 8), jnp.float32),
        ]
    return pl.pallas_call(
        kernel,
        grid=(nq,),
        in_specs=in_specs,
        out_specs=out_specs,
        out_shape=out_shape,
        compiler_params=pltpu.CompilerParams(dimension_semantics=("arbitrary",)),
    )(*args)


def match(queries, targets, width):
    count, chans = queries.shape
    tk = targets.shape[0]
    cap = max(8, (1024 * 2048 // tk) // 8 * 8)
    nq = -(-count // cap)
    tq = -(-(-(-count // nq)) // 8) * 8
    padded = tq * nq
    if padded != count:
        queries = jnp.pad(queries, ((0, padded - count), (0, 0)))
    n = lax.axis_size("match")
    me = lax.axis_index("match")
    shards = [(targets, me, None)]
    if n % 2 == 0:
        chips = n // 2
        sibling = [(j, j ^ 1) for j in range(n)]
        shards.append((lax.ppermute(targets, "match", sibling), me ^ 1, None))
        for shift in range(1, chips):
            hop = [(j, ((j // 2 + shift) % chips) * 2 + j % 2) for j in range(n)]
            moved = lax.ppermute(targets, "match", hop)
            owner = ((me // 2 - shift) % chips) * 2 + me % 2
            shards.append((moved, owner, sibling))
            shards.append((None, owner ^ 1, None))
    else:
        for shift in range(1, n):
            moved = lax.ppermute(targets, "match", [(j, (j + shift) % n) for j in range(n)])
            shards.append((moved, (me - shift) % n, None))
    state = None
    if tk % width == 0:
        owners = jnp.stack([owner for _, owner, _ in shards]) * (tk // width)
        owners = jnp.pad(owners.astype(jnp.float32), (0, 128 - n))
        table = jnp.broadcast_to(owners[None, :], (8, 128))
    pending = None
    whole_rows = tk % width == 0
    if whole_rows and n > 1:
        groups = [[i, i + 1] for i in range(0, n, 2)]
    else:
        groups = [[i] for i in range(n)]
    for group in groups:
        keys = []
        for step in group:
            key, owner, forward = shards[step]
            if key is None:
                key = pending
            if forward:
                key, state = lax.optimization_barrier((key, state))
                pending = lax.ppermute(key, "match", forward)
            keys.append(key)
        if tk % width == 0:
            pos = table
            seg = width
        else:
            pos = positions(tk, shards[group[0]][1] * tk, width)
            seg = 0
        state = match_step(
            queries, keys, pos, state, tq, group[0] == 0, group[-1] == n - 1, seg,
            tuple(step % 128 for step in group),
        )
    warped, flow = state
    return warped[:count], flow[:count, 0], flow[:count, 1]


def local(source, targets, conv_in, flow_proj, in_bias, conv_out):
    rows, cols, chans = source.shape
    all_rows = rows * lax.axis_size("space")
    width = cols * lax.axis_size("match")
    row_first = lax.axis_index("space") * rows
    col_first = lax.axis_index("match") * cols
    ext = extended(source, (("match", 1),), HALO)
    ext = ext.reshape(rows * (cols + 2 * HALO), chans)
    small = jnp.concatenate([flow_proj, in_bias[None, :]], axis=0)
    taps = jnp.transpose(conv_out, (3, 0, 1, 2)).reshape(chans, -1)
    targets, ext, conv_in, small, taps = lax.optimization_barrier(
        (targets, ext, conv_in, small, taps)
    )
    ext = extended(ext, (("space", 0),), HALO * (cols + 2 * HALO))
    erows, ecols = rows + 2 * HALO, cols + 2 * HALO
    warped, sum_x, sum_y = match(ext, targets, width)
    warped = warped.reshape(erows, ecols, chans)
    grow = row_first - HALO + jnp.arange(erows, dtype=jnp.int32)
    gcol = col_first - HALO + jnp.arange(ecols, dtype=jnp.int32)
    inside = ((grow >= 0) & (grow < all_rows))[:, None] & ((gcol >= 0) & (gcol < width))[None, :]
    warped = jnp.where(inside[:, :, None], warped, 0.0)
    col_pos = gcol.astype(jnp.float32) / width
    row_pos = grow.astype(jnp.float32) / width
    flow_x = sum_x.reshape(erows, ecols) - col_pos[None, :]
    flow_y = sum_y.reshape(erows, ecols) - row_pos[:, None]

    hi, rest = split_bf16(warped)
    mid, lo = split_bf16(rest.astype(jnp.float32) + (warped - hi.astype(jnp.float32) - rest.astype(jnp.float32)))
    pieces = jnp.concatenate([hi, mid, lo], axis=-1)
    pre = lax.conv_general_dilated(
        pieces[None], jnp.concatenate([conv_in] * 3, axis=2), (1, 1), "VALID",
        dimension_numbers=("NHWC", "HWIO", "NHWC"),
        preferred_element_type=jnp.float32,
    )[0]
    fx1 = flow_x[1:-1, 1:-1]
    fy1 = flow_y[1:-1, 1:-1]
    pre = pre + fx1[:, :, None] * small[0] + fy1[:, :, None] * small[1] + small[2]
    hidden = jax.nn.silu(pre).astype(jnp.bfloat16)
    hidden = jnp.where(inside[1:-1, 1:-1, None], hidden, jnp.zeros((), jnp.bfloat16))
    proj = jnp.einsum("hwc,ck->hwk", hidden, taps, preferred_element_type=jnp.float32)
    delta = None
    for tap_a in range(3):
        for tap_b in range(3):
            part = proj[tap_a:tap_a + rows, tap_b:tap_b + cols]
            part = jnp.stack([part[..., o * 9 + tap_a * 3 + tap_b] for o in range(2)])
            delta = part if delta is None else delta + part
    flows = jnp.stack([flow_x[HALO:-HALO, HALO:-HALO], flow_y[HALO:-HALO, HALO:-HALO]])
    return flows + delta


def solution(mesh):
    in_specs = (P("space", "match", None), P("match", None), P(), P(), P(), P())
    out_specs = P(None, "space", "match")
    return jax.shard_map(local, mesh=mesh, in_specs=in_specs, out_specs=out_specs, check_vma=False)
```

```python
import functools
import math

import jax
import jax.numpy as jnp
from jax import lax
from jax.experimental import pallas as pl
from jax.experimental.pallas import tpu as pltpu
from jax.sharding import PartitionSpec as P

HALO = 2


def extended(block, sides, width):
    for axis, dim in sides:
        count = lax.axis_size(axis)
        forward = [(i, i + 1) for i in range(count - 1)]
        backward = [(target, source) for source, target in forward]
        low = lax.ppermute(
            lax.slice_in_dim(block, block.shape[dim] - width, None, axis=dim), axis, forward
        )
        high = lax.ppermute(lax.slice_in_dim(block, 0, width, axis=dim), axis, backward)
        block = jnp.concatenate([low, block, high], axis=dim)
    return block


def row_sums(w, base_ref, width, slot):
    count = w.shape[1] // width
    parts = [w[:, g * width:(g + 1) * width] for g in range(count)]
    weighted = None
    area = parts[-1]
    for g in range(count - 1, 0, -1):
        if g < count - 1:
            area = area + parts[g]
        weighted = area if weighted is None else weighted + area
    if count > 1:
        area = area + parts[0]
    lane = lax.broadcasted_iota(jnp.int32, (1, width), 1)
    col = lane.astype(jnp.float32) / width
    total = jnp.sum(area, axis=1, keepdims=True)
    sum_x = jnp.sum(area * col, axis=1, keepdims=True)
    local = jnp.zeros_like(total) if weighted is None else jnp.sum(weighted, axis=1, keepdims=True)
    sum_y = (base_ref[0:1, slot:slot + 1] * total + local) / width
    lane8 = lax.broadcasted_iota(jnp.int32, (w.shape[0], 8), 1)
    zero = jnp.zeros((), jnp.float32)
    return jnp.where(lane8 == 0, total, jnp.where(lane8 == 1, sum_x, jnp.where(lane8 == 3, sum_y, zero)))


def shard_kernel(*refs, scale, chans, first, last, width, slots):
    parts = len(slots)
    q_ref = refs[0]
    k_refs = refs[1:1 + parts]
    pos_ref = refs[1 + parts]
    rest = refs[2 + parts:]
    if not first:
        m_ref, acc_ref, st_ref = rest[:3]
        rest = rest[3:]
    outs = rest
    scores = [
        lax.dot_general(
            q_ref[...], k_ref[...], (((1,), (1,)), ((), ())),
            preferred_element_type=jnp.float32,
        )
        for k_ref in k_refs
    ]
    peak = jnp.max(scores[0], axis=1, keepdims=True)
    for s in scores[1:]:
        peak = jnp.maximum(peak, jnp.max(s, axis=1, keepdims=True))
    if not first:
        old = m_ref[:, 0:1]
        peak = jnp.maximum(old, peak)
    rate = scale * math.log2(math.e)
    acc = None
    st = None
    for s, k_ref, slot in zip(scores, k_refs, slots):
        w = jnp.exp2((s - peak) * rate)
        hi = w.astype(jnp.bfloat16)
        part_acc = jnp.dot(hi, k_ref[...], preferred_element_type=jnp.float32)
        if width:
            part_st = row_sums(w, pos_ref, width, slot)
        else:
            lo = (w - hi.astype(jnp.float32)).astype(jnp.bfloat16)
            lanes = (((1,), (1,)), ((), ()))
            part_st = lax.dot_general(
                hi, pos_ref[...], lanes, preferred_element_type=jnp.float32
            ) + lax.dot_general(lo, pos_ref[...], lanes, preferred_element_type=jnp.float32)
        acc = part_acc if acc is None else acc + part_acc
        st = part_st if st is None else st + part_st
    if not first:
        alpha = jnp.exp2((old - peak) * rate)
        acc = acc_ref[...] * alpha + acc
        st = st_ref[...] * alpha + st
    if last:
        warped_ref, flow_ref = outs
        total = st[:, 0:1]
        inverse = 1.0 / total
        warped_ref[...] = acc * inverse
        fx = (st[:, 1:2] + st[:, 2:3]) / total
        fy = (st[:, 3:4] + st[:, 4:5]) / total
        lane = lax.broadcasted_iota(jnp.int32, flow_ref.shape, 1)
        flow_ref[...] = jnp.where(lane == 0, fx, jnp.where(lane == 1, fy, 0.0))
    else:
        m_out, acc_out, st_out = outs
        m_out[...] = jnp.broadcast_to(peak, m_out.shape)
        acc_out[...] = acc
        st_out[...] = st


def split_bf16(x):
    hi = x.astype(jnp.bfloat16)
    return hi, (x - hi.astype(jnp.float32)).astype(jnp.bfloat16)


def positions(count, offset, width):
    index = offset + jnp.arange(count, dtype=jnp.int32)
    col_hi, col_lo = split_bf16((index % width).astype(jnp.float32) / width)
    row_hi, row_lo = split_bf16((index // width).astype(jnp.float32) / width)
    zero = jnp.zeros((count,), jnp.bfloat16)
    one = jnp.ones((count,), jnp.bfloat16)
    return jnp.stack([one, col_hi, col_lo, row_hi, row_lo, zero, zero, zero])


def match_step(queries, keys, pos, state, tq, first, last, width, slots):
    padded, chans = queries.shape
    nq = padded // tq
    tk = keys[0].shape[0]
    kernel = functools.partial(
        shard_kernel, scale=1.0 / math.sqrt(chans), chans=chans, first=first, last=last,
        width=width, slots=slots,
    )
    row_spec = lambda width: pl.BlockSpec((tq, width), lambda i: (i, 0))
    in_specs = [row_spec(chans)]
    in_specs += [pl.BlockSpec((tk, chans), lambda i: (0, 0)) for _ in keys]
    in_specs += [pl.BlockSpec(pos.shape, lambda i: (0, 0))]
    args = [queries, *keys, pos]
    if not first:
        in_specs += [row_spec(8), row_spec(chans), row_spec(8)]
        args += list(state)
    if last:
        out_specs = [row_spec(chans), row_spec(8)]
        out_shape = [
            jax.ShapeDtypeStruct((padded, chans), jnp.float32),
            jax.ShapeDtypeStruct((padded, 8), jnp.float32),
        ]
    else:
        out_specs = [row_spec(8), row_spec(chans), row_spec(8)]
        out_shape = [
            jax.ShapeDtypeStruct((padded, 8), jnp.float32),
            jax.ShapeDtypeStruct((padded, chans), jnp.float32),
            jax.ShapeDtypeStruct((padded, 8), jnp.float32),
        ]
    return pl.pallas_call(
        kernel,
        grid=(nq,),
        in_specs=in_specs,
        out_specs=out_specs,
        out_shape=out_shape,
        compiler_params=pltpu.CompilerParams(dimension_semantics=("arbitrary",)),
    )(*args)


def match(queries, targets, width):
    count, chans = queries.shape
    tk = targets.shape[0]
    cap = max(8, (1024 * 2048 // tk) // 8 * 8)
    nq = -(-count // cap)
    tq = -(-(-(-count // nq)) // 8) * 8
    padded = tq * nq
    if padded != count:
        queries = jnp.pad(queries, ((0, padded - count), (0, 0)))
    n = lax.axis_size("match")
    me = lax.axis_index("match")
    shards = [(targets, me, None)]
    if n % 2 == 0:
        chips = n // 2
        sibling = [(j, j ^ 1) for j in range(n)]
        shards.append((lax.ppermute(targets, "match", sibling), me ^ 1, None))
        for shift in range(1, chips):
            hop = [(j, ((j // 2 + shift) % chips) * 2 + j % 2) for j in range(n)]
            moved = lax.ppermute(targets, "match", hop)
            owner = ((me // 2 - shift) % chips) * 2 + me % 2
            shards.append((moved, owner, sibling))
            shards.append((None, owner ^ 1, None))
    else:
        for shift in range(1, n):
            moved = lax.ppermute(targets, "match", [(j, (j + shift) % n) for j in range(n)])
            shards.append((moved, (me - shift) % n, None))
    state = None
    if tk % width == 0:
        owners = jnp.stack([owner for _, owner, _ in shards]) * (tk // width)
        owners = jnp.pad(owners.astype(jnp.float32), (0, 128 - n))
        table = jnp.broadcast_to(owners[None, :], (8, 128))
    pending = None
    whole_rows = tk % width == 0
    if whole_rows and n > 1:
        groups = [[i, i + 1] for i in range(0, n, 2)]
    else:
        groups = [[i] for i in range(n)]
    for group in groups:
        keys = []
        for step in group:
            key, owner, forward = shards[step]
            if key is None:
                key = pending
            if forward:
                key, state = lax.optimization_barrier((key, state))
                pending = lax.ppermute(key, "match", forward)
            keys.append(key)
        if tk % width == 0:
            pos = table
            seg = width
        else:
            pos = positions(tk, shards[group[0]][1] * tk, width)
            seg = 0
        state = match_step(
            queries, keys, pos, state, tq, group[0] == 0, group[-1] == n - 1, seg,
            tuple(step % 128 for step in group),
        )
    warped, flow = state
    return warped[:count], flow[:count, 0], flow[:count, 1]


def local(source, targets, conv_in, flow_proj, in_bias, conv_out):
    rows, cols, chans = source.shape
    all_rows = rows * lax.axis_size("space")
    width = cols * lax.axis_size("match")
    row_first = lax.axis_index("space") * rows
    col_first = lax.axis_index("match") * cols
    ext = extended(source, (("match", 1),), HALO)
    ext = ext.reshape(rows * (cols + 2 * HALO), chans)
    small = jnp.concatenate([flow_proj, in_bias[None, :]], axis=0)
    taps = jnp.transpose(conv_out, (3, 0, 1, 2)).reshape(chans, -1)
    targets, ext, conv_in, small, taps = lax.optimization_barrier(
        (targets, ext, conv_in, small, taps)
    )
    ext = extended(ext, (("space", 0),), HALO * (cols + 2 * HALO))
    erows, ecols = rows + 2 * HALO, cols + 2 * HALO
    warped, sum_x, sum_y = match(ext, targets, width)
    warped = warped.reshape(erows, ecols, chans)
    grow = row_first - HALO + jnp.arange(erows, dtype=jnp.int32)
    gcol = col_first - HALO + jnp.arange(ecols, dtype=jnp.int32)
    inside = ((grow >= 0) & (grow < all_rows))[:, None] & ((gcol >= 0) & (gcol < width))[None, :]
    warped = jnp.where(inside[:, :, None], warped, 0.0)
    col_pos = gcol.astype(jnp.float32) / width
    row_pos = grow.astype(jnp.float32) / width
    flow_x = sum_x.reshape(erows, ecols) - col_pos[None, :]
    flow_y = sum_y.reshape(erows, ecols) - row_pos[:, None]

    pre = lax.conv_general_dilated(
        warped[None], conv_in.astype(jnp.float32), (1, 1), "VALID",
        dimension_numbers=("NHWC", "HWIO", "NHWC"),
        precision=lax.Precision.HIGHEST,
        preferred_element_type=jnp.float32,
    )[0]
    fx1 = flow_x[1:-1, 1:-1]
    fy1 = flow_y[1:-1, 1:-1]
    pre = pre + fx1[:, :, None] * small[0] + fy1[:, :, None] * small[1] + small[2]
    hidden = jax.nn.silu(pre).astype(jnp.bfloat16)
    hidden = jnp.where(inside[1:-1, 1:-1, None], hidden, jnp.zeros((), jnp.bfloat16))
    proj = jnp.einsum("hwc,ck->hwk", hidden, taps, preferred_element_type=jnp.float32)
    delta = None
    for tap_a in range(3):
        for tap_b in range(3):
            part = proj[tap_a:tap_a + rows, tap_b:tap_b + cols]
            part = jnp.stack([part[..., o * 9 + tap_a * 3 + tap_b] for o in range(2)])
            delta = part if delta is None else delta + part
    flows = jnp.stack([flow_x[HALO:-HALO, HALO:-HALO], flow_y[HALO:-HALO, HALO:-HALO]])
    return flows + delta


def solution(mesh):
    in_specs = (P("space", "match", None), P("match", None), P(), P(), P(), P())
    out_specs = P(None, "space", "match")
    return jax.shard_map(local, mesh=mesh, in_specs=in_specs, out_specs=out_specs, check_vma=False)
```
